32 devices in a mesh: groups: 2 (over x), seq: 16 (over z, y, core).
Axes of the slice: x: 2, y: 2, z: 4, core: 2. Of those that a mesh axis runs over, the one named last changes fastest.
Arguments:
- video_q: bfloat16 [16384, 2048], P(('groups', 'seq')), parts along dimension 0, may hold values from -64 to 64
- video_k: bfloat16 [16384, 2048], P(('groups', 'seq')), parts along dimension 0, may hold values from -6 to 6
- video_v: bfloat16 [16384, 2048], P(('groups', 'seq')), parts along dimension 0, may hold values from -4 to 4
- audio_q: bfloat16 [256, 2048], P(('groups', 'seq')), parts along dimension 0, may hold values from -64 to 64
- audio_k: bfloat16 [256, 2048], P(('groups', 'seq')), parts along dimension 0, may hold values from -6 to 6
- audio_v: bfloat16 [256, 2048], P(('groups', 'seq')), parts along dimension 0, may hold values from -4 to 4
Outputs:
- video_out: bfloat16 [16384, 2048], P(('groups', 'seq')), parts along dimension 0
- audio_out: bfloat16 [256, 2048], P(('groups', 'seq')), parts along dimension 0
The draws below stay inside these ranges and needn't reach their ends.
There are 2 independent parts, one for each index of `groups`. The reference program is written for one: setup_inputs(seed, part) draws one part's arguments, and reference() takes and returns one part's arrays. A program takes and returns all parts, laid end to end along the dimension named above; each array names one. Nothing has to cross between parts.
All inputs are finite; a program needn't handle non-finite values.
Results may differ from the reference program's by a relative error of at most 0.007.
Values may be sent and summed in bfloat16 or wider, within the bound.
No kernel may reach another device: no remote copies, remote signals or barrier semaphores. Data moves between devices by JAX's collectives and lax.ppermute only.
A program may use at most 128 MiB of HBM per device.

```python
import jax
import jax.numpy as jnp
from jax import lax

HEADS = 32
HEAD_DIM = 64
TOKENS = 8192
AUDIO = 128


def base_fields(key):
    subkeys = [jax.random.fold_in(key, 7100 + number) for number in range(4)]
    model_width = HEADS * HEAD_DIM
    video_query = 2.0 * jnp.clip(jax.random.normal(subkeys[0], (TOKENS, model_width), jnp.float32), -6.0, 6.0)
    video_key = jnp.clip(jax.random.normal(subkeys[1], (TOKENS, model_width), jnp.float32), -6.0, 6.0)
    audio_query = 2.0 * jnp.clip(jax.random.normal(subkeys[2], (AUDIO, model_width), jnp.float32), -6.0, 6.0)
    audio_key = jnp.clip(jax.random.normal(subkeys[3], (AUDIO, model_width), jnp.float32), -6.0, 6.0)
    return (video_query, video_key, audio_query, audio_key)


def draw_video_q(key, part):
    return base_fields(key)[0].astype(jnp.bfloat16)


def draw_video_k(key, part):
    return base_fields(key)[1].astype(jnp.bfloat16)


def draw_audio_q(key, part):
    return base_fields(key)[2].astype(jnp.bfloat16)


def draw_audio_k(key, part):
    return base_fields(key)[3].astype(jnp.bfloat16)


def block_levels(rng, extent, cuts, smallest, top_value):
    def one(position, blocks):
        steps = jax.random.uniform(jax.random.fold_in(jax.random.fold_in(rng, 6), position), (blocks,), jnp.float32, smallest / len(cuts), top_value / len(cuts))
        return jnp.repeat(jnp.exp(steps), extent[position] // blocks).reshape((-1,) + (1,) * (len(extent) - position - 1))

    gain = one(*cuts[0])
    for cut in cuts[1:]:
        gain = gain * one(*cut)
    return gain


def centred(own_key, dims, scale, bound, cuts=(), held_as=jnp.bfloat16):
    entries = scale * jax.random.normal(own_key, dims, jnp.float32)
    if cuts:
        entries = entries * block_levels(own_key, dims, cuts, -0.22, 0.18)
    return jnp.clip(entries, -bound, bound).astype(held_as)


def setup_inputs(seed: int = 0, part: int = 0) -> dict:
    arg_keys = jax.random.split(jax.random.key(seed), 7)
    part_splits = jax.random.split(jax.random.fold_in(arg_keys[6], part), 7)
    return {
        "video_q": draw_video_q(jax.random.fold_in(jax.random.fold_in(arg_keys[6], part), 71), part),
        "video_k": draw_video_k(jax.random.fold_in(jax.random.fold_in(arg_keys[6], part), 71), part),
        "video_v": centred(part_splits[2], (TOKENS, HEADS * HEAD_DIM), 0.25, 4.0, ((0, 16),)),
        "audio_q": draw_audio_q(jax.random.fold_in(jax.random.fold_in(arg_keys[6], part), 71), part),
        "audio_k": draw_audio_k(jax.random.fold_in(jax.random.fold_in(arg_keys[6], part), 71), part),
        "audio_v": centred(part_splits[5], (AUDIO, HEADS * HEAD_DIM), 0.25, 4.0, ((0, 16),)),
    }


def one_head(queries, keys, values):
    scores = jnp.dot(queries, keys.T, preferred_element_type=jnp.float32) * 0.125
    highest = jnp.max(scores, axis=1, keepdims=True)
    weights = jnp.exp(scores - highest)
    totals = jnp.sum(weights, axis=1, keepdims=True)
    summed = jnp.dot(weights.astype(jnp.bfloat16), values, preferred_element_type=jnp.float32)
    return (summed / totals).astype(jnp.bfloat16)


def split_heads(matrix):
    return matrix.reshape(matrix.shape[0], HEADS, HEAD_DIM).transpose(1, 0, 2)


def attend(queries, keys, values):
    triple = (split_heads(queries), split_heads(keys), split_heads(values))
    result = lax.map(lambda member: one_head(member[0], member[1], member[2]), triple)
    return result.transpose(1, 0, 2).reshape(queries.shape[0], HEADS * HEAD_DIM)


def reference(video_q, video_k, video_v, audio_q, audio_k, audio_v):
    video_out = attend(video_q, audio_k, audio_v)
    audio_out = attend(audio_q, video_k, video_v)
    return (video_out, audio_out)
```

```python
import jax
import jax.numpy as jnp
from jax import lax
from jax.sharding import PartitionSpec as P

HEAD_DIM = 64


def spread(scales):
    return jnp.repeat(scales, HEAD_DIM, axis=1)


def exchange(value, bit, count):
    pairs = [(source, source ^ bit) for source in range(count)]
    return lax.ppermute(value, "seq", pairs)


def gather_rows(block):
    count = lax.axis_size("seq")
    me = lax.axis_index("seq")
    held = block[None]
    bit = count // 2
    while bit >= 1:
        arrived = exchange(held, bit, count)
        upper = (me & bit) != 0
        low = jnp.where(upper, arrived, held)
        high = jnp.where(upper, held, arrived)
        held = jnp.stack([low, high], axis=1).reshape((-1,) + block.shape)
        bit //= 2
    return held.reshape((count * block.shape[0],) + block.shape[1:])


def merge(first, second, heads):
    width = heads * HEAD_DIM
    top = jnp.maximum(first[:, width + heads :], second[:, width + heads :])
    first_scale = jnp.exp(first[:, width + heads :] - top)
    second_scale = jnp.exp(second[:, width + heads :] - top)
    totals = first[:, width : width + heads] * first_scale + second[:, width : width + heads] * second_scale
    summed = first[:, :width] * spread(first_scale) + second[:, :width] * spread(second_scale)
    return jnp.concatenate([summed, totals, top], axis=1)


def scatter_rows(state, heads):
    count = lax.axis_size("seq")
    me = lax.axis_index("seq")
    rows = state.shape[0] // count
    held = state.reshape((count, rows, state.shape[1]))
    bit = 1
    while bit < count:
        pairs = held.reshape((-1, 2, rows, state.shape[1]))
        upper = (me & bit) != 0
        keep = jnp.where(upper, pairs[:, 1], pairs[:, 0])
        give = jnp.where(upper, pairs[:, 0], pairs[:, 1])
        arrived = exchange(give, bit, count)
        held = merge(
            keep.reshape((-1, state.shape[1])), arrived.reshape((-1, state.shape[1])), heads
        ).reshape((-1, rows, state.shape[1]))
        bit *= 2
    return held.reshape((rows, state.shape[1]))


def attend_block(queries, keys, values):
    heads = queries.shape[1] // HEAD_DIM
    query_heads = queries.reshape(queries.shape[0], heads, HEAD_DIM)
    key_heads = keys.reshape(keys.shape[0], heads, HEAD_DIM)
    value_heads = values.reshape(values.shape[0], heads, HEAD_DIM)
    scores = (
        jnp.einsum("rhd,shd->hrs", query_heads, key_heads, preferred_element_type=jnp.float32)
        * 0.125
    )
    highest = jnp.max(scores, axis=2)
    weights = jnp.exp(scores - highest[:, :, None])
    totals = jnp.sum(weights, axis=2)
    summed = jnp.einsum(
        "hrs,shd->rhd",
        weights.astype(jnp.bfloat16),
        value_heads,
        preferred_element_type=jnp.float32,
    )
    return highest.T, totals.T, summed.reshape(queries.shape[0], heads * HEAD_DIM)


def local(video_q, video_k, video_v, audio_q, audio_k, audio_v):
    width = video_q.shape[1]
    heads = width // HEAD_DIM
    packed = jnp.concatenate([audio_q, audio_k, audio_v], axis=1)
    gathered = gather_rows(packed)
    all_queries = gathered[:, :width]
    all_keys = gathered[:, width : 2 * width]
    all_values = gathered[:, 2 * width :]

    highest, totals, summed = attend_block(all_queries, video_k, video_v)
    state = jnp.concatenate([summed, totals, highest], axis=1)
    mine = scatter_rows(state, heads)
    audio_out = (mine[:, :width] / spread(mine[:, width : width + heads])).astype(jnp.bfloat16)

    ignored, video_totals, video_sums = attend_block(video_q, all_keys, all_values)
    video_out = (video_sums / spread(video_totals)).astype(jnp.bfloat16)
    return video_out, audio_out


def solution(mesh):
    placed = P(("groups", "seq"), None)
    return jax.shard_map(
        local,
        mesh=mesh,
        in_specs=(placed,) * 6,
        out_specs=(placed, placed),
        check_vma=False,
    )
```

```python
import jax
import jax.numpy as jnp
from jax import lax
from jax.experimental import pallas as pl
from jax.experimental.pallas import tpu as pltpu
from jax.sharding import PartitionSpec as P

HEAD_DIM = 64


def spread(scales):
    return jnp.repeat(scales, HEAD_DIM, axis=1)


def exchange(value, bit, count):
    pairs = [(source, source ^ bit) for source in range(count)]
    return lax.ppermute(value, "seq", pairs)


def gather_rows(block):
    count = lax.axis_size("seq")
    me = lax.axis_index("seq")
    held = block[None]
    bit = count // 2
    while bit >= 1:
        arrived = exchange(held, bit, count)
        upper = (me & bit) != 0
        low = jnp.where(upper, arrived, held)
        high = jnp.where(upper, held, arrived)
        held = jnp.stack([low, high], axis=1).reshape((-1,) + block.shape)
        bit //= 2
    return held.reshape((count * block.shape[0],) + block.shape[1:])


def merge(first, second, heads):
    width = heads * HEAD_DIM
    top = jnp.maximum(first[:, width + heads :], second[:, width + heads :])
    first_scale = jnp.exp(first[:, width + heads :] - top)
    second_scale = jnp.exp(second[:, width + heads :] - top)
    totals = first[:, width : width + heads] * first_scale + second[:, width : width + heads] * second_scale
    summed = first[:, :width] * spread(first_scale) + second[:, :width] * spread(second_scale)
    return jnp.concatenate([summed, totals, top], axis=1)


def scatter_rows(state, heads):
    count = lax.axis_size("seq")
    me = lax.axis_index("seq")
    rows = state.shape[0] // count
    held = state.reshape((count, rows, state.shape[1]))
    bit = 1
    while bit < count:
        pairs = held.reshape((-1, 2, rows, state.shape[1]))
        upper = (me & bit) != 0
        keep = jnp.where(upper, pairs[:, 1], pairs[:, 0])
        give = jnp.where(upper, pairs[:, 0], pairs[:, 1])
        arrived = exchange(give, bit, count)
        held = merge(
            keep.reshape((-1, state.shape[1])), arrived.reshape((-1, state.shape[1])), heads
        ).reshape((-1, rows, state.shape[1]))
        bit *= 2
    return held.reshape((rows, state.shape[1]))


def head_masks(rows):
    lane = lax.broadcasted_iota(jnp.int32, (rows, 2 * HEAD_DIM), 1)
    return lane < HEAD_DIM


def pair_scores(queries, keys, first):
    masked = jnp.where(first, queries, jnp.zeros_like(queries))
    return (
        lax.dot_general(
            masked, keys, (((1,), (1,)), ((), ())), preferred_element_type=jnp.float32
        )
        * 0.125
    )


def video_kernel(query_ref, key_ref, value_ref, out_ref):
    queries = query_ref[...]
    keys = key_ref[...]
    values = value_ref[...]
    first = head_masks(queries.shape[0])
    results = []
    for lanes in (first, jnp.logical_not(first)):
        scores = pair_scores(queries, keys, lanes)
        highest = jnp.max(scores, axis=1, keepdims=True)
        weights = jnp.exp(scores - highest)
        totals = jnp.sum(weights, axis=1, keepdims=True)
        summed = jnp.dot(
            weights.astype(jnp.bfloat16), values, preferred_element_type=jnp.float32
        )
        results.append(summed / totals)
    out_ref[...] = jnp.where(first, results[0], results[1]).astype(out_ref.dtype)


def video_attention(queries, keys, values):
    rows, width = queries.shape
    pairs = width // (2 * HEAD_DIM)
    key_rows = keys.shape[0]
    return pl.pallas_call(
        video_kernel,
        grid=(pairs,),
        in_specs=[
            pl.BlockSpec((rows, 2 * HEAD_DIM), lambda p: (0, p)),
            pl.BlockSpec((key_rows, 2 * HEAD_DIM), lambda p: (0, p)),
            pl.BlockSpec((key_rows, 2 * HEAD_DIM), lambda p: (0, p)),
        ],
        out_specs=pl.BlockSpec((rows, 2 * HEAD_DIM), lambda p: (0, p)),
        out_shape=jax.ShapeDtypeStruct((rows, width), jnp.bfloat16),
        cost_estimate=pl.CostEstimate(
            flops=8 * rows * key_rows * width,
            transcendentals=rows * key_rows * width // HEAD_DIM,
            bytes_accessed=2 * (2 * rows * width + 2 * key_rows * width),
        ),
    )(queries, keys, values)


def audio_kernel(query_ref, key_ref, value_ref, sum_ref, total_ref, top_ref):
    pair = pl.program_id(0)
    queries = query_ref[...]
    keys = key_ref[...]
    values = value_ref[...]
    rows = queries.shape[0]
    first = head_masks(rows)

    @pl.when(pair == 0)
    def _():
        total_ref[...] = jnp.zeros_like(total_ref)
        top_ref[...] = jnp.zeros_like(top_ref)

    column = lax.broadcasted_iota(jnp.int32, total_ref.shape, 1)
    results = []
    totals_now = total_ref[...]
    tops_now = top_ref[...]
    for half, lanes in enumerate((first, jnp.logical_not(first))):
        scores = pair_scores(queries, keys, lanes)
        highest = jnp.max(scores, axis=1, keepdims=True)
        weights = jnp.exp(scores - highest)
        totals = jnp.sum(weights, axis=1, keepdims=True)
        results.append(
            jnp.dot(weights.astype(jnp.bfloat16), values, preferred_element_type=jnp.float32)
        )
        here = column == 2 * pair + half
        totals_now = jnp.where(here, totals, totals_now)
        tops_now = jnp.where(here, highest, tops_now)
    total_ref[...] = totals_now
    top_ref[...] = tops_now
    sum_ref[...] = jnp.where(first, results[0], results[1])


def audio_partial(queries, keys, values):
    rows, width = queries.shape
    heads = width // HEAD_DIM
    key_rows = keys.shape[0]
    return pl.pallas_call(
        audio_kernel,
        grid=(heads // 2,),
        in_specs=[
            pl.BlockSpec((rows, 2 * HEAD_DIM), lambda p: (0, p)),
            pl.BlockSpec((key_rows, 2 * HEAD_DIM), lambda p: (0, p)),
            pl.BlockSpec((key_rows, 2 * HEAD_DIM), lambda p: (0, p)),
        ],
        out_specs=[
            pl.BlockSpec((rows, 2 * HEAD_DIM), lambda p: (0, p)),
            pl.BlockSpec((rows, heads), lambda p: (0, 0)),
            pl.BlockSpec((rows, heads), lambda p: (0, 0)),
        ],
        out_shape=[
            jax.ShapeDtypeStruct((rows, width), jnp.float32),
            jax.ShapeDtypeStruct((rows, heads), jnp.float32),
            jax.ShapeDtypeStruct((rows, heads), jnp.float32),
        ],
        compiler_params=pltpu.CompilerParams(dimension_semantics=("arbitrary",)),
        cost_estimate=pl.CostEstimate(
            flops=8 * rows * key_rows * width,
            transcendentals=rows * key_rows * heads,
            bytes_accessed=2 * rows * width + 4 * key_rows * width + 4 * rows * width,
        ),
    )(queries, keys, values)


def local(video_q, video_k, video_v, audio_q, audio_k, audio_v):
    width = video_q.shape[1]
    heads = width // HEAD_DIM
    packed = jnp.concatenate([audio_q, audio_k, audio_v], axis=1)
    gathered = gather_rows(packed)
    all_queries = gathered[:, :width]
    all_keys = gathered[:, width : 2 * width]
    all_values = gathered[:, 2 * width :]

    summed, totals, highest = audio_partial(all_queries, video_k, video_v)
    state = jnp.concatenate([summed, totals, highest], axis=1)
    mine = scatter_rows(state, heads)
    audio_out = (mine[:, :width] / spread(mine[:, width : width + heads])).astype(jnp.bfloat16)

    video_out = video_attention(video_q, all_keys, all_values)
    return video_out, audio_out


def solution(mesh):
    placed = P(("groups", "seq"), None)
    return jax.shard_map(
        local,
        mesh=mesh,
        in_specs=(placed,) * 6,
        out_specs=(placed, placed),
        check_vma=False,
    )
```

```python
import jax
import jax.numpy as jnp
from jax import lax
from jax.experimental import pallas as pl
from jax.experimental.pallas import tpu as pltpu
from jax.sharding import PartitionSpec as P

HEAD_DIM = 64


def spread(scales):
    return jnp.repeat(scales, HEAD_DIM, axis=1)


def exchange(value, bit, count):
    pairs = [(source, source ^ bit) for source in range(count)]
    return lax.ppermute(value, "seq", pairs)


def gather_rows(block):
    count = lax.axis_size("seq")
    me = lax.axis_index("seq")
    held = block[None]
    bit = count // 2
    while bit >= 1:
        arrived = exchange(held, bit, count)
        upper = (me & bit) != 0
        low = jnp.where(upper, arrived, held)
        high = jnp.where(upper, held, arrived)
        held = jnp.stack([low, high], axis=1).reshape((-1,) + block.shape)
        bit //= 2
    return held.reshape((count * block.shape[0],) + block.shape[1:])


def merge(first, second, heads):
    width = heads * HEAD_DIM
    top = jnp.maximum(first[:, width + heads :], second[:, width + heads :])
    first_scale = jnp.exp(first[:, width + heads :] - top)
    second_scale = jnp.exp(second[:, width + heads :] - top)
    totals = first[:, width : width + heads] * first_scale + second[:, width : width + heads] * second_scale
    summed = first[:, :width] * spread(first_scale) + second[:, :width] * spread(second_scale)
    return jnp.concatenate([summed, totals, top], axis=1)


def scatter_rows(state, heads):
    count = lax.axis_size("seq")
    me = lax.axis_index("seq")
    rows = state.shape[0] // count
    held = state.reshape((count, rows, state.shape[1]))
    bit = 1
    while bit < count:
        pairs = held.reshape((-1, 2, rows, state.shape[1]))
        upper = (me & bit) != 0
        keep = jnp.where(upper, pairs[:, 1], pairs[:, 0])
        give = jnp.where(upper, pairs[:, 0], pairs[:, 1])
        arrived = exchange(give, bit, count)
        held = merge(
            keep.reshape((-1, state.shape[1])), arrived.reshape((-1, state.shape[1])), heads
        ).reshape((-1, rows, state.shape[1]))
        bit *= 2
    return held.reshape((rows, state.shape[1]))


def head_masks(rows):
    lane = lax.broadcasted_iota(jnp.int32, (rows, 2 * HEAD_DIM), 1)
    return lane < HEAD_DIM


def pair_scores(queries, keys, first):
    masked = jnp.where(first, queries, jnp.zeros_like(queries))
    return (
        lax.dot_general(
            masked, keys, (((1,), (1,)), ((), ())), preferred_element_type=jnp.float32
        )
        * 0.125
    )


def video_kernel(query_ref, key_ref, value_ref, earlier_ref, out_ref):
    del earlier_ref
    queries = query_ref[...]
    keys = key_ref[...]
    values = value_ref[...]
    first = head_masks(queries.shape[0])
    sums = []
    counts = []
    for lanes in (first, jnp.logical_not(first)):
        scores = pair_scores(queries, keys, lanes)
        highest = jnp.max(scores, axis=1, keepdims=True)
        weights = jnp.exp(scores - highest)
        counts.append(jnp.sum(weights, axis=1, keepdims=True))
        sums.append(
            jnp.dot(weights.astype(jnp.bfloat16), values, preferred_element_type=jnp.float32)
        )
    summed = jnp.where(first, sums[0], sums[1])
    totals = jnp.where(first, counts[0], counts[1])
    out_ref[...] = (summed / totals).astype(out_ref.dtype)


def video_attention(queries, keys, values, groups):
    rows, width = queries.shape
    pairs = width // (2 * HEAD_DIM) // groups
    key_rows = keys.shape[0]
    out = jnp.zeros((rows, width), jnp.bfloat16)
    for group in range(groups):
        first_pair = group * pairs
        out = pl.pallas_call(
            video_kernel,
            grid=(pairs,),
            in_specs=[
                pl.BlockSpec((rows, 2 * HEAD_DIM), lambda p, f=first_pair: (0, p + f)),
                pl.BlockSpec((key_rows, 2 * HEAD_DIM), lambda p, f=first_pair: (0, p + f)),
                pl.BlockSpec((key_rows, 2 * HEAD_DIM), lambda p, f=first_pair: (0, p + f)),
                pl.BlockSpec(memory_space=pl.ANY),
            ],
            out_specs=pl.BlockSpec((rows, 2 * HEAD_DIM), lambda p, f=first_pair: (0, p + f)),
            out_shape=jax.ShapeDtypeStruct((rows, width), jnp.bfloat16),
            input_output_aliases={3: 0},
            cost_estimate=pl.CostEstimate(
                flops=8 * rows * key_rows * width // groups,
                transcendentals=rows * key_rows * width // HEAD_DIM // groups,
                bytes_accessed=2 * (2 * rows * width + 2 * key_rows * width) // groups,
            ),
        )(queries, keys, values, out)
    return out


def audio_kernel(query_ref, key_ref, value_ref, sum_ref, total_ref, top_ref):
    pair = pl.program_id(0)
    queries = query_ref[...]
    keys = key_ref[...]
    values = value_ref[...]
    rows = queries.shape[0]
    first = head_masks(rows)

    @pl.when(pair == 0)
    def _():
        total_ref[...] = jnp.zeros_like(total_ref)
        top_ref[...] = jnp.zeros_like(top_ref)

    column = lax.broadcasted_iota(jnp.int32, total_ref.shape, 1)
    results = []
    totals_now = total_ref[...]
    tops_now = top_ref[...]
    for half, lanes in enumerate((first, jnp.logical_not(first))):
        scores = pair_scores(queries, keys, lanes)
        highest = jnp.max(scores, axis=1, keepdims=True)
        weights = jnp.exp(scores - highest)
        totals = jnp.sum(weights, axis=1, keepdims=True)
        results.append(
            jnp.dot(weights.astype(jnp.bfloat16), values, preferred_element_type=jnp.float32)
        )
        here = column == 2 * pair + half
        totals_now = jnp.where(here, totals, totals_now)
        tops_now = jnp.where(here, highest, tops_now)
    total_ref[...] = totals_now
    top_ref[...] = tops_now
    sum_ref[...] = jnp.where(first, results[0], results[1])


def audio_partial(queries, keys, values, group, groups):
    rows, width = queries.shape
    heads = width // HEAD_DIM // groups
    first_pair = group * heads // 2
    key_rows = keys.shape[0]
    return pl.pallas_call(
        audio_kernel,
        grid=(heads // 2,),
        in_specs=[
            pl.BlockSpec((rows, 2 * HEAD_DIM), lambda p: (0, p + first_pair)),
            pl.BlockSpec((key_rows, 2 * HEAD_DIM), lambda p: (0, p + first_pair)),
            pl.BlockSpec((key_rows, 2 * HEAD_DIM), lambda p: (0, p + first_pair)),
        ],
        out_specs=[
            pl.BlockSpec((rows, 2 * HEAD_DIM), lambda p: (0, p)),
            pl.BlockSpec((rows, heads), lambda p: (0, 0)),
            pl.BlockSpec((rows, heads), lambda p: (0, 0)),
        ],
        out_shape=[
            jax.ShapeDtypeStruct((rows, heads * HEAD_DIM), jnp.float32),
            jax.ShapeDtypeStruct((rows, heads), jnp.float32),
            jax.ShapeDtypeStruct((rows, heads), jnp.float32),
        ],
        compiler_params=pltpu.CompilerParams(dimension_semantics=("arbitrary",)),
        cost_estimate=pl.CostEstimate(
            flops=8 * rows * key_rows * width // groups,
            transcendentals=rows * key_rows * heads,
            bytes_accessed=(2 * rows * width + 4 * key_rows * width + 4 * rows * width) // groups,
        ),
    )(queries, keys, values)


def local(video_q, video_k, video_v, audio_q, audio_k, audio_v):
    width = video_q.shape[1]
    heads = width // HEAD_DIM
    groups = 4
    all_queries = gather_rows(audio_q)
    all_queries, packed = lax.optimization_barrier(
        (all_queries, jnp.concatenate([audio_k, audio_v], axis=1))
    )
    gathered = gather_rows(packed)
    all_keys = gathered[:, :width]
    all_values = gathered[:, width:]

    parts = [audio_partial(all_queries, video_k, video_v, g, groups) for g in range(groups)]
    state = jnp.concatenate(
        [part[0] for part in parts] + [part[1] for part in parts] + [part[2] for part in parts],
        axis=1,
    )
    mine = scatter_rows(state, heads)
    audio_out = (mine[:, :width] / spread(mine[:, width : width + heads])).astype(jnp.bfloat16)

    video_out = video_attention(video_q, all_keys, all_values, groups)
    return video_out, audio_out


def solution(mesh):
    placed = P(("groups", "seq"), None)
    return jax.shard_map(
        local,
        mesh=mesh,
        in_specs=(placed,) * 6,
        out_specs=(placed, placed),
        check_vma=False,
    )
```

```python
import jax
import jax.numpy as jnp
from jax import lax
from jax.experimental import pallas as pl
from jax.experimental.pallas import tpu as pltpu
from jax.sharding import PartitionSpec as P

HEAD_DIM = 64


def spread(scales):
    return jnp.repeat(scales, HEAD_DIM, axis=1)


def exchange(value, bit, count):
    pairs = [(source, source ^ bit) for source in range(count)]
    return lax.ppermute(value, "seq", pairs)


def gather_rows(block, during=()):
    count = lax.axis_size("seq")
    me = lax.axis_index("seq")
    held = block[None]
    results = []
    bit = count // 2
    step = 0
    while bit >= 1:
        work = during[step] if step < len(during) else None
        if work is not None:
            held, ready = lax.optimization_barrier((held, work[1]))
        arrived = exchange(held, bit, count)
        if work is not None:
            done = work[0](ready)
            arrived, done = lax.optimization_barrier((arrived, done))
            results.append(done)
        upper = (me & bit) != 0
        low = jnp.where(upper, arrived, held)
        high = jnp.where(upper, held, arrived)
        held = jnp.stack([low, high], axis=1).reshape((-1,) + block.shape)
        bit //= 2
        step += 1
    return held.reshape((count * block.shape[0],) + block.shape[1:]), results


def merge(first, second, heads):
    width = heads * HEAD_DIM
    top = jnp.maximum(first[:, width + heads :], second[:, width + heads :])
    first_scale = jnp.exp(first[:, width + heads :] - top)
    second_scale = jnp.exp(second[:, width + heads :] - top)
    totals = first[:, width : width + heads] * first_scale + second[:, width : width + heads] * second_scale
    summed = first[:, :width] * spread(first_scale) + second[:, :width] * spread(second_scale)
    return jnp.concatenate([summed, totals, top], axis=1)


def scatter_rows(state, heads, during=()):
    count = lax.axis_size("seq")
    me = lax.axis_index("seq")
    rows = state.shape[0] // count
    held = state.reshape((count, rows, state.shape[1]))
    carried = None
    bit = 1
    step = 0
    while bit < count:
        pairs = held.reshape((-1, 2, rows, state.shape[1]))
        upper = (me & bit) != 0
        keep = jnp.where(upper, pairs[:, 1], pairs[:, 0])
        give = jnp.where(upper, pairs[:, 0], pairs[:, 1])
        work = during[step] if step < len(during) else None
        if work is not None:
            give, carried = lax.optimization_barrier((give, carried))
        arrived = exchange(give, bit, count)
        if work is not None:
            carried = work(carried)
            arrived, carried = lax.optimization_barrier((arrived, carried))
        held = merge(
            keep.reshape((-1, state.shape[1])), arrived.reshape((-1, state.shape[1])), heads
        ).reshape((-1, rows, state.shape[1]))
        bit *= 2
        step += 1
    for work in during[step:]:
        carried = work(carried)
    return held.reshape((rows, state.shape[1])), carried


def head_masks(rows):
    lane = lax.broadcasted_iota(jnp.int32, (rows, 2 * HEAD_DIM), 1)
    return lane < HEAD_DIM


def pair_scores(queries, keys, first):
    masked = jnp.where(first, queries, jnp.zeros_like(queries))
    return (
        lax.dot_general(
            masked, keys, (((1,), (1,)), ((), ())), preferred_element_type=jnp.float32
        )
        * 0.125
    )


def video_kernel(query_ref, key_ref, value_ref, *refs):
    out_ref = refs[-1]
    queries = query_ref[...]
    keys = key_ref[...]
    values = value_ref[...]
    first = head_masks(queries.shape[0])
    sums = []
    counts = []
    for lanes in (first, jnp.logical_not(first)):
        scores = pair_scores(queries, keys, lanes)
        highest = jnp.max(scores, axis=1, keepdims=True)
        weights = jnp.exp(scores - highest)
        counts.append(jnp.sum(weights, axis=1, keepdims=True))
        sums.append(
            jnp.dot(weights.astype(jnp.bfloat16), values, preferred_element_type=jnp.float32)
        )
    summed = jnp.where(first, sums[0], sums[1])
    totals = jnp.where(first, counts[0], counts[1])
    out_ref[...] = (summed / totals).astype(out_ref.dtype)


def video_part(queries, keys, values, earlier, group, groups):
    rows, width = queries.shape
    pairs = width // (2 * HEAD_DIM) // groups
    first_pair = group * pairs
    key_rows = keys.shape[0]
    specs = [
        pl.BlockSpec((rows, 2 * HEAD_DIM), lambda p: (0, p + first_pair)),
        pl.BlockSpec((key_rows, 2 * HEAD_DIM), lambda p: (0, p + first_pair)),
        pl.BlockSpec((key_rows, 2 * HEAD_DIM), lambda p: (0, p + first_pair)),
    ]
    operands = [queries, keys, values]
    aliases = {}
    if earlier is not None:
        specs.append(pl.BlockSpec(memory_space=pl.ANY))
        operands.append(earlier)
        aliases = {3: 0}
    return pl.pallas_call(
        video_kernel,
        grid=(pairs,),
        in_specs=specs,
        out_specs=pl.BlockSpec((rows, 2 * HEAD_DIM), lambda p: (0, p + first_pair)),
        out_shape=jax.ShapeDtypeStruct((rows, width), jnp.bfloat16),
        input_output_aliases=aliases,
        cost_estimate=pl.CostEstimate(
            flops=8 * rows * key_rows * width // groups,
            transcendentals=rows * key_rows * width // HEAD_DIM // groups,
            bytes_accessed=2 * (2 * rows * width + 2 * key_rows * width) // groups,
        ),
    )(*operands)


def audio_kernel(query_ref, key_ref, value_ref, sum_ref, total_ref, top_ref):
    pair = pl.program_id(0)
    queries = query_ref[...]
    keys = key_ref[...]
    values = value_ref[...]
    rows = queries.shape[0]
    first = head_masks(rows)

    @pl.when(pair == 0)
    def _():
        total_ref[...] = jnp.zeros_like(total_ref)
        top_ref[...] = jnp.zeros_like(top_ref)

    column = lax.broadcasted_iota(jnp.int32, total_ref.shape, 1)
    results = []
    totals_now = total_ref[...]
    tops_now = top_ref[...]
    for half, lanes in enumerate((first, jnp.logical_not(first))):
        scores = pair_scores(queries, keys, lanes)
        highest = jnp.max(scores, axis=1, keepdims=True)
        weights = jnp.exp(scores - highest)
        totals = jnp.sum(weights, axis=1, keepdims=True)
        results.append(
            jnp.dot(weights.astype(jnp.bfloat16), values, preferred_element_type=jnp.float32)
        )
        here = column == 2 * pair + half
        totals_now = jnp.where(here, totals, totals_now)
        tops_now = jnp.where(here, highest, tops_now)
    total_ref[...] = totals_now
    top_ref[...] = tops_now
    sum_ref[...] = jnp.where(first, results[0], results[1])


def audio_partial(queries, keys, values, group, groups):
    rows, width = queries.shape
    heads = width // HEAD_DIM // groups
    first_pair = group * heads // 2
    key_rows = keys.shape[0]
    return pl.pallas_call(
        audio_kernel,
        grid=(heads // 2,),
        in_specs=[
            pl.BlockSpec((rows, 2 * HEAD_DIM), lambda p: (0, p + first_pair)),
            pl.BlockSpec((key_rows, 2 * HEAD_DIM), lambda p: (0, p + first_pair)),
            pl.BlockSpec((key_rows, 2 * HEAD_DIM), lambda p: (0, p + first_pair)),
        ],
        out_specs=[
            pl.BlockSpec((rows, 2 * HEAD_DIM), lambda p: (0, p)),
            pl.BlockSpec((rows, heads), lambda p: (0, 0)),
            pl.BlockSpec((rows, heads), lambda p: (0, 0)),
        ],
        out_shape=[
            jax.ShapeDtypeStruct((rows, heads * HEAD_DIM), jnp.float32),
            jax.ShapeDtypeStruct((rows, heads), jnp.float32),
            jax.ShapeDtypeStruct((rows, heads), jnp.float32),
        ],
        compiler_params=pltpu.CompilerParams(dimension_semantics=("arbitrary",)),
        cost_estimate=pl.CostEstimate(
            flops=8 * rows * key_rows * width // groups,
            transcendentals=rows * key_rows * heads,
            bytes_accessed=(2 * rows * width + 4 * key_rows * width + 4 * rows * width) // groups,
        ),
    )(queries, keys, values)


def local(video_q, video_k, video_v, audio_q, audio_k, audio_v):
    width = video_q.shape[1]
    heads = width // HEAD_DIM
    groups = 4
    all_queries, ignored = gather_rows(audio_q)
    audio_calls = [
        (lambda q, g=g: audio_partial(q, video_k, video_v, g, groups), all_queries)
        for g in range(groups)
    ]
    gathered, parts = gather_rows(jnp.concatenate([audio_k, audio_v], axis=1), audio_calls)
    parts = parts + [call[0](all_queries) for call in audio_calls[len(parts) :]]
    all_keys = gathered[:, :width]
    all_values = gathered[:, width:]
    state = jnp.concatenate(
        [part[0] for part in parts] + [part[1] for part in parts] + [part[2] for part in parts],
        axis=1,
    )
    video_calls = [
        lambda earlier, g=g: video_part(video_q, all_keys, all_values, earlier, g, groups)
        for g in range(groups)
    ]
    mine, video_out = scatter_rows(state, heads, video_calls)
    audio_out = (mine[:, :width] / spread(mine[:, width : width + heads])).astype(jnp.bfloat16)
    return video_out, audio_out


def solution(mesh):
    placed = P(("groups", "seq"), None)
    return jax.shard_map(
        local,
        mesh=mesh,
        in_specs=(placed,) * 6,
        out_specs=(placed, placed),
        check_vma=False,
    )
```

```python
import jax
import jax.numpy as jnp
from jax import lax
from jax.experimental import pallas as pl
from jax.experimental.pallas import tpu as pltpu
from jax.sharding import PartitionSpec as P

HEAD_DIM = 64


def spread(scales):
    return jnp.repeat(scales, HEAD_DIM, axis=1)


def exchange(value, bit, count):
    pairs = [(source, source ^ bit) for source in range(count)]
    return lax.ppermute(value, "seq", pairs)


def gather_rows(block, during=()):
    count = lax.axis_size("seq")
    me = lax.axis_index("seq")
    held = block[None]
    results = []
    bit = count // 2
    step = 0
    while bit >= 1:
        work = during[step] if step < len(during) else None
        if work is not None:
            held, ready = lax.optimization_barrier((held, work[1]))
        arrived = exchange(held, bit, count)
        if work is not None:
            done = work[0](ready)
            arrived, done = lax.optimization_barrier((arrived, done))
            results.append(done)
        upper = (me & bit) != 0
        low = jnp.where(upper, arrived, held)
        high = jnp.where(upper, held, arrived)
        held = jnp.stack([low, high], axis=1).reshape((-1,) + block.shape)
        bit //= 2
        step += 1
    return held.reshape((count * block.shape[0],) + block.shape[1:]), results


def gather_levels(block):
    count = lax.axis_size("seq")
    me = lax.axis_index("seq")
    held = block[None]
    levels = []
    bit = count // 2
    if bit >= 2:
        levels.append((bit, bit // 2))
        bit //= 4
    while bit >= 1:
        levels.append((bit,))
        bit //= 2
    for level in levels:
        mask = sum(level)
        offsets = [0]
        for b in level:
            offsets = offsets + [o + b for o in offsets]
        pieces = {0: held}
        for offset in offsets[1:]:
            pairs = [(source, source ^ offset) for source in range(count)]
            pieces[offset] = lax.ppermute(held, "seq", pairs)
        mine = me & mask
        ordered = []
        for target in sorted(offsets):
            choice = pieces[0]
            for offset in offsets[1:]:
                choice = jnp.where((mine ^ offset) == target, pieces[offset], choice)
            ordered.append(choice)
        held = jnp.stack(ordered, axis=1).reshape((-1,) + block.shape)
    return held.reshape((count * block.shape[0],) + block.shape[1:])


def merge(first, second, heads):
    width = heads * HEAD_DIM
    top = jnp.maximum(first[:, width + heads :], second[:, width + heads :])
    first_scale = jnp.exp(first[:, width + heads :] - top)
    second_scale = jnp.exp(second[:, width + heads :] - top)
    totals = first[:, width : width + heads] * first_scale + second[:, width : width + heads] * second_scale
    summed = first[:, :width] * spread(first_scale) + second[:, :width] * spread(second_scale)
    return jnp.concatenate([summed, totals, top], axis=1)


def scatter_rows(state, heads, during=()):
    count = lax.axis_size("seq")
    me = lax.axis_index("seq")
    rows = state.shape[0] // count
    held = state.reshape((count, rows, state.shape[1]))
    carried = None
    bit = 1
    step = 0
    while bit < count:
        pairs = held.reshape((-1, 2, rows, state.shape[1]))
        upper = (me & bit) != 0
        keep = jnp.where(upper, pairs[:, 1], pairs[:, 0])
        give = jnp.where(upper, pairs[:, 0], pairs[:, 1])
        work = during[step] if step < len(during) else None
        if work is not None:
            give, carried = lax.optimization_barrier((give, carried))
        arrived = exchange(give, bit, count)
        if work is not None:
            carried = work(carried)
            arrived, carried = lax.optimization_barrier((arrived, carried))
        held = merge(
            keep.reshape((-1, state.shape[1])), arrived.reshape((-1, state.shape[1])), heads
        ).reshape((-1, rows, state.shape[1]))
        bit *= 2
        step += 1
    for work in during[step:]:
        carried = work(carried)
    return held.reshape((rows, state.shape[1])), carried


def head_masks(rows):
    lane = lax.broadcasted_iota(jnp.int32, (rows, 2 * HEAD_DIM), 1)
    return lane < HEAD_DIM


def split_pair(block):
    first = head_masks(block.shape[0])
    zeros = jnp.zeros_like(block)
    return jnp.concatenate([jnp.where(first, block, zeros), jnp.where(first, zeros, block)], axis=0)


def pair_attention(queries, keys, values):
    key_rows = keys.shape[0]
    scores = (
        lax.dot_general(
            queries, split_pair(keys), (((1,), (1,)), ((), ())), preferred_element_type=jnp.float32
        )
        * 0.125
    )
    weights = []
    tops = []
    counts = []
    for half in range(2):
        part = scores[:, half * key_rows : (half + 1) * key_rows]
        highest = jnp.max(part, axis=1, keepdims=True)
        exps = jnp.exp(part - highest)
        tops.append(highest)
        counts.append(jnp.sum(exps, axis=1, keepdims=True))
        weights.append(exps.astype(jnp.bfloat16))
    summed = jnp.dot(
        jnp.concatenate(weights, axis=1), split_pair(values), preferred_element_type=jnp.float32
    )
    return summed, tops, counts


def video_kernel(query_ref, key_ref, value_ref, *refs):
    out_ref = refs[-1]
    summed, tops, counts = pair_attention(query_ref[...], key_ref[...], value_ref[...])
    first = head_masks(summed.shape[0])
    totals = jnp.where(first, counts[0], counts[1])
    out_ref[...] = (summed / totals).astype(out_ref.dtype)


def video_part(queries, keys, values, earlier, group, groups):
    rows, width = queries.shape
    pairs = width // (2 * HEAD_DIM) // groups
    first_pair = group * pairs
    key_rows = keys.shape[0]
    specs = [
        pl.BlockSpec((rows, 2 * HEAD_DIM), lambda p: (0, p + first_pair)),
        pl.BlockSpec((key_rows, 2 * HEAD_DIM), lambda p: (0, p + first_pair)),
        pl.BlockSpec((key_rows, 2 * HEAD_DIM), lambda p: (0, p + first_pair)),
    ]
    operands = [queries, keys, values]
    aliases = {}
    if earlier is not None:
        specs.append(pl.BlockSpec(memory_space=pl.ANY))
        operands.append(earlier)
        aliases = {3: 0}
    return pl.pallas_call(
        video_kernel,
        grid=(pairs,),
        in_specs=specs,
        out_specs=pl.BlockSpec((rows, 2 * HEAD_DIM), lambda p: (0, p + first_pair)),
        out_shape=jax.ShapeDtypeStruct((rows, width), jnp.bfloat16),
        input_output_aliases=aliases,
        cost_estimate=pl.CostEstimate(
            flops=8 * rows * key_rows * width // groups,
            transcendentals=rows * key_rows * width // HEAD_DIM // groups,
            bytes_accessed=2 * (2 * rows * width + 2 * key_rows * width) // groups,
        ),
    )(*operands)


def audio_kernel(query_ref, key_ref, value_ref, sum_ref, total_ref, top_ref):
    pair = pl.program_id(0)

    @pl.when(pair == 0)
    def _():
        total_ref[...] = jnp.zeros_like(total_ref)
        top_ref[...] = jnp.zeros_like(top_ref)

    summed, tops, counts = pair_attention(query_ref[...], key_ref[...], value_ref[...])
    column = lax.broadcasted_iota(jnp.int32, total_ref.shape, 1)
    totals_now = total_ref[...]
    tops_now = top_ref[...]
    for half in range(2):
        here = column == 2 * pair + half
        totals_now = jnp.where(here, counts[half], totals_now)
        tops_now = jnp.where(here, tops[half], tops_now)
    total_ref[...] = totals_now
    top_ref[...] = tops_now
    sum_ref[...] = summed


def audio_partial(queries, keys, values, group, groups):
    rows, width = queries.shape
    heads = width // HEAD_DIM // groups
    first_pair = group * heads // 2
    key_rows = keys.shape[0]
    return pl.pallas_call(
        audio_kernel,
        grid=(heads // 2,),
        in_specs=[
            pl.BlockSpec((rows, 2 * HEAD_DIM), lambda p: (0, p + first_pair)),
            pl.BlockSpec((key_rows, 2 * HEAD_DIM), lambda p: (0, p + first_pair)),
            pl.BlockSpec((key_rows, 2 * HEAD_DIM), lambda p: (0, p + first_pair)),
        ],
        out_specs=[
            pl.BlockSpec((rows, 2 * HEAD_DIM), lambda p: (0, p)),
            pl.BlockSpec((rows, heads), lambda p: (0, 0)),
            pl.BlockSpec((rows, heads), lambda p: (0, 0)),
        ],
        out_shape=[
            jax.ShapeDtypeStruct((rows, heads * HEAD_DIM), jnp.float32),
            jax.ShapeDtypeStruct((rows, heads), jnp.float32),
            jax.ShapeDtypeStruct((rows, heads), jnp.float32),
        ],
        compiler_params=pltpu.CompilerParams(dimension_semantics=("arbitrary",)),
        cost_estimate=pl.CostEstimate(
            flops=8 * rows * key_rows * width // groups,
            transcendentals=rows * key_rows * heads,
            bytes_accessed=(2 * rows * width + 4 * key_rows * width + 4 * rows * width) // groups,
        ),
    )(queries, keys, values)


def local(video_q, video_k, video_v, audio_q, audio_k, audio_v):
    width = video_q.shape[1]
    heads = width // HEAD_DIM
    groups = 4
    all_queries = gather_levels(audio_q)
    audio_calls = [
        (lambda q, g=g: audio_partial(q, video_k, video_v, g, groups), all_queries)
        for g in range(groups)
    ]
    gathered, parts = gather_rows(jnp.concatenate([audio_k, audio_v], axis=1), audio_calls)
    parts = parts + [call[0](all_queries) for call in audio_calls[len(parts) :]]
    all_keys = gathered[:, :width]
    all_values = gathered[:, width:]
    state = jnp.concatenate(
        [part[0] for part in parts] + [part[1] for part in parts] + [part[2] for part in parts],
        axis=1,
    )
    video_calls = [
        lambda earlier, g=g: video_part(video_q, all_keys, all_values, earlier, g, groups)
        for g in range(groups)
    ]
    mine, video_out = scatter_rows(state, heads, video_calls)
    audio_out = (mine[:, :width] / spread(mine[:, width : width + heads])).astype(jnp.bfloat16)
    return video_out, audio_out


def solution(mesh):
    placed = P(("groups", "seq"), None)
    return jax.shard_map(
        local,
        mesh=mesh,
        in_specs=(placed,) * 6,
        out_specs=(placed, placed),
        check_vma=False,
    )
```

```python
import jax
import jax.numpy as jnp
from jax import lax
from jax.experimental import pallas as pl
from jax.experimental.pallas import tpu as pltpu
from jax.sharding import PartitionSpec as P

HEAD_DIM = 64


def spread(scales):
    return jnp.repeat(scales, HEAD_DIM, axis=1)


def exchange(value, bit, count):
    pairs = [(source, source ^ bit) for source in range(count)]
    return lax.ppermute(value, "seq", pairs)


def gather_rows(block, during=(), carried=None):
    count = lax.axis_size("seq")
    me = lax.axis_index("seq")
    held = block[None]
    bit = count // 2
    step = 0
    while bit >= 1:
        work = during[step] if step < len(during) else None
        if work is not None:
            held, carried = lax.optimization_barrier((held, carried))
        arrived = exchange(held, bit, count)
        if work is not None:
            carried = work(carried)
            arrived, carried = lax.optimization_barrier((arrived, carried))
        upper = (me & bit) != 0
        low = jnp.where(upper, arrived, held)
        high = jnp.where(upper, held, arrived)
        held = jnp.stack([low, high], axis=1).reshape((-1,) + block.shape)
        bit //= 2
        step += 1
    for work in during[step:]:
        carried = work(carried)
    return held.reshape((count * block.shape[0],) + block.shape[1:]), carried


def merge(first, second, heads):
    width = heads * HEAD_DIM
    top = jnp.maximum(first[:, width + heads :], second[:, width + heads :])
    first_scale = jnp.exp(first[:, width + heads :] - top)
    second_scale = jnp.exp(second[:, width + heads :] - top)
    totals = first[:, width : width + heads] * first_scale + second[:, width : width + heads] * second_scale
    summed = first[:, :width] * spread(first_scale) + second[:, :width] * spread(second_scale)
    return jnp.concatenate([summed, totals, top], axis=1)


def scatter_rows(state, heads, during=()):
    count = lax.axis_size("seq")
    me = lax.axis_index("seq")
    rows = state.shape[0] // count
    held = state.reshape((count, rows, state.shape[1]))
    carried = None
    bit = 1
    step = 0
    while bit < count:
        pairs = held.reshape((-1, 2, rows, state.shape[1]))
        upper = (me & bit) != 0
        keep = jnp.where(upper, pairs[:, 1], pairs[:, 0])
        give = jnp.where(upper, pairs[:, 0], pairs[:, 1])
        work = during[step] if step < len(during) else None
        if work is not None:
            give, carried = lax.optimization_barrier((give, carried))
        arrived = exchange(give, bit, count)
        if work is not None:
            carried = work(carried)
            arrived, carried = lax.optimization_barrier((arrived, carried))
        held = merge(
            keep.reshape((-1, state.shape[1])), arrived.reshape((-1, state.shape[1])), heads
        ).reshape((-1, rows, state.shape[1]))
        bit *= 2
        step += 1
    for work in during[step:]:
        carried = work(carried)
    return held.reshape((rows, state.shape[1])), carried


def head_masks(rows):
    lane = lax.broadcasted_iota(jnp.int32, (rows, 2 * HEAD_DIM), 1)
    return lane < HEAD_DIM


def split_pair(block):
    first = head_masks(block.shape[0])
    zeros = jnp.zeros_like(block)
    return jnp.concatenate([jnp.where(first, block, zeros), jnp.where(first, zeros, block)], axis=0)


def pair_attention(queries, keys, values):
    key_rows = keys.shape[0]
    scores = (
        lax.dot_general(
            queries, split_pair(keys), (((1,), (1,)), ((), ())), preferred_element_type=jnp.float32
        )
        * 0.125
    )
    weights = []
    tops = []
    counts = []
    for half in range(2):
        part = scores[:, half * key_rows : (half + 1) * key_rows]
        highest = jnp.max(part, axis=1, keepdims=True)
        exps = jnp.exp(part - highest)
        tops.append(highest)
        counts.append(jnp.sum(exps, axis=1, keepdims=True))
        weights.append(exps.astype(jnp.bfloat16))
    summed = jnp.dot(
        jnp.concatenate(weights, axis=1), split_pair(values), preferred_element_type=jnp.float32
    )
    return summed, tops, counts


def video_kernel(query_ref, key_ref, value_ref, *refs):
    out_ref = refs[-1]
    summed, tops, counts = pair_attention(query_ref[...], key_ref[...], value_ref[...])
    first = head_masks(summed.shape[0])
    totals = jnp.where(first, counts[0], counts[1])
    out_ref[...] = (summed / totals).astype(out_ref.dtype)


def video_part(queries, packed, earlier, group, groups):
    rows, width = queries.shape
    pairs = width // (2 * HEAD_DIM) // groups
    first_pair = group * pairs
    value_pair = first_pair + width // (2 * HEAD_DIM)
    key_rows = packed.shape[0]
    specs = [
        pl.BlockSpec((rows, 2 * HEAD_DIM), lambda p: (0, p + first_pair)),
        pl.BlockSpec((key_rows, 2 * HEAD_DIM), lambda p: (0, p + first_pair)),
        pl.BlockSpec((key_rows, 2 * HEAD_DIM), lambda p: (0, p + value_pair)),
    ]
    operands = [queries, packed, packed]
    aliases = {}
    if earlier is not None:
        specs.append(pl.BlockSpec(memory_space=pl.ANY))
        operands.append(earlier)
        aliases = {3: 0}
    return pl.pallas_call(
        video_kernel,
        grid=(pairs,),
        in_specs=specs,
        out_specs=pl.BlockSpec((rows, 2 * HEAD_DIM), lambda p: (0, p + first_pair)),
        out_shape=jax.ShapeDtypeStruct((rows, width), jnp.bfloat16),
        input_output_aliases=aliases,
        cost_estimate=pl.CostEstimate(
            flops=8 * rows * key_rows * width // groups,
            transcendentals=rows * key_rows * width // HEAD_DIM // groups,
            bytes_accessed=2 * (2 * rows * width + 2 * key_rows * width) // groups,
        ),
    )(*operands)


def audio_kernel(query_ref, key_ref, value_ref, *refs):
    sum_ref, total_ref, top_ref = refs[-3:]
    pair = pl.program_id(0)

    @pl.when(pair == 0)
    def _():
        total_ref[...] = jnp.zeros_like(total_ref)
        top_ref[...] = jnp.zeros_like(top_ref)

    summed, tops, counts = pair_attention(query_ref[...], key_ref[...], value_ref[...])
    column = lax.broadcasted_iota(jnp.int32, total_ref.shape, 1)
    totals_now = total_ref[...]
    tops_now = top_ref[...]
    for half in range(2):
        here = column == 2 * pair + half
        totals_now = jnp.where(here, counts[half], totals_now)
        tops_now = jnp.where(here, tops[half], tops_now)
    total_ref[...] = totals_now
    top_ref[...] = tops_now
    sum_ref[...] = summed


def audio_part(queries, keys, values, earlier, group, groups):
    rows, width = queries.shape
    heads = width // HEAD_DIM // groups
    first_pair = group * heads // 2
    key_rows = keys.shape[0]
    state_width = width + 2 * width // HEAD_DIM
    specs = [
        pl.BlockSpec((rows, 2 * HEAD_DIM), lambda p: (0, p + first_pair)),
        pl.BlockSpec((key_rows, 2 * HEAD_DIM), lambda p: (0, p + first_pair)),
        pl.BlockSpec((key_rows, 2 * HEAD_DIM), lambda p: (0, p + first_pair)),
    ]
    operands = [queries, keys, values]
    aliases = {}
    if earlier is not None:
        specs.append(pl.BlockSpec(memory_space=pl.ANY))
        operands.append(earlier)
        aliases = {3: 0}
    return pl.pallas_call(
        audio_kernel,
        grid=(heads // 2,),
        in_specs=specs,
        out_specs=[
            pl.BlockSpec((rows, 2 * HEAD_DIM), lambda p: (0, p + first_pair)),
            pl.BlockSpec((rows, heads), lambda p: (0, 0)),
            pl.BlockSpec((rows, heads), lambda p: (0, 0)),
        ],
        out_shape=[
            jax.ShapeDtypeStruct((rows, state_width), jnp.float32),
            jax.ShapeDtypeStruct((rows, heads), jnp.float32),
            jax.ShapeDtypeStruct((rows, heads), jnp.float32),
        ],
        input_output_aliases=aliases,
        compiler_params=pltpu.CompilerParams(dimension_semantics=("arbitrary",)),
        cost_estimate=pl.CostEstimate(
            flops=8 * rows * key_rows * width // groups,
            transcendentals=rows * key_rows * heads,
            bytes_accessed=(2 * rows * width + 4 * key_rows * width + 4 * rows * width) // groups,
        ),
    )(*operands)


def local(video_q, video_k, video_v, audio_q, audio_k, audio_v):
    width = video_q.shape[1]
    heads = width // HEAD_DIM
    groups = 4
    all_queries, ignored = gather_rows(audio_q)

    def audio_step(carried, g):
        queries, state, totals, tops = carried
        state, total, top = audio_part(queries, video_k, video_v, state, g, groups)
        return queries, state, totals + (total,), tops + (top,)

    audio_calls = [lambda c, g=g: audio_step(c, g) for g in range(groups)]
    packed, (ignored, state, totals, tops) = gather_rows(
        jnp.concatenate([audio_k, audio_v], axis=1), audio_calls, (all_queries, None, (), ())
    )
    state = lax.dynamic_update_slice(
        state, jnp.concatenate(totals + tops, axis=1), (0, width)
    )
    video_calls = [
        lambda earlier, g=g: video_part(video_q, packed, earlier, g, groups)
        for g in range(groups)
    ]
    mine, video_out = scatter_rows(state, heads, video_calls)
    audio_out = (mine[:, :width] / spread(mine[:, width : width + heads])).astype(jnp.bfloat16)
    return video_out, audio_out


def solution(mesh):
    placed = P(("groups", "seq"), None)
    return jax.shard_map(
        local,
        mesh=mesh,
        in_specs=(placed,) * 6,
        out_specs=(placed, placed),
        check_vma=False,
    )
```

```python
import jax
import jax.numpy as jnp
from jax import lax
from jax.experimental import pallas as pl
from jax.experimental.pallas import tpu as pltpu
from jax.sharding import PartitionSpec as P

HEAD_DIM = 64


def spread(scales):
    return jnp.repeat(scales, HEAD_DIM, axis=1)


def exchange(value, bit, count):
    pairs = [(source, source ^ bit) for source in range(count)]
    return lax.ppermute(value, "seq", pairs)


def gather_rows(block, during=()):
    count = lax.axis_size("seq")
    me = lax.axis_index("seq")
    held = block[None]
    results = []
    bit = count // 2
    step = 0
    while bit >= 1:
        work = during[step] if step < len(during) else None
        if work is not None:
            held, ready = lax.optimization_barrier((held, work[1]))
        arrived = exchange(held, bit, count)
        if work is not None:
            done = work[0](ready)
            arrived, done = lax.optimization_barrier((arrived, done))
            results.append(done)
        upper = (me & bit) != 0
        low = jnp.where(upper, arrived, held)
        high = jnp.where(upper, held, arrived)
        held = jnp.stack([low, high], axis=1).reshape((-1,) + block.shape)
        bit //= 2
        step += 1
    return held.reshape((count * block.shape[0],) + block.shape[1:]), results


def gather_levels(block):
    count = lax.axis_size("seq")
    me = lax.axis_index("seq")
    held = block[None]
    levels = []
    bit = count // 2
    if bit >= 2:
        levels.append((bit, bit // 2))
        bit //= 4
    while bit >= 1:
        levels.append((bit,))
        bit //= 2
    for level in levels:
        mask = sum(level)
        offsets = [0]
        for b in level:
            offsets = offsets + [o + b for o in offsets]
        pieces = {0: held}
        for offset in offsets[1:]:
            pairs = [(source, source ^ offset) for source in range(count)]
            pieces[offset] = lax.ppermute(held, "seq", pairs)
        mine = me & mask
        ordered = []
        for target in sorted(offsets):
            choice = pieces[0]
            for offset in offsets[1:]:
                choice = jnp.where((mine ^ offset) == target, pieces[offset], choice)
            ordered.append(choice)
        held = jnp.stack(ordered, axis=1).reshape((-1,) + block.shape)
    return held.reshape((count * block.shape[0],) + block.shape[1:])


def merge(first, second, heads):
    width = heads * HEAD_DIM
    top = jnp.maximum(first[:, width + heads :], second[:, width + heads :])
    first_scale = jnp.exp(first[:, width + heads :] - top)
    second_scale = jnp.exp(second[:, width + heads :] - top)
    totals = first[:, width : width + heads] * first_scale + second[:, width : width + heads] * second_scale
    summed = first[:, :width] * spread(first_scale) + second[:, :width] * spread(second_scale)
    return jnp.concatenate([summed, totals, top], axis=1)


def scatter_rows(state, heads, during=()):
    count = lax.axis_size("seq")
    me = lax.axis_index("seq")
    rows = state.shape[0] // count
    held = state.reshape((count, rows, state.shape[1]))
    carried = None
    bit = 1
    step = 0
    while bit < count:
        pairs = held.reshape((-1, 2, rows, state.shape[1]))
        upper = (me & bit) != 0
        keep = jnp.where(upper, pairs[:, 1], pairs[:, 0])
        give = jnp.where(upper, pairs[:, 0], pairs[:, 1])
        work = during[step] if step < len(during) else None
        if work is not None:
            give, carried = lax.optimization_barrier((give, carried))
        arrived = exchange(give, bit, count)
        if work is not None:
            carried = work(carried)
            arrived, carried = lax.optimization_barrier((arrived, carried))
        held = merge(
            keep.reshape((-1, state.shape[1])), arrived.reshape((-1, state.shape[1])), heads
        ).reshape((-1, rows, state.shape[1]))
        bit *= 2
        step += 1
    for work in during[step:]:
        carried = work(carried)
    return held.reshape((rows, state.shape[1])), carried


def head_masks(rows):
    lane = lax.broadcasted_iota(jnp.int32, (rows, 2 * HEAD_DIM), 1)
    return lane < HEAD_DIM


def split_pair(block):
    first = head_masks(block.shape[0])
    zeros = jnp.zeros_like(block)
    return jnp.concatenate([jnp.where(first, block, zeros), jnp.where(first, zeros, block)], axis=0)


def pair_attention(queries, keys, values):
    key_rows = keys.shape[0]
    scores = (
        lax.dot_general(
            queries, split_pair(keys), (((1,), (1,)), ((), ())), preferred_element_type=jnp.float32
        )
        * 0.125
    )
    weights = []
    tops = []
    counts = []
    for half in range(2):
        part = scores[:, half * key_rows : (half + 1) * key_rows]
        highest = jnp.max(part, axis=1, keepdims=True)
        exps = jnp.exp(part - highest)
        tops.append(highest)
        counts.append(jnp.sum(exps, axis=1, keepdims=True))
        weights.append(exps.astype(jnp.bfloat16))
    summed = jnp.dot(
        jnp.concatenate(weights, axis=1), split_pair(values), preferred_element_type=jnp.float32
    )
    return summed, tops, counts


def video_kernel(query_ref, key_ref, value_ref, *refs):
    out_ref = refs[-1]
    queries = query_ref[...]
    key_rows = key_ref.shape[0]
    scores = (
        lax.dot_general(
            split_pair(key_ref[...]), queries, (((1,), (1,)), ((), ())),
            preferred_element_type=jnp.float32,
        )
        * 0.125
    )
    weights = []
    counts = []
    for half in range(2):
        part = scores[half * key_rows : (half + 1) * key_rows]
        highest = jnp.max(part, axis=0, keepdims=True)
        exps = jnp.exp(part - highest)
        counts.append(jnp.sum(exps, axis=0, keepdims=True))
        weights.append(exps.astype(jnp.bfloat16))
    summed = lax.dot_general(
        split_pair(value_ref[...]), jnp.concatenate(weights, axis=0), (((0,), (0,)), ((), ())),
        preferred_element_type=jnp.float32,
    )
    lane = lax.broadcasted_iota(jnp.int32, summed.shape, 0)
    totals = jnp.where(lane < HEAD_DIM, counts[0], counts[1])
    out_ref[...] = (summed / totals).T.astype(out_ref.dtype)


def video_part(queries, keys, values, earlier, group, groups):
    rows, width = queries.shape
    pairs = width // (2 * HEAD_DIM) // groups
    first_pair = group * pairs
    key_rows = keys.shape[0]
    specs = [
        pl.BlockSpec((rows, 2 * HEAD_DIM), lambda p: (0, p + first_pair)),
        pl.BlockSpec((key_rows, 2 * HEAD_DIM), lambda p: (0, p + first_pair)),
        pl.BlockSpec((key_rows, 2 * HEAD_DIM), lambda p: (0, p + first_pair)),
    ]
    operands = [queries, keys, values]
    aliases = {}
    if earlier is not None:
        specs.append(pl.BlockSpec(memory_space=pl.ANY))
        operands.append(earlier)
        aliases = {3: 0}
    return pl.pallas_call(
        video_kernel,
        grid=(pairs,),
        in_specs=specs,
        out_specs=pl.BlockSpec((rows, 2 * HEAD_DIM), lambda p: (0, p + first_pair)),
        out_shape=jax.ShapeDtypeStruct((rows, width), jnp.bfloat16),
        input_output_aliases=aliases,
        cost_estimate=pl.CostEstimate(
            flops=8 * rows * key_rows * width // groups,
            transcendentals=rows * key_rows * width // HEAD_DIM // groups,
            bytes_accessed=2 * (2 * rows * width + 2 * key_rows * width) // groups,
        ),
    )(*operands)


def audio_kernel(query_ref, key_ref, value_ref, sum_ref, total_ref, top_ref):
    pair = pl.program_id(0)

    @pl.when(pair == 0)
    def _():
        total_ref[...] = jnp.zeros_like(total_ref)
        top_ref[...] = jnp.zeros_like(top_ref)

    summed, tops, counts = pair_attention(query_ref[...], key_ref[...], value_ref[...])
    column = lax.broadcasted_iota(jnp.int32, total_ref.shape, 1)
    totals_now = total_ref[...]
    tops_now = top_ref[...]
    for half in range(2):
        here = column == 2 * pair + half
        totals_now = jnp.where(here, counts[half], totals_now)
        tops_now = jnp.where(here, tops[half], tops_now)
    total_ref[...] = totals_now
    top_ref[...] = tops_now
    sum_ref[...] = summed


def audio_partial(queries, keys, values, group, groups):
    rows, width = queries.shape
    heads = width // HEAD_DIM // groups
    first_pair = group * heads // 2
    key_rows = keys.shape[0]
    return pl.pallas_call(
        audio_kernel,
        grid=(heads // 2,),
        in_specs=[
            pl.BlockSpec((rows, 2 * HEAD_DIM), lambda p: (0, p + first_pair)),
            pl.BlockSpec((key_rows, 2 * HEAD_DIM), lambda p: (0, p + first_pair)),
            pl.BlockSpec((key_rows, 2 * HEAD_DIM), lambda p: (0, p + first_pair)),
        ],
        out_specs=[
            pl.BlockSpec((rows, 2 * HEAD_DIM), lambda p: (0, p)),
            pl.BlockSpec((rows, heads), lambda p: (0, 0)),
            pl.BlockSpec((rows, heads), lambda p: (0, 0)),
        ],
        out_shape=[
            jax.ShapeDtypeStruct((rows, heads * HEAD_DIM), jnp.float32),
            jax.ShapeDtypeStruct((rows, heads), jnp.float32),
            jax.ShapeDtypeStruct((rows, heads), jnp.float32),
        ],
        compiler_params=pltpu.CompilerParams(dimension_semantics=("arbitrary",)),
        cost_estimate=pl.CostEstimate(
            flops=8 * rows * key_rows * width // groups,
            transcendentals=rows * key_rows * heads,
            bytes_accessed=(2 * rows * width + 4 * key_rows * width + 4 * rows * width) // groups,
        ),
    )(queries, keys, values)


def local(video_q, video_k, video_v, audio_q, audio_k, audio_v):
    width = video_q.shape[1]
    heads = width // HEAD_DIM
    groups = 4
    all_queries = gather_levels(audio_q)
    audio_calls = [
        (lambda q, g=g: audio_partial(q, video_k, video_v, g, groups), all_queries)
        for g in range(groups)
    ]
    gathered, parts = gather_rows(jnp.concatenate([audio_k, audio_v], axis=1), audio_calls)
    parts = parts + [call[0](all_queries) for call in audio_calls[len(parts) :]]
    all_keys = gathered[:, :width]
    all_values = gathered[:, width:]
    state = jnp.concatenate(
        [part[0] for part in parts] + [part[1] for part in parts] + [part[2] for part in parts],
        axis=1,
    )
    video_calls = [
        lambda earlier, g=g: video_part(video_q, all_keys, all_values, earlier, g, groups)
        for g in range(groups)
    ]
    mine, video_out = scatter_rows(state, heads, video_calls)
    audio_out = (mine[:, :width] / spread(mine[:, width : width + heads])).astype(jnp.bfloat16)
    return video_out, audio_out


def solution(mesh):
    placed = P(("groups", "seq"), None)
    return jax.shard_map(
        local,
        mesh=mesh,
        in_specs=(placed,) * 6,
        out_specs=(placed, placed),
        check_vma=False,
    )
```

```python
import jax
import jax.numpy as jnp
from jax import lax
from jax.experimental import pallas as pl
from jax.experimental.pallas import tpu as pltpu
from jax.sharding import PartitionSpec as P

HEAD_DIM = 64


def spread(scales):
    return jnp.repeat(scales, HEAD_DIM, axis=1)


def exchange(value, bit, count):
    pairs = [(source, source ^ bit) for source in range(count)]
    return lax.ppermute(value, "seq", pairs)


def gather_rows(block, during=()):
    count = lax.axis_size("seq")
    me = lax.axis_index("seq")
    held = block[None]
    results = []
    bit = count // 2
    step = 0
    while bit >= 1:
        work = during[step] if step < len(during) else None
        if work is not None:
            held, ready = lax.optimization_barrier((held, work[1]))
        arrived = exchange(held, bit, count)
        if work is not None:
            done = work[0](ready)
            arrived, done = lax.optimization_barrier((arrived, done))
            results.append(done)
        upper = (me & bit) != 0
        low = jnp.where(upper, arrived, held)
        high = jnp.where(upper, held, arrived)
        held = jnp.stack([low, high], axis=1).reshape((-1,) + block.shape)
        bit //= 2
        step += 1
    return held.reshape((count * block.shape[0],) + block.shape[1:]), results


def gather_levels(block):
    count = lax.axis_size("seq")
    me = lax.axis_index("seq")
    held = block[None]
    levels = []
    bit = count // 2
    if bit >= 2:
        levels.append((bit, bit // 2))
        bit //= 4
    while bit >= 1:
        levels.append((bit,))
        bit //= 2
    for level in levels:
        mask = sum(level)
        offsets = [0]
        for b in level:
            offsets = offsets + [o + b for o in offsets]
        pieces = {0: held}
        for offset in offsets[1:]:
            pairs = [(source, source ^ offset) for source in range(count)]
            pieces[offset] = lax.ppermute(held, "seq", pairs)
        mine = me & mask
        ordered = []
        for target in sorted(offsets):
            choice = pieces[0]
            for offset in offsets[1:]:
                choice = jnp.where((mine ^ offset) == target, pieces[offset], choice)
            ordered.append(choice)
        held = jnp.stack(ordered, axis=1).reshape((-1,) + block.shape)
    return held.reshape((count * block.shape[0],) + block.shape[1:])


def merge(first, second, heads):
    width = heads * HEAD_DIM
    top = jnp.maximum(first[:, width + heads :], second[:, width + heads :])
    first_scale = jnp.exp(first[:, width + heads :] - top)
    second_scale = jnp.exp(second[:, width + heads :] - top)
    totals = first[:, width : width + heads] * first_scale + second[:, width : width + heads] * second_scale
    summed = first[:, :width] * spread(first_scale) + second[:, :width] * spread(second_scale)
    return jnp.concatenate([summed, totals, top], axis=1)


def scatter_rows(state, heads, during=()):
    count = lax.axis_size("seq")
    me = lax.axis_index("seq")
    rows = state.shape[0] // count
    held = state.reshape((count, rows, state.shape[1]))
    carried = None
    bit = 1
    step = 0
    while bit < count:
        pairs = held.reshape((-1, 2, rows, state.shape[1]))
        upper = (me & bit) != 0
        keep = jnp.where(upper, pairs[:, 1], pairs[:, 0])
        give = jnp.where(upper, pairs[:, 0], pairs[:, 1])
        work = during[step] if step < len(during) else None
        if work is not None:
            give, carried = lax.optimization_barrier((give, carried))
        arrived = exchange(give, bit, count)
        if work is not None:
            carried = work(carried)
            arrived, carried = lax.optimization_barrier((arrived, carried))
        held = merge(
            keep.reshape((-1, state.shape[1])), arrived.reshape((-1, state.shape[1])), heads
        ).reshape((-1, rows, state.shape[1]))
        bit *= 2
        step += 1
    for work in during[step:]:
        carried = work(carried)
    return held.reshape((rows, state.shape[1])), carried


def head_masks(rows):
    lane = lax.broadcasted_iota(jnp.int32, (rows, 2 * HEAD_DIM), 1)
    return lane < HEAD_DIM


def split_pair(block):
    first = head_masks(block.shape[0])
    zeros = jnp.zeros_like(block)
    return jnp.concatenate([jnp.where(first, block, zeros), jnp.where(first, zeros, block)], axis=0)


def pair_attention(queries, keys, values):
    key_rows = keys.shape[0]
    scores = (
        lax.dot_general(
            queries, split_pair(keys), (((1,), (1,)), ((), ())), preferred_element_type=jnp.float32
        )
        * 0.125
    )
    weights = []
    tops = []
    counts = []
    for half in range(2):
        part = scores[:, half * key_rows : (half + 1) * key_rows]
        highest = jnp.max(part, axis=1, keepdims=True)
        exps = jnp.exp(part - highest)
        tops.append(highest)
        counts.append(jnp.sum(exps, axis=1, keepdims=True))
        weights.append(exps.astype(jnp.bfloat16))
    summed = jnp.dot(
        jnp.concatenate(weights, axis=1), split_pair(values), preferred_element_type=jnp.float32
    )
    return summed, tops, counts


PER_STEP = 2


def video_kernel(query_ref, key_ref, value_ref, *refs):
    out_ref = refs[-1]
    key_rows = key_ref.shape[0]
    for sub in range(PER_STEP):
        lanes = slice(sub * 2 * HEAD_DIM, (sub + 1) * 2 * HEAD_DIM)
        queries = query_ref[:, lanes]
        scores = (
            lax.dot_general(
                split_pair(key_ref[:, lanes]), queries, (((1,), (1,)), ((), ())),
                preferred_element_type=jnp.float32,
            )
            * 0.125
        )
        weights = []
        counts = []
        for half in range(2):
            part = scores[half * key_rows : (half + 1) * key_rows]
            highest = jnp.max(part, axis=0, keepdims=True)
            exps = jnp.exp(part - highest)
            counts.append(jnp.sum(exps, axis=0, keepdims=True))
            weights.append(exps.astype(jnp.bfloat16))
        summed = lax.dot_general(
            split_pair(value_ref[:, lanes]), jnp.concatenate(weights, axis=0),
            (((0,), (0,)), ((), ())), preferred_element_type=jnp.float32,
        )
        lane = lax.broadcasted_iota(jnp.int32, summed.shape, 0)
        totals = jnp.where(lane < HEAD_DIM, counts[0], counts[1])
        out_ref[:, lanes] = (summed / totals).T.astype(out_ref.dtype)


def video_part(queries, keys, values, earlier, group, groups):
    rows, width = queries.shape
    pairs = width // (2 * HEAD_DIM) // groups
    first_pair = group * pairs // PER_STEP
    key_rows = keys.shape[0]
    lanes = 2 * HEAD_DIM * PER_STEP
    specs = [
        pl.BlockSpec((rows, lanes), lambda p: (0, p + first_pair)),
        pl.BlockSpec((key_rows, lanes), lambda p: (0, p + first_pair)),
        pl.BlockSpec((key_rows, lanes), lambda p: (0, p + first_pair)),
    ]
    operands = [queries, keys, values]
    aliases = {}
    if earlier is not None:
        specs.append(pl.BlockSpec(memory_space=pl.ANY))
        operands.append(earlier)
        aliases = {3: 0}
    return pl.pallas_call(
        video_kernel,
        grid=(pairs // PER_STEP,),
        in_specs=specs,
        out_specs=pl.BlockSpec((rows, lanes), lambda p: (0, p + first_pair)),
        out_shape=jax.ShapeDtypeStruct((rows, width), jnp.bfloat16),
        input_output_aliases=aliases,
        cost_estimate=pl.CostEstimate(
            flops=8 * rows * key_rows * width // groups,
            transcendentals=rows * key_rows * width // HEAD_DIM // groups,
            bytes_accessed=2 * (2 * rows * width + 2 * key_rows * width) // groups,
        ),
    )(*operands)


def audio_kernel(query_ref, key_ref, value_ref, sum_ref, total_ref, top_ref):
    step = pl.program_id(0)

    @pl.when(step == 0)
    def _():
        total_ref[...] = jnp.zeros_like(total_ref)
        top_ref[...] = jnp.zeros_like(top_ref)

    column = lax.broadcasted_iota(jnp.int32, total_ref.shape, 1)
    totals_now = total_ref[...]
    tops_now = top_ref[...]
    for sub in range(PER_STEP):
        lanes = slice(sub * 2 * HEAD_DIM, (sub + 1) * 2 * HEAD_DIM)
        summed, tops, counts = pair_attention(
            query_ref[:, lanes], key_ref[:, lanes], value_ref[:, lanes]
        )
        for half in range(2):
            here = column == 2 * (step * PER_STEP + sub) + half
            totals_now = jnp.where(here, counts[half], totals_now)
            tops_now = jnp.where(here, tops[half], tops_now)
        sum_ref[:, lanes] = summed
    total_ref[...] = totals_now
    top_ref[...] = tops_now


def audio_partial(queries, keys, values, group, groups):
    rows, width = queries.shape
    heads = width // HEAD_DIM // groups
    first_pair = group * heads // 2 // PER_STEP
    lanes = 2 * HEAD_DIM * PER_STEP
    key_rows = keys.shape[0]
    return pl.pallas_call(
        audio_kernel,
        grid=(heads // 2 // PER_STEP,),
        in_specs=[
            pl.BlockSpec((rows, lanes), lambda p: (0, p + first_pair)),
            pl.BlockSpec((key_rows, lanes), lambda p: (0, p + first_pair)),
            pl.BlockSpec((key_rows, lanes), lambda p: (0, p + first_pair)),
        ],
        out_specs=[
            pl.BlockSpec((rows, lanes), lambda p: (0, p)),
            pl.BlockSpec((rows, heads), lambda p: (0, 0)),
            pl.BlockSpec((rows, heads), lambda p: (0, 0)),
        ],
        out_shape=[
            jax.ShapeDtypeStruct((rows, heads * HEAD_DIM), jnp.float32),
            jax.ShapeDtypeStruct((rows, heads), jnp.float32),
            jax.ShapeDtypeStruct((rows, heads), jnp.float32),
        ],
        compiler_params=pltpu.CompilerParams(dimension_semantics=("arbitrary",)),
        cost_estimate=pl.CostEstimate(
            flops=8 * rows * key_rows * width // groups,
            transcendentals=rows * key_rows * heads,
            bytes_accessed=(2 * rows * width + 4 * key_rows * width + 4 * rows * width) // groups,
        ),
    )(queries, keys, values)


def local(video_q, video_k, video_v, audio_q, audio_k, audio_v):
    width = video_q.shape[1]
    heads = width // HEAD_DIM
    groups = 4
    all_queries = gather_levels(audio_q)
    audio_calls = [
        (lambda q, g=g: audio_partial(q, video_k, video_v, g, groups), all_queries)
        for g in range(groups)
    ]
    gathered, parts = gather_rows(jnp.concatenate([audio_k, audio_v], axis=1), audio_calls)
    parts = parts + [call[0](all_queries) for call in audio_calls[len(parts) :]]
    all_keys = gathered[:, :width]
    all_values = gathered[:, width:]
    state = jnp.concatenate(
        [part[0] for part in parts] + [part[1] for part in parts] + [part[2] for part in parts],
        axis=1,
    )
    video_calls = [
        lambda earlier, g=g: video_part(video_q, all_keys, all_values, earlier, g, groups)
        for g in range(groups)
    ]
    mine, video_out = scatter_rows(state, heads, video_calls)
    audio_out = (mine[:, :width] / spread(mine[:, width : width + heads])).astype(jnp.bfloat16)
    return video_out, audio_out


def solution(mesh):
    placed = P(("groups", "seq"), None)
    return jax.shard_map(
        local,
        mesh=mesh,
        in_specs=(placed,) * 6,
        out_specs=(placed, placed),
        check_vma=False,
    )
```

```python
import jax
import jax.numpy as jnp
from jax import lax
from jax.experimental import pallas as pl
from jax.experimental.pallas import tpu as pltpu
from jax.sharding import PartitionSpec as P

HEAD_DIM = 64


def spread(scales):
    return jnp.repeat(scales, HEAD_DIM, axis=1)


def exchange(value, bit, count):
    pairs = [(source, source ^ bit) for source in range(count)]
    return lax.ppermute(value, "seq", pairs)


def merge(first, second, heads):
    width = heads * HEAD_DIM
    top = jnp.maximum(first[:, width + heads :], second[:, width + heads :])
    first_scale = jnp.exp(first[:, width + heads :] - top)
    second_scale = jnp.exp(second[:, width + heads :] - top)
    totals = first[:, width : width + heads] * first_scale + second[:, width : width + heads] * second_scale
    summed = first[:, :width] * spread(first_scale) + second[:, :width] * spread(second_scale)
    return jnp.concatenate([summed, totals, top], axis=1)


def scatter_rows(state, heads, during=()):
    count = lax.axis_size("seq")
    me = lax.axis_index("seq")
    rows = state.shape[0] // count
    held = state.reshape((count, rows, state.shape[1]))
    carried = None
    bit = 1
    step = 0
    while bit < count:
        pairs = held.reshape((-1, 2, rows, state.shape[1]))
        upper = (me & bit) != 0
        keep = jnp.where(upper, pairs[:, 1], pairs[:, 0])
        give = jnp.where(upper, pairs[:, 0], pairs[:, 1])
        work = during[step] if step < len(during) else None
        if work is not None:
            give, carried = lax.optimization_barrier((give, carried))
        arrived = exchange(give, bit, count)
        if work is not None:
            carried = work(carried)
            arrived, carried = lax.optimization_barrier((arrived, carried))
        held = merge(
            keep.reshape((-1, state.shape[1])), arrived.reshape((-1, state.shape[1])), heads
        ).reshape((-1, rows, state.shape[1]))
        bit *= 2
        step += 1
    for work in during[step:]:
        carried = work(carried)
    return held.reshape((rows, state.shape[1])), carried


def head_masks(rows):
    lane = lax.broadcasted_iota(jnp.int32, (rows, 2 * HEAD_DIM), 1)
    return lane < HEAD_DIM


def split_pair(block):
    first = head_masks(block.shape[0])
    zeros = jnp.zeros_like(block)
    return jnp.concatenate([jnp.where(first, block, zeros), jnp.where(first, zeros, block)], axis=0)


def pair_attention(queries, keys, values):
    key_rows = keys.shape[0]
    scores = (
        lax.dot_general(
            queries, split_pair(keys), (((1,), (1,)), ((), ())), preferred_element_type=jnp.float32
        )
        * 0.125
    )
    weights = []
    tops = []
    counts = []
    for half in range(2):
        part = scores[:, half * key_rows : (half + 1) * key_rows]
        highest = jnp.max(part, axis=1, keepdims=True)
        exps = jnp.exp(part - highest)
        tops.append(highest)
        counts.append(jnp.sum(exps, axis=1, keepdims=True))
        weights.append(exps.astype(jnp.bfloat16))
    summed = jnp.dot(
        jnp.concatenate(weights, axis=1), split_pair(values), preferred_element_type=jnp.float32
    )
    return summed, tops, counts


PER_STEP = 2


def video_kernel(query_ref, key_ref, value_ref, *refs):
    out_ref = refs[-1]
    key_rows = key_ref.shape[0]
    for sub in range(PER_STEP):
        lanes = slice(sub * 2 * HEAD_DIM, (sub + 1) * 2 * HEAD_DIM)
        queries = query_ref[:, lanes]
        scores = (
            lax.dot_general(
                split_pair(key_ref[:, lanes]), queries, (((1,), (1,)), ((), ())),
                preferred_element_type=jnp.float32,
            )
            * 0.125
        )
        weights = []
        counts = []
        for half in range(2):
            part = scores[half * key_rows : (half + 1) * key_rows]
            highest = jnp.max(part, axis=0, keepdims=True)
            exps = jnp.exp(part - highest)
            counts.append(jnp.sum(exps, axis=0, keepdims=True))
            weights.append(exps.astype(jnp.bfloat16))
        summed = lax.dot_general(
            split_pair(value_ref[:, lanes]), jnp.concatenate(weights, axis=0),
            (((0,), (0,)), ((), ())), preferred_element_type=jnp.float32,
        )
        lane = lax.broadcasted_iota(jnp.int32, summed.shape, 0)
        totals = jnp.where(lane < HEAD_DIM, counts[0], counts[1])
        out_ref[:, lanes] = (summed / totals).T.astype(out_ref.dtype)


def video_part(queries, gathered, earlier, group, groups):
    rows, width = queries.shape
    pairs = width // (2 * HEAD_DIM) // groups
    first_pair = group * pairs // PER_STEP
    key_rows = gathered.shape[0]
    blocks = width // (2 * HEAD_DIM * PER_STEP)
    lanes = 2 * HEAD_DIM * PER_STEP
    specs = [
        pl.BlockSpec((rows, lanes), lambda p: (0, p + first_pair)),
        pl.BlockSpec((key_rows, lanes), lambda p: (0, p + first_pair + blocks)),
        pl.BlockSpec((key_rows, lanes), lambda p: (0, p + first_pair + 2 * blocks)),
    ]
    operands = [queries, gathered, gathered]
    aliases = {}
    if earlier is not None:
        specs.append(pl.BlockSpec(memory_space=pl.ANY))
        operands.append(earlier)
        aliases = {3: 0}
    return pl.pallas_call(
        video_kernel,
        grid=(pairs // PER_STEP,),
        in_specs=specs,
        out_specs=pl.BlockSpec((rows, lanes), lambda p: (0, p + first_pair)),
        out_shape=jax.ShapeDtypeStruct((rows, width), jnp.bfloat16),
        input_output_aliases=aliases,
        cost_estimate=pl.CostEstimate(
            flops=8 * rows * key_rows * width // groups,
            transcendentals=rows * key_rows * width // HEAD_DIM // groups,
            bytes_accessed=2 * (2 * rows * width + 2 * key_rows * width) // groups,
        ),
    )(*operands)


def audio_kernel(query_ref, key_ref, value_ref, sum_ref, total_ref, top_ref):
    step = pl.program_id(0)

    @pl.when(step == 0)
    def _():
        total_ref[...] = jnp.zeros_like(total_ref)
        top_ref[...] = jnp.zeros_like(top_ref)

    column = lax.broadcasted_iota(jnp.int32, total_ref.shape, 1)
    totals_now = total_ref[...]
    tops_now = top_ref[...]
    for sub in range(PER_STEP):
        lanes = slice(sub * 2 * HEAD_DIM, (sub + 1) * 2 * HEAD_DIM)
        summed, tops, counts = pair_attention(
            query_ref[:, lanes], key_ref[:, lanes], value_ref[:, lanes]
        )
        for half in range(2):
            here = column == 2 * (step * PER_STEP + sub) + half
            totals_now = jnp.where(here, counts[half], totals_now)
            tops_now = jnp.where(here, tops[half], tops_now)
        sum_ref[:, lanes] = summed
    total_ref[...] = totals_now
    top_ref[...] = tops_now


def audio_rows(packed, keys, values):
    rows = packed.shape[0]
    width = keys.shape[1]
    heads = width // HEAD_DIM
    key_rows = keys.shape[0]
    lanes = 2 * HEAD_DIM * PER_STEP
    summed, totals, tops = pl.pallas_call(
        audio_kernel,
        grid=(heads // 2 // PER_STEP,),
        in_specs=[
            pl.BlockSpec((rows, lanes), lambda p: (0, p)),
            pl.BlockSpec((key_rows, lanes), lambda p: (0, p)),
            pl.BlockSpec((key_rows, lanes), lambda p: (0, p)),
        ],
        out_specs=[
            pl.BlockSpec((rows, lanes), lambda p: (0, p)),
            pl.BlockSpec((rows, heads), lambda p: (0, 0)),
            pl.BlockSpec((rows, heads), lambda p: (0, 0)),
        ],
        out_shape=[
            jax.ShapeDtypeStruct((rows, width), jnp.float32),
            jax.ShapeDtypeStruct((rows, heads), jnp.float32),
            jax.ShapeDtypeStruct((rows, heads), jnp.float32),
        ],
        compiler_params=pltpu.CompilerParams(dimension_semantics=("arbitrary",)),
        cost_estimate=pl.CostEstimate(
            flops=8 * rows * key_rows * width,
            transcendentals=rows * key_rows * heads,
            bytes_accessed=2 * rows * width + 4 * key_rows * width + 4 * rows * width,
        ),
    )(packed, keys, values)
    return jnp.concatenate([summed, totals, tops], axis=1)


def fold(mine, other, bit):
    upper = (lax.axis_index("seq") & bit) != 0
    low = jnp.where(upper, other, mine)
    high = jnp.where(upper, mine, other)
    return jnp.stack([low, high], axis=1).reshape((-1,) + mine.shape[1:])


def gather_with_audio(packed, keys, values):
    count = lax.axis_size("seq")
    rows = packed.shape[0]
    held = packed[None]
    pending = held
    state = None
    before = None
    bit = count // 2
    while bit >= 1:
        held, pending = lax.optimization_barrier((held, pending))
        arrived = exchange(held, bit, count)
        computed = audio_rows(pending.reshape((-1, packed.shape[1])), keys, values)
        arrived, computed = lax.optimization_barrier((arrived, computed))
        computed = computed.reshape((-1, rows, computed.shape[1]))
        state = computed if state is None else fold(state, computed, before)
        held = fold(held, arrived, bit)
        pending = arrived
        before = bit
        bit //= 2
    computed = audio_rows(pending.reshape((-1, packed.shape[1])), keys, values)
    state = fold(state, computed.reshape((-1, rows, computed.shape[1])), before)
    return (
        held.reshape((count * rows, packed.shape[1])),
        state.reshape((count * rows, state.shape[2])),
    )


def local(video_q, video_k, video_v, audio_q, audio_k, audio_v):
    width = video_q.shape[1]
    heads = width // HEAD_DIM
    groups = 4
    gathered, state = gather_with_audio(
        jnp.concatenate([audio_q, audio_k, audio_v], axis=1), video_k, video_v
    )
    video_calls = [
        lambda earlier, g=g: video_part(video_q, gathered, earlier, g, groups)
        for g in range(groups)
    ]
    mine, video_out = scatter_rows(state, heads, video_calls)
    audio_out = (mine[:, :width] / spread(mine[:, width : width + heads])).astype(jnp.bfloat16)
    return video_out, audio_out


def solution(mesh):
    placed = P(("groups", "seq"), None)
    return jax.shard_map(
        local,
        mesh=mesh,
        in_specs=(placed,) * 6,
        out_specs=(placed, placed),
        check_vma=False,
    )
```

```python
import jax
import jax.numpy as jnp
from jax import lax
from jax.experimental import pallas as pl
from jax.experimental.pallas import tpu as pltpu
from jax.sharding import PartitionSpec as P

HEAD_DIM = 64


def spread(scales):
    return jnp.repeat(scales, HEAD_DIM, axis=1)


def exchange(value, bit, count):
    pairs = [(source, source ^ bit) for source in range(count)]
    return lax.ppermute(value, "seq", pairs)


def gather_rows(block, during=()):
    count = lax.axis_size("seq")
    me = lax.axis_index("seq")
    held = block[None]
    results = []
    bit = count // 2
    step = 0
    while bit >= 1:
        work = during[step] if step < len(during) else None
        if work is not None:
            held, ready = lax.optimization_barrier((held, work[1]))
        arrived = exchange(held, bit, count)
        if work is not None:
            done = work[0](ready)
            arrived, done = lax.optimization_barrier((arrived, done))
            results.append(done)
        upper = (me & bit) != 0
        low = jnp.where(upper, arrived, held)
        high = jnp.where(upper, held, arrived)
        held = jnp.stack([low, high], axis=1).reshape((-1,) + block.shape)
        bit //= 2
        step += 1
    return held.reshape((count * block.shape[0],) + block.shape[1:]), results


def gather_levels(block):
    count = lax.axis_size("seq")
    me = lax.axis_index("seq")
    held = block[None]
    levels = []
    bit = count // 2
    if bit >= 2:
        levels.append((bit, bit // 2))
        bit //= 4
    while bit >= 1:
        levels.append((bit,))
        bit //= 2
    for level in levels:
        mask = sum(level)
        offsets = [0]
        for b in level:
            offsets = offsets + [o + b for o in offsets]
        pieces = {0: held}
        for offset in offsets[1:]:
            pairs = [(source, source ^ offset) for source in range(count)]
            pieces[offset] = lax.ppermute(held, "seq", pairs)
        mine = me & mask
        ordered = []
        for target in sorted(offsets):
            choice = pieces[0]
            for offset in offsets[1:]:
                choice = jnp.where((mine ^ offset) == target, pieces[offset], choice)
            ordered.append(choice)
        held = jnp.stack(ordered, axis=1).reshape((-1,) + block.shape)
    return held.reshape((count * block.shape[0],) + block.shape[1:])


def merge(first, second, heads):
    width = heads * HEAD_DIM
    top = jnp.maximum(first[:, width + heads :], second[:, width + heads :])
    first_scale = jnp.exp(first[:, width + heads :] - top)
    second_scale = jnp.exp(second[:, width + heads :] - top)
    totals = first[:, width : width + heads] * first_scale + second[:, width : width + heads] * second_scale
    summed = first[:, :width] * spread(first_scale) + second[:, :width] * spread(second_scale)
    return jnp.concatenate([summed, totals, top], axis=1)


def pieces(value, count):
    terms = []
    rest = value
    for ignored in range(count):
        rounded = lax.reduce_precision(rest, exponent_bits=8, mantissa_bits=7)
        terms.append(rounded.astype(jnp.bfloat16))
        rest = rest - rounded
    return terms


def encode(state, heads):
    width = heads * HEAD_DIM
    summed = state[..., :width].astype(jnp.bfloat16)
    totals = pieces(state[..., width : width + heads], 2)
    tops = pieces(state[..., width + heads :], 3)
    return jnp.concatenate([summed] + totals + tops, axis=-1)


def decode(sent, heads):
    width = heads * HEAD_DIM
    summed = sent[..., :width].astype(jnp.float32)
    parts = [
        sent[..., width + i * heads : width + (i + 1) * heads].astype(jnp.float32) for i in range(5)
    ]
    totals = parts[0] + parts[1]
    tops = (parts[2] + parts[3]) + parts[4]
    return jnp.concatenate([summed, totals, tops], axis=-1)


def scatter_rows(state, heads, during=()):
    count = lax.axis_size("seq")
    me = lax.axis_index("seq")
    rows = state.shape[0] // count
    held = state.reshape((count, rows, state.shape[1]))
    carried = None
    bit = 1
    step = 0
    while bit < count:
        pairs = held.reshape((-1, 2, rows, state.shape[1]))
        upper = (me & bit) != 0
        keep = jnp.where(upper, pairs[:, 1], pairs[:, 0])
        give = jnp.where(upper, pairs[:, 0], pairs[:, 1])
        work = during[step] if step < len(during) else None
        if work is not None:
            give, carried = lax.optimization_barrier((give, carried))
        arrived = decode(exchange(encode(give, heads), bit, count), heads)
        if work is not None:
            carried = work(carried)
            arrived, carried = lax.optimization_barrier((arrived, carried))
        held = merge(
            keep.reshape((-1, state.shape[1])), arrived.reshape((-1, state.shape[1])), heads
        ).reshape((-1, rows, state.shape[1]))
        bit *= 2
        step += 1
    for work in during[step:]:
        carried = work(carried)
    return held.reshape((rows, state.shape[1])), carried


def head_masks(rows):
    lane = lax.broadcasted_iota(jnp.int32, (rows, 2 * HEAD_DIM), 1)
    return lane < HEAD_DIM


def split_pair(block):
    first = head_masks(block.shape[0])
    zeros = jnp.zeros_like(block)
    return jnp.concatenate([jnp.where(first, block, zeros), jnp.where(first, zeros, block)], axis=0)


def pair_attention(queries, keys, values):
    key_rows = keys.shape[0]
    scores = (
        lax.dot_general(
            queries, split_pair(keys), (((1,), (1,)), ((), ())), preferred_element_type=jnp.float32
        )
        * 0.125
    )
    weights = []
    tops = []
    counts = []
    for half in range(2):
        part = scores[:, half * key_rows : (half + 1) * key_rows]
        highest = jnp.max(part, axis=1, keepdims=True)
        exps = jnp.exp(part - highest)
        tops.append(highest)
        counts.append(jnp.sum(exps, axis=1, keepdims=True))
        weights.append(exps.astype(jnp.bfloat16))
    summed = jnp.dot(
        jnp.concatenate(weights, axis=1), split_pair(values), preferred_element_type=jnp.float32
    )
    return summed, tops, counts


PER_STEP = 2


def video_kernel(query_ref, key_ref, value_ref, *refs):
    out_ref = refs[-1]
    key_rows = key_ref.shape[0]
    for sub in range(PER_STEP):
        lanes = slice(sub * 2 * HEAD_DIM, (sub + 1) * 2 * HEAD_DIM)
        queries = query_ref[:, lanes]
        scores = (
            lax.dot_general(
                split_pair(key_ref[:, lanes]), queries, (((1,), (1,)), ((), ())),
                preferred_element_type=jnp.float32,
            )
            * 0.125
        )
        weights = []
        counts = []
        for half in range(2):
            part = scores[half * key_rows : (half + 1) * key_rows]
            highest = jnp.max(part, axis=0, keepdims=True)
            exps = jnp.exp(part - highest)
            counts.append(jnp.sum(exps, axis=0, keepdims=True))
            weights.append(exps.astype(jnp.bfloat16))
        summed = lax.dot_general(
            split_pair(value_ref[:, lanes]), jnp.concatenate(weights, axis=0),
            (((0,), (0,)), ((), ())), preferred_element_type=jnp.float32,
        )
        lane = lax.broadcasted_iota(jnp.int32, summed.shape, 0)
        totals = jnp.where(lane < HEAD_DIM, counts[0], counts[1])
        out_ref[:, lanes] = (summed / totals).T.astype(out_ref.dtype)


def video_part(queries, keys, values, earlier, group, groups):
    rows, width = queries.shape
    pairs = width // (2 * HEAD_DIM) // groups
    first_pair = group * pairs // PER_STEP
    key_rows = keys.shape[0]
    lanes = 2 * HEAD_DIM * PER_STEP
    specs = [
        pl.BlockSpec((rows, lanes), lambda p: (0, p + first_pair)),
        pl.BlockSpec((key_rows, lanes), lambda p: (0, p + first_pair)),
        pl.BlockSpec((key_rows, lanes), lambda p: (0, p + first_pair)),
    ]
    operands = [queries, keys, values]
    aliases = {}
    if earlier is not None:
        specs.append(pl.BlockSpec(memory_space=pl.ANY))
        operands.append(earlier)
        aliases = {3: 0}
    return pl.pallas_call(
        video_kernel,
        grid=(pairs // PER_STEP,),
        in_specs=specs,
        out_specs=pl.BlockSpec((rows, lanes), lambda p: (0, p + first_pair)),
        out_shape=jax.ShapeDtypeStruct((rows, width), jnp.bfloat16),
        input_output_aliases=aliases,
        cost_estimate=pl.CostEstimate(
            flops=8 * rows * key_rows * width // groups,
            transcendentals=rows * key_rows * width // HEAD_DIM // groups,
            bytes_accessed=2 * (2 * rows * width + 2 * key_rows * width) // groups,
        ),
    )(*operands)


def audio_kernel(query_ref, key_ref, value_ref, sum_ref, total_ref, top_ref):
    step = pl.program_id(0)

    @pl.when(step == 0)
    def _():
        total_ref[...] = jnp.zeros_like(total_ref)
        top_ref[...] = jnp.zeros_like(top_ref)

    column = lax.broadcasted_iota(jnp.int32, total_ref.shape, 1)
    totals_now = total_ref[...]
    tops_now = top_ref[...]
    for sub in range(PER_STEP):
        lanes = slice(sub * 2 * HEAD_DIM, (sub + 1) * 2 * HEAD_DIM)
        summed, tops, counts = pair_attention(
            query_ref[:, lanes], key_ref[:, lanes], value_ref[:, lanes]
        )
        for half in range(2):
            here = column == 2 * (step * PER_STEP + sub) + half
            totals_now = jnp.where(here, counts[half], totals_now)
            tops_now = jnp.where(here, tops[half], tops_now)
        sum_ref[:, lanes] = summed
    total_ref[...] = totals_now
    top_ref[...] = tops_now


def audio_partial(queries, keys, values, group, groups):
    rows, width = queries.shape
    heads = width // HEAD_DIM // groups
    first_pair = group * heads // 2 // PER_STEP
    lanes = 2 * HEAD_DIM * PER_STEP
    key_rows = keys.shape[0]
    return pl.pallas_call(
        audio_kernel,
        grid=(heads // 2 // PER_STEP,),
        in_specs=[
            pl.BlockSpec((rows, lanes), lambda p: (0, p + first_pair)),
            pl.BlockSpec((key_rows, lanes), lambda p: (0, p + first_pair)),
            pl.BlockSpec((key_rows, lanes), lambda p: (0, p + first_pair)),
        ],
        out_specs=[
            pl.BlockSpec((rows, lanes), lambda p: (0, p)),
            pl.BlockSpec((rows, heads), lambda p: (0, 0)),
            pl.BlockSpec((rows, heads), lambda p: (0, 0)),
        ],
        out_shape=[
            jax.ShapeDtypeStruct((rows, heads * HEAD_DIM), jnp.float32),
            jax.ShapeDtypeStruct((rows, heads), jnp.float32),
            jax.ShapeDtypeStruct((rows, heads), jnp.float32),
        ],
        compiler_params=pltpu.CompilerParams(dimension_semantics=("arbitrary",)),
        cost_estimate=pl.CostEstimate(
            flops=8 * rows * key_rows * width // groups,
            transcendentals=rows * key_rows * heads,
            bytes_accessed=(2 * rows * width + 4 * key_rows * width + 4 * rows * width) // groups,
        ),
    )(queries, keys, values)


def local(video_q, video_k, video_v, audio_q, audio_k, audio_v):
    width = video_q.shape[1]
    heads = width // HEAD_DIM
    groups = 4
    all_queries = gather_levels(audio_q)
    audio_calls = [
        (lambda q, g=g: audio_partial(q, video_k, video_v, g, groups), all_queries)
        for g in range(groups)
    ]
    gathered, parts = gather_rows(jnp.concatenate([audio_k, audio_v], axis=1), audio_calls)
    parts = parts + [call[0](all_queries) for call in audio_calls[len(parts) :]]
    all_keys = gathered[:, :width]
    all_values = gathered[:, width:]
    state = jnp.concatenate(
        [part[0] for part in parts] + [part[1] for part in parts] + [part[2] for part in parts],
        axis=1,
    )
    video_calls = [
        lambda earlier, g=g: video_part(video_q, all_keys, all_values, earlier, g, groups)
        for g in range(groups)
    ]
    mine, video_out = scatter_rows(state, heads, video_calls)
    audio_out = (mine[:, :width] / spread(mine[:, width : width + heads])).astype(jnp.bfloat16)
    return video_out, audio_out


def solution(mesh):
    placed = P(("groups", "seq"), None)
    return jax.shard_map(
        local,
        mesh=mesh,
        in_specs=(placed,) * 6,
        out_specs=(placed, placed),
        check_vma=False,
    )
```

```python
import jax
import jax.numpy as jnp
from jax import lax
from jax.experimental import pallas as pl
from jax.experimental.pallas import tpu as pltpu
from jax.sharding import PartitionSpec as P

HEAD_DIM = 64


def spread(scales):
    return jnp.repeat(scales, HEAD_DIM, axis=1)


def exchange(value, bit, count):
    pairs = [(source, source ^ bit) for source in range(count)]
    return lax.ppermute(value, "seq", pairs)


def gather_rows(block, during=()):
    count = lax.axis_size("seq")
    me = lax.axis_index("seq")
    held = block[None]
    results = []
    bit = count // 2
    step = 0
    while bit >= 1:
        work = during[step] if step < len(during) else None
        if work is not None:
            held, ready = lax.optimization_barrier((held, work[1]))
        arrived = exchange(held, bit, count)
        if work is not None:
            done = work[0](ready)
            arrived, done = lax.optimization_barrier((arrived, done))
            results.append(done)
        upper = (me & bit) != 0
        low = jnp.where(upper, arrived, held)
        high = jnp.where(upper, held, arrived)
        held = jnp.stack([low, high], axis=1).reshape((-1,) + block.shape)
        bit //= 2
        step += 1
    return held.reshape((count * block.shape[0],) + block.shape[1:]), results


def gather_levels(block):
    count = lax.axis_size("seq")
    me = lax.axis_index("seq")
    held = block[None]
    levels = []
    bit = count // 2
    if bit >= 2:
        levels.append((bit, bit // 2))
        bit //= 4
    while bit >= 1:
        levels.append((bit,))
        bit //= 2
    for level in levels:
        mask = sum(level)
        offsets = [0]
        for b in level:
            offsets = offsets + [o + b for o in offsets]
        pieces = {0: held}
        for offset in offsets[1:]:
            pairs = [(source, source ^ offset) for source in range(count)]
            pieces[offset] = lax.ppermute(held, "seq", pairs)
        mine = me & mask
        ordered = []
        for target in sorted(offsets):
            choice = pieces[0]
            for offset in offsets[1:]:
                choice = jnp.where((mine ^ offset) == target, pieces[offset], choice)
            ordered.append(choice)
        held = jnp.stack(ordered, axis=1).reshape((-1,) + block.shape)
    return held.reshape((count * block.shape[0],) + block.shape[1:])


def merge(first, second, heads):
    width = heads * HEAD_DIM
    top = jnp.maximum(first[:, width + heads :], second[:, width + heads :])
    first_scale = jnp.exp(first[:, width + heads :] - top)
    second_scale = jnp.exp(second[:, width + heads :] - top)
    totals = first[:, width : width + heads] * first_scale + second[:, width : width + heads] * second_scale
    summed = first[:, :width] * spread(first_scale) + second[:, :width] * spread(second_scale)
    return jnp.concatenate([summed, totals, top], axis=1)


def pieces(value, count):
    terms = []
    rest = value
    for ignored in range(count):
        rounded = lax.reduce_precision(rest, exponent_bits=8, mantissa_bits=7)
        terms.append(rounded.astype(jnp.bfloat16))
        rest = rest - rounded
    return terms


def encode(state, heads):
    width = heads * HEAD_DIM
    summed = state[..., :width].astype(jnp.bfloat16)
    totals = pieces(state[..., width : width + heads], 2)
    tops = pieces(state[..., width + heads :], 3)
    return jnp.concatenate([summed] + totals + tops, axis=-1)


def decode(sent, heads):
    width = heads * HEAD_DIM
    summed = sent[..., :width].astype(jnp.float32)
    parts = [
        sent[..., width + i * heads : width + (i + 1) * heads].astype(jnp.float32) for i in range(5)
    ]
    totals = parts[0] + parts[1]
    tops = (parts[2] + parts[3]) + parts[4]
    return jnp.concatenate([summed, totals, tops], axis=-1)


def scatter_rows(state, heads, during=()):
    count = lax.axis_size("seq")
    me = lax.axis_index("seq")
    rows = state.shape[0] // count
    held = state.reshape((count, rows, state.shape[1]))
    carried = None
    bit = 1
    step = 0
    while bit < count:
        pairs = held.reshape((-1, 2, rows, state.shape[1]))
        upper = (me & bit) != 0
        keep = jnp.where(upper, pairs[:, 1], pairs[:, 0])
        give = jnp.where(upper, pairs[:, 0], pairs[:, 1])
        work = during[step] if step < len(during) else None
        if work is not None:
            give, carried = lax.optimization_barrier((give, carried))
        arrived = decode(exchange(encode(give, heads), bit, count), heads)
        if work is not None:
            carried = work(carried)
            arrived, carried = lax.optimization_barrier((arrived, carried))
        held = merge(
            keep.reshape((-1, state.shape[1])), arrived.reshape((-1, state.shape[1])), heads
        ).reshape((-1, rows, state.shape[1]))
        bit *= 2
        step += 1
    for work in during[step:]:
        carried = work(carried)
    return held.reshape((rows, state.shape[1])), carried


def head_masks(rows):
    lane = lax.broadcasted_iota(jnp.int32, (rows, 2 * HEAD_DIM), 1)
    return lane < HEAD_DIM


def split_pair(block):
    first = head_masks(block.shape[0])
    zeros = jnp.zeros_like(block)
    return jnp.concatenate([jnp.where(first, block, zeros), jnp.where(first, zeros, block)], axis=0)


def pair_attention(queries, keys, values):
    key_rows = keys.shape[0]
    scores = (
        lax.dot_general(
            queries, split_pair(keys), (((1,), (1,)), ((), ())), preferred_element_type=jnp.float32
        )
        * 0.125
    )
    weights = []
    tops = []
    counts = []
    for half in range(2):
        part = scores[:, half * key_rows : (half + 1) * key_rows]
        highest = jnp.max(part, axis=1, keepdims=True)
        exps = jnp.exp(part - highest)
        tops.append(highest)
        counts.append(jnp.sum(exps, axis=1, keepdims=True))
        weights.append(exps.astype(jnp.bfloat16))
    summed = jnp.dot(
        jnp.concatenate(weights, axis=1), split_pair(values), preferred_element_type=jnp.float32
    )
    return summed, tops, counts


PER_STEP = 2


def video_kernel(query_ref, key_ref, value_ref, *refs):
    out_ref = refs[-1]
    key_rows = key_ref.shape[0]
    for sub in range(PER_STEP):
        lanes = slice(sub * 2 * HEAD_DIM, (sub + 1) * 2 * HEAD_DIM)
        queries = query_ref[:, lanes]
        scores = (
            lax.dot_general(
                split_pair(key_ref[:, lanes]), queries, (((1,), (1,)), ((), ())),
                preferred_element_type=jnp.float32,
            )
            * 0.125
        )
        weights = []
        counts = []
        for half in range(2):
            part = scores[half * key_rows : (half + 1) * key_rows]
            highest = jnp.max(part, axis=0, keepdims=True)
            exps = jnp.exp(part - highest)
            counts.append(jnp.sum(exps, axis=0, keepdims=True))
            weights.append(exps.astype(jnp.bfloat16))
        summed = lax.dot_general(
            split_pair(value_ref[:, lanes]), jnp.concatenate(weights, axis=0),
            (((0,), (0,)), ((), ())), preferred_element_type=jnp.float32,
        )
        lane = lax.broadcasted_iota(jnp.int32, summed.shape, 0)
        totals = jnp.where(lane < HEAD_DIM, counts[0], counts[1])
        out_ref[:, lanes] = (summed / totals).T.astype(out_ref.dtype)


def video_part(queries, keys, values, earlier, group, groups):
    rows, width = queries.shape
    pairs = width // (2 * HEAD_DIM) // groups
    first_pair = group * pairs // PER_STEP
    key_rows = keys.shape[0]
    lanes = 2 * HEAD_DIM * PER_STEP
    specs = [
        pl.BlockSpec((rows, lanes), lambda p: (0, p + first_pair)),
        pl.BlockSpec((key_rows, lanes), lambda p: (0, p + first_pair)),
        pl.BlockSpec((key_rows, lanes), lambda p: (0, p + first_pair)),
    ]
    operands = [queries, keys, values]
    aliases = {}
    if earlier is not None:
        specs.append(pl.BlockSpec(memory_space=pl.ANY))
        operands.append(earlier)
        aliases = {3: 0}
    return pl.pallas_call(
        video_kernel,
        grid=(pairs // PER_STEP,),
        in_specs=specs,
        out_specs=pl.BlockSpec((rows, lanes), lambda p: (0, p + first_pair)),
        out_shape=jax.ShapeDtypeStruct((rows, width), jnp.bfloat16),
        input_output_aliases=aliases,
        cost_estimate=pl.CostEstimate(
            flops=8 * rows * key_rows * width // groups,
            transcendentals=rows * key_rows * width // HEAD_DIM // groups,
            bytes_accessed=2 * (2 * rows * width + 2 * key_rows * width) // groups,
        ),
    )(*operands)


def audio_kernel(query_ref, key_ref, value_ref, sum_ref, total_ref, top_ref):
    step = pl.program_id(0)

    @pl.when(step == 0)
    def _():
        total_ref[...] = jnp.zeros_like(total_ref)
        top_ref[...] = jnp.zeros_like(top_ref)

    column = lax.broadcasted_iota(jnp.int32, total_ref.shape, 1)
    totals_now = total_ref[...]
    tops_now = top_ref[...]
    for sub in range(PER_STEP):
        lanes = slice(sub * 2 * HEAD_DIM, (sub + 1) * 2 * HEAD_DIM)
        summed, tops, counts = pair_attention(
            query_ref[:, lanes], key_ref[:, lanes], value_ref[:, lanes]
        )
        for half in range(2):
            here = column == 2 * (step * PER_STEP + sub) + half
            totals_now = jnp.where(here, counts[half], totals_now)
            tops_now = jnp.where(here, tops[half], tops_now)
        sum_ref[:, lanes] = summed
    total_ref[...] = totals_now
    top_ref[...] = tops_now


def audio_partial(queries, keys, values, group, groups):
    rows, width = queries.shape
    heads = width // HEAD_DIM // groups
    first_pair = group * heads // 2 // PER_STEP
    lanes = 2 * HEAD_DIM * PER_STEP
    key_rows = keys.shape[0]
    return pl.pallas_call(
        audio_kernel,
        grid=(heads // 2 // PER_STEP,),
        in_specs=[
            pl.BlockSpec((rows, lanes), lambda p: (0, p + first_pair)),
            pl.BlockSpec((key_rows, lanes), lambda p: (0, p + first_pair)),
            pl.BlockSpec((key_rows, lanes), lambda p: (0, p + first_pair)),
        ],
        out_specs=[
            pl.BlockSpec((rows, lanes), lambda p: (0, p)),
            pl.BlockSpec((rows, heads), lambda p: (0, 0)),
            pl.BlockSpec((rows, heads), lambda p: (0, 0)),
        ],
        out_shape=[
            jax.ShapeDtypeStruct((rows, heads * HEAD_DIM), jnp.float32),
            jax.ShapeDtypeStruct((rows, heads), jnp.float32),
            jax.ShapeDtypeStruct((rows, heads), jnp.float32),
        ],
        compiler_params=pltpu.CompilerParams(dimension_semantics=("arbitrary",)),
        cost_estimate=pl.CostEstimate(
            flops=8 * rows * key_rows * width // groups,
            transcendentals=rows * key_rows * heads,
            bytes_accessed=(2 * rows * width + 4 * key_rows * width + 4 * rows * width) // groups,
        ),
    )(queries, keys, values)


def local(video_q, video_k, video_v, audio_q, audio_k, audio_v):
    width = video_q.shape[1]
    heads = width // HEAD_DIM
    groups = 4
    steps = (lax.axis_size("seq") - 1).bit_length()
    all_queries = gather_levels(audio_q)
    audio_calls = [
        (
            lambda q, gs=gs: tuple(audio_partial(q, video_k, video_v, g, groups) for g in gs),
            all_queries,
        )
        for gs in ((0, 1), (2, 3))
    ]
    gathered, results = gather_rows(
        jnp.concatenate([audio_k, audio_v], axis=1), [None] * (steps - 2) + audio_calls
    )
    parts = [part for result in results for part in result]
    all_keys = gathered[:, :width]
    all_values = gathered[:, width:]
    state = jnp.concatenate(
        [part[0] for part in parts] + [part[1] for part in parts] + [part[2] for part in parts],
        axis=1,
    )
    video_calls = [
        lambda earlier, g=g: video_part(video_q, all_keys, all_values, earlier, g, groups)
        for g in range(groups)
    ]
    mine, video_out = scatter_rows(state, heads, video_calls)
    audio_out = (mine[:, :width] / spread(mine[:, width : width + heads])).astype(jnp.bfloat16)
    return video_out, audio_out


def solution(mesh):
    placed = P(("groups", "seq"), None)
    return jax.shard_map(
        local,
        mesh=mesh,
        in_specs=(placed,) * 6,
        out_specs=(placed, placed),
        check_vma=False,
    )
```

```python
import jax
import jax.numpy as jnp
from jax import lax
from jax.experimental import pallas as pl
from jax.experimental.pallas import tpu as pltpu
from jax.sharding import PartitionSpec as P

HEAD_DIM = 64


def spread(scales):
    heads = scales.shape[1]
    shape = (heads, heads * HEAD_DIM)
    columns = lax.broadcasted_iota(jnp.int32, shape, 1) // HEAD_DIM
    expand = (columns == lax.broadcasted_iota(jnp.int32, shape, 0)).astype(jnp.float32)
    return jnp.dot(
        scales, expand, precision=lax.Precision.HIGHEST, preferred_element_type=jnp.float32
    )


def exchange(value, bit, count):
    pairs = [(source, source ^ bit) for source in range(count)]
    return lax.ppermute(value, "seq", pairs)


def gather_rows(block, during=()):
    count = lax.axis_size("seq")
    me = lax.axis_index("seq")
    held = block[None]
    results = []
    bit = count // 2
    step = 0
    while bit >= 1:
        work = during[step] if step < len(during) else None
        if work is not None:
            held, ready = lax.optimization_barrier((held, work[1]))
        arrived = exchange(held, bit, count)
        if work is not None:
            done = work[0](ready)
            arrived, done = lax.optimization_barrier((arrived, done))
            results.append(done)
        upper = (me & bit) != 0
        low = jnp.where(upper, arrived, held)
        high = jnp.where(upper, held, arrived)
        held = jnp.stack([low, high], axis=1).reshape((-1,) + block.shape)
        bit //= 2
        step += 1
    return held.reshape((count * block.shape[0],) + block.shape[1:]), results


def gather_levels(block):
    count = lax.axis_size("seq")
    me = lax.axis_index("seq")
    held = block[None]
    levels = []
    bit = count // 2
    if bit >= 2:
        levels.append((bit, bit // 2))
        bit //= 4
    while bit >= 1:
        levels.append((bit,))
        bit //= 2
    for level in levels:
        mask = sum(level)
        offsets = [0]
        for b in level:
            offsets = offsets + [o + b for o in offsets]
        pieces = {0: held}
        for offset in offsets[1:]:
            pairs = [(source, source ^ offset) for source in range(count)]
            pieces[offset] = lax.ppermute(held, "seq", pairs)
        mine = me & mask
        ordered = []
        for target in sorted(offsets):
            choice = pieces[0]
            for offset in offsets[1:]:
                choice = jnp.where((mine ^ offset) == target, pieces[offset], choice)
            ordered.append(choice)
        held = jnp.stack(ordered, axis=1).reshape((-1,) + block.shape)
    return held.reshape((count * block.shape[0],) + block.shape[1:])


def merge(first, second, heads):
    width = heads * HEAD_DIM
    top = jnp.maximum(first[:, width + heads :], second[:, width + heads :])
    first_scale = jnp.exp(first[:, width + heads :] - top)
    second_scale = jnp.exp(second[:, width + heads :] - top)
    totals = first[:, width : width + heads] * first_scale + second[:, width : width + heads] * second_scale
    summed = first[:, :width] * spread(first_scale) + second[:, :width] * spread(second_scale)
    return jnp.concatenate([summed, totals, top], axis=1)


def pieces(value, count):
    terms = []
    rest = value
    for ignored in range(count):
        rounded = lax.reduce_precision(rest, exponent_bits=8, mantissa_bits=7)
        terms.append(rounded.astype(jnp.bfloat16))
        rest = rest - rounded
    return terms


def encode(state, heads):
    width = heads * HEAD_DIM
    summed = state[..., :width].astype(jnp.bfloat16)
    totals = pieces(state[..., width : width + heads], 2)
    tops = pieces(state[..., width + heads :], 3)
    return jnp.concatenate([summed] + totals + tops, axis=-1)


def decode(sent, heads):
    width = heads * HEAD_DIM
    summed = sent[..., :width].astype(jnp.float32)
    parts = [
        sent[..., width + i * heads : width + (i + 1) * heads].astype(jnp.float32) for i in range(5)
    ]
    totals = parts[0] + parts[1]
    tops = (parts[2] + parts[3]) + parts[4]
    return jnp.concatenate([summed, totals, tops], axis=-1)


def scatter_rows(state, heads, during=()):
    count = lax.axis_size("seq")
    me = lax.axis_index("seq")
    rows = state.shape[0] // count
    held = state.reshape((count, rows, state.shape[1]))
    carried = None
    bit = 1
    step = 0
    while bit < count:
        pairs = held.reshape((-1, 2, rows, state.shape[1]))
        upper = (me & bit) != 0
        keep = jnp.where(upper, pairs[:, 1], pairs[:, 0])
        give = jnp.where(upper, pairs[:, 0], pairs[:, 1])
        work = during[step] if step < len(during) else None
        if work is not None:
            give, carried = lax.optimization_barrier((give, carried))
        arrived = decode(exchange(encode(give, heads), bit, count), heads)
        if work is not None:
            carried = work(carried)
            arrived, carried = lax.optimization_barrier((arrived, carried))
        held = merge(
            keep.reshape((-1, state.shape[1])), arrived.reshape((-1, state.shape[1])), heads
        ).reshape((-1, rows, state.shape[1]))
        bit *= 2
        step += 1
    for work in during[step:]:
        carried = work(carried)
    return held.reshape((rows, state.shape[1])), carried


def head_masks(rows):
    lane = lax.broadcasted_iota(jnp.int32, (rows, 2 * HEAD_DIM), 1)
    return lane < HEAD_DIM


def split_pair(block):
    first = head_masks(block.shape[0])
    zeros = jnp.zeros_like(block)
    return jnp.concatenate([jnp.where(first, block, zeros), jnp.where(first, zeros, block)], axis=0)


def pair_attention(queries, keys, values):
    key_rows = keys.shape[0]
    scores = (
        lax.dot_general(
            queries, split_pair(keys), (((1,), (1,)), ((), ())), preferred_element_type=jnp.float32
        )
        * 0.125
    )
    weights = []
    tops = []
    counts = []
    for half in range(2):
        part = scores[:, half * key_rows : (half + 1) * key_rows]
        highest = jnp.max(part, axis=1, keepdims=True)
        exps = jnp.exp(part - highest)
        tops.append(highest)
        counts.append(jnp.sum(exps, axis=1, keepdims=True))
        weights.append(exps.astype(jnp.bfloat16))
    summed = jnp.dot(
        jnp.concatenate(weights, axis=1), split_pair(values), preferred_element_type=jnp.float32
    )
    return summed, tops, counts


PER_STEP = 2


def video_kernel(query_ref, key_ref, value_ref, *refs):
    out_ref = refs[-1]
    key_rows = key_ref.shape[0]
    for sub in range(PER_STEP):
        lanes = slice(sub * 2 * HEAD_DIM, (sub + 1) * 2 * HEAD_DIM)
        queries = query_ref[:, lanes]
        scores = (
            lax.dot_general(
                split_pair(key_ref[:, lanes]), queries, (((1,), (1,)), ((), ())),
                preferred_element_type=jnp.float32,
            )
            * 0.125
        )
        weights = []
        counts = []
        for half in range(2):
            part = scores[half * key_rows : (half + 1) * key_rows]
            highest = jnp.max(part, axis=0, keepdims=True)
            exps = jnp.exp(part - highest)
            counts.append(jnp.sum(exps, axis=0, keepdims=True))
            weights.append(exps.astype(jnp.bfloat16))
        summed = lax.dot_general(
            split_pair(value_ref[:, lanes]), jnp.concatenate(weights, axis=0),
            (((0,), (0,)), ((), ())), preferred_element_type=jnp.float32,
        )
        lane = lax.broadcasted_iota(jnp.int32, summed.shape, 0)
        totals = jnp.where(lane < HEAD_DIM, counts[0], counts[1])
        out_ref[:, lanes] = (summed / totals).T.astype(out_ref.dtype)


def video_part(queries, keys, values, earlier, group, groups):
    rows, width = queries.shape
    pairs = width // (2 * HEAD_DIM) // groups
    first_pair = group * pairs // PER_STEP
    key_rows = keys.shape[0]
    lanes = 2 * HEAD_DIM * PER_STEP
    specs = [
        pl.BlockSpec((rows, lanes), lambda p: (0, p + first_pair)),
        pl.BlockSpec((key_rows, lanes), lambda p: (0, p + first_pair)),
        pl.BlockSpec((key_rows, lanes), lambda p: (0, p + first_pair)),
    ]
    operands = [queries, keys, values]
    aliases = {}
    if earlier is not None:
        specs.append(pl.BlockSpec(memory_space=pl.ANY))
        operands.append(earlier)
        aliases = {3: 0}
    return pl.pallas_call(
        video_kernel,
        grid=(pairs // PER_STEP,),
        in_specs=specs,
        out_specs=pl.BlockSpec((rows, lanes), lambda p: (0, p + first_pair)),
        out_shape=jax.ShapeDtypeStruct((rows, width), jnp.bfloat16),
        input_output_aliases=aliases,
        cost_estimate=pl.CostEstimate(
            flops=8 * rows * key_rows * width // groups,
            transcendentals=rows * key_rows * width // HEAD_DIM // groups,
            bytes_accessed=2 * (2 * rows * width + 2 * key_rows * width) // groups,
        ),
    )(*operands)


def audio_kernel(query_ref, key_ref, value_ref, sum_ref, total_ref, top_ref):
    step = pl.program_id(0)

    @pl.when(step == 0)
    def _():
        total_ref[...] = jnp.zeros_like(total_ref)
        top_ref[...] = jnp.zeros_like(top_ref)

    column = lax.broadcasted_iota(jnp.int32, total_ref.shape, 1)
    totals_now = total_ref[...]
    tops_now = top_ref[...]
    for sub in range(PER_STEP):
        lanes = slice(sub * 2 * HEAD_DIM, (sub + 1) * 2 * HEAD_DIM)
        summed, tops, counts = pair_attention(
            query_ref[:, lanes], key_ref[:, lanes], value_ref[:, lanes]
        )
        for half in range(2):
            here = column == 2 * (step * PER_STEP + sub) + half
            totals_now = jnp.where(here, counts[half], totals_now)
            tops_now = jnp.where(here, tops[half], tops_now)
        sum_ref[:, lanes] = summed
    total_ref[...] = totals_now
    top_ref[...] = tops_now


def audio_partial(queries, keys, values, group, groups):
    rows, width = queries.shape
    heads = width // HEAD_DIM // groups
    first_pair = group * heads // 2 // PER_STEP
    lanes = 2 * HEAD_DIM * PER_STEP
    key_rows = keys.shape[0]
    return pl.pallas_call(
        audio_kernel,
        grid=(heads // 2 // PER_STEP,),
        in_specs=[
            pl.BlockSpec((rows, lanes), lambda p: (0, p + first_pair)),
            pl.BlockSpec((key_rows, lanes), lambda p: (0, p + first_pair)),
            pl.BlockSpec((key_rows, lanes), lambda p: (0, p + first_pair)),
        ],
        out_specs=[
            pl.BlockSpec((rows, lanes), lambda p: (0, p)),
            pl.BlockSpec((rows, heads), lambda p: (0, 0)),
            pl.BlockSpec((rows, heads), lambda p: (0, 0)),
        ],
        out_shape=[
            jax.ShapeDtypeStruct((rows, heads * HEAD_DIM), jnp.float32),
            jax.ShapeDtypeStruct((rows, heads), jnp.float32),
            jax.ShapeDtypeStruct((rows, heads), jnp.float32),
        ],
        compiler_params=pltpu.CompilerParams(dimension_semantics=("arbitrary",)),
        cost_estimate=pl.CostEstimate(
            flops=8 * rows * key_rows * width // groups,
            transcendentals=rows * key_rows * heads,
            bytes_accessed=(2 * rows * width + 4 * key_rows * width + 4 * rows * width) // groups,
        ),
    )(queries, keys, values)


def local(video_q, video_k, video_v, audio_q, audio_k, audio_v):
    width = video_q.shape[1]
    heads = width // HEAD_DIM
    groups = 4
    steps = (lax.axis_size("seq") - 1).bit_length()
    all_queries = gather_levels(audio_q)
    audio_calls = [
        (
            lambda q, gs=gs: tuple(audio_partial(q, video_k, video_v, g, groups) for g in gs),
            all_queries,
        )
        for gs in ((0, 1), (2, 3))
    ]
    gathered, results = gather_rows(
        jnp.concatenate([audio_k, audio_v], axis=1), [None] * (steps - 2) + audio_calls
    )
    parts = [part for result in results for part in result]
    all_keys = gathered[:, :width]
    all_values = gathered[:, width:]
    state = jnp.concatenate(
        [part[0] for part in parts] + [part[1] for part in parts] + [part[2] for part in parts],
        axis=1,
    )
    video_calls = [
        lambda earlier, g=g: video_part(video_q, all_keys, all_values, earlier, g, groups)
        for g in range(groups)
    ]
    mine, video_out = scatter_rows(state, heads, video_calls)
    audio_out = (mine[:, :width] / spread(mine[:, width : width + heads])).astype(jnp.bfloat16)
    return video_out, audio_out


def solution(mesh):
    placed = P(("groups", "seq"), None)
    return jax.shard_map(
        local,
        mesh=mesh,
        in_specs=(placed,) * 6,
        out_specs=(placed, placed),
        check_vma=False,
    )
```

```python
import jax
import jax.numpy as jnp
from jax import lax
from jax.experimental import pallas as pl
from jax.experimental.pallas import tpu as pltpu
from jax.sharding import PartitionSpec as P

HEAD_DIM = 64


def spread(scales):
    heads = scales.shape[1]
    shape = (heads, heads * HEAD_DIM)
    columns = lax.broadcasted_iota(jnp.int32, shape, 1) // HEAD_DIM
    expand = (columns == lax.broadcasted_iota(jnp.int32, shape, 0)).astype(jnp.float32)
    return jnp.dot(
        scales, expand, precision=lax.Precision.HIGHEST, preferred_element_type=jnp.float32
    )


def exchange(value, bit, count):
    pairs = [(source, source ^ bit) for source in range(count)]
    return lax.ppermute(value, "seq", pairs)


def gather_rows(block, during=()):
    count = lax.axis_size("seq")
    me = lax.axis_index("seq")
    held = block[None]
    results = []
    bit = count // 2
    step = 0
    while bit >= 1:
        work = during[step] if step < len(during) else None
        if work is not None:
            held, ready = lax.optimization_barrier((held, work[1]))
        arrived = exchange(held, bit, count)
        if work is not None:
            done = work[0](ready)
            arrived, done = lax.optimization_barrier((arrived, done))
            results.append(done)
        upper = (me & bit) != 0
        low = jnp.where(upper, arrived, held)
        high = jnp.where(upper, held, arrived)
        held = jnp.stack([low, high], axis=1).reshape((-1,) + block.shape)
        bit //= 2
        step += 1
    return held.reshape((count * block.shape[0],) + block.shape[1:]), results


def gather_levels(block):
    count = lax.axis_size("seq")
    me = lax.axis_index("seq")
    held = block[None]
    levels = []
    bit = count // 2
    if bit >= 2:
        levels.append((bit, bit // 2))
        bit //= 4
    while bit >= 1:
        levels.append((bit,))
        bit //= 2
    for level in levels:
        mask = sum(level)
        offsets = [0]
        for b in level:
            offsets = offsets + [o + b for o in offsets]
        pieces = {0: held}
        for offset in offsets[1:]:
            pairs = [(source, source ^ offset) for source in range(count)]
            pieces[offset] = lax.ppermute(held, "seq", pairs)
        mine = me & mask
        ordered = []
        for target in sorted(offsets):
            choice = pieces[0]
            for offset in offsets[1:]:
                choice = jnp.where((mine ^ offset) == target, pieces[offset], choice)
            ordered.append(choice)
        held = jnp.stack(ordered, axis=1).reshape((-1,) + block.shape)
    return held.reshape((count * block.shape[0],) + block.shape[1:])


def merge(first, second, heads):
    width = heads * HEAD_DIM
    top = jnp.maximum(first[:, width + heads :], second[:, width + heads :])
    first_scale = jnp.exp(first[:, width + heads :] - top)
    second_scale = jnp.exp(second[:, width + heads :] - top)
    totals = first[:, width : width + heads] * first_scale + second[:, width : width + heads] * second_scale
    summed = first[:, :width] * spread(first_scale) + second[:, :width] * spread(second_scale)
    return jnp.concatenate([summed, totals, top], axis=1)


def pieces(value, count):
    terms = []
    rest = value
    for ignored in range(count):
        rounded = lax.reduce_precision(rest, exponent_bits=8, mantissa_bits=7)
        terms.append(rounded.astype(jnp.bfloat16))
        rest = rest - rounded
    return terms


def encode(state, heads):
    width = heads * HEAD_DIM
    summed = state[..., :width].astype(jnp.bfloat16)
    totals = pieces(state[..., width : width + heads], 2)
    tops = pieces(state[..., width + heads :], 3)
    return jnp.concatenate([summed] + totals + tops, axis=-1)


def decode(sent, heads):
    width = heads * HEAD_DIM
    summed = sent[..., :width].astype(jnp.float32)
    parts = [
        sent[..., width + i * heads : width + (i + 1) * heads].astype(jnp.float32) for i in range(5)
    ]
    totals = parts[0] + parts[1]
    tops = (parts[2] + parts[3]) + parts[4]
    return jnp.concatenate([summed, totals, tops], axis=-1)


def scatter_rows(state, heads, during=()):
    count = lax.axis_size("seq")
    me = lax.axis_index("seq")
    rows = state.shape[0] // count
    held = state.reshape((count, rows, state.shape[1]))
    carried = None
    bit = 1
    step = 0
    while bit < count:
        pairs = held.reshape((-1, 2, rows, state.shape[1]))
        upper = (me & bit) != 0
        keep = jnp.where(upper, pairs[:, 1], pairs[:, 0])
        give = jnp.where(upper, pairs[:, 0], pairs[:, 1])
        work = during[step] if step < len(during) else None
        if work is not None:
            give, carried = lax.optimization_barrier((give, carried))
        arrived = decode(exchange(encode(give, heads), bit, count), heads)
        if work is not None:
            carried = work(carried)
            arrived, carried = lax.optimization_barrier((arrived, carried))
        held = merge(
            keep.reshape((-1, state.shape[1])), arrived.reshape((-1, state.shape[1])), heads
        ).reshape((-1, rows, state.shape[1]))
        bit *= 2
        step += 1
    for work in during[step:]:
        carried = work(carried)
    return held.reshape((rows, state.shape[1])), carried


def head_masks(rows):
    lane = lax.broadcasted_iota(jnp.int32, (rows, 2 * HEAD_DIM), 1)
    return lane < HEAD_DIM


def split_pair(block):
    first = head_masks(block.shape[0])
    zeros = jnp.zeros_like(block)
    return jnp.concatenate([jnp.where(first, block, zeros), jnp.where(first, zeros, block)], axis=0)


def pair_attention(queries, keys, values):
    key_rows = keys.shape[0]
    scores = (
        lax.dot_general(
            queries, split_pair(keys), (((1,), (1,)), ((), ())), preferred_element_type=jnp.float32
        )
        * 0.125
    )
    weights = []
    tops = []
    counts = []
    for half in range(2):
        part = scores[:, half * key_rows : (half + 1) * key_rows]
        highest = jnp.max(part, axis=1, keepdims=True)
        exps = jnp.exp(part - highest)
        tops.append(highest)
        counts.append(jnp.sum(exps, axis=1, keepdims=True))
        weights.append(exps.astype(jnp.bfloat16))
    summed = jnp.dot(
        jnp.concatenate(weights, axis=1), split_pair(values), preferred_element_type=jnp.float32
    )
    return summed, tops, counts


PER_STEP = 4


def video_kernel(query_ref, key_ref, value_ref, *refs):
    out_ref = refs[-1]
    key_rows = key_ref.shape[0]
    for sub in range(PER_STEP):
        lanes = slice(sub * 2 * HEAD_DIM, (sub + 1) * 2 * HEAD_DIM)
        queries = query_ref[:, lanes]
        scores = (
            lax.dot_general(
                split_pair(key_ref[:, lanes]), queries, (((1,), (1,)), ((), ())),
                preferred_element_type=jnp.float32,
            )
            * 0.125
        )
        weights = []
        counts = []
        for half in range(2):
            part = scores[half * key_rows : (half + 1) * key_rows]
            highest = jnp.max(part, axis=0, keepdims=True)
            exps = jnp.exp(part - highest)
            counts.append(jnp.sum(exps, axis=0, keepdims=True))
            weights.append(exps.astype(jnp.bfloat16))
        summed = lax.dot_general(
            split_pair(value_ref[:, lanes]), jnp.concatenate(weights, axis=0),
            (((0,), (0,)), ((), ())), preferred_element_type=jnp.float32,
        )
        lane = lax.broadcasted_iota(jnp.int32, summed.shape, 0)
        totals = jnp.where(lane < HEAD_DIM, counts[0], counts[1])
        out_ref[:, lanes] = (summed / totals).T.astype(out_ref.dtype)


def video_part(queries, keys, values, earlier, group, groups):
    rows, width = queries.shape
    pairs = width // (2 * HEAD_DIM) // groups
    first_pair = group * pairs // PER_STEP
    key_rows = keys.shape[0]
    lanes = 2 * HEAD_DIM * PER_STEP
    specs = [
        pl.BlockSpec((rows, lanes), lambda p: (0, p + first_pair)),
        pl.BlockSpec((key_rows, lanes), lambda p: (0, p + first_pair)),
        pl.BlockSpec((key_rows, lanes), lambda p: (0, p + first_pair)),
    ]
    operands = [queries, keys, values]
    aliases = {}
    if earlier is not None:
        specs.append(pl.BlockSpec(memory_space=pl.ANY))
        operands.append(earlier)
        aliases = {3: 0}
    return pl.pallas_call(
        video_kernel,
        grid=(pairs // PER_STEP,),
        in_specs=specs,
        out_specs=pl.BlockSpec((rows, lanes), lambda p: (0, p + first_pair)),
        out_shape=jax.ShapeDtypeStruct((rows, width), jnp.bfloat16),
        input_output_aliases=aliases,
        cost_estimate=pl.CostEstimate(
            flops=8 * rows * key_rows * width // groups,
            transcendentals=rows * key_rows * width // HEAD_DIM // groups,
            bytes_accessed=2 * (2 * rows * width + 2 * key_rows * width) // groups,
        ),
    )(*operands)


def audio_kernel(query_ref, key_ref, value_ref, sum_ref, total_ref, top_ref):
    step = pl.program_id(0)

    @pl.when(step == 0)
    def _():
        total_ref[...] = jnp.zeros_like(total_ref)
        top_ref[...] = jnp.zeros_like(top_ref)

    column = lax.broadcasted_iota(jnp.int32, total_ref.shape, 1)
    totals_now = total_ref[...]
    tops_now = top_ref[...]
    for sub in range(PER_STEP):
        lanes = slice(sub * 2 * HEAD_DIM, (sub + 1) * 2 * HEAD_DIM)
        summed, tops, counts = pair_attention(
            query_ref[:, lanes], key_ref[:, lanes], value_ref[:, lanes]
        )
        for half in range(2):
            here = column == 2 * (step * PER_STEP + sub) + half
            totals_now = jnp.where(here, counts[half], totals_now)
            tops_now = jnp.where(here, tops[half], tops_now)
        sum_ref[:, lanes] = summed
    total_ref[...] = totals_now
    top_ref[...] = tops_now


def audio_partial(queries, keys, values, group, groups):
    rows, width = queries.shape
    heads = width // HEAD_DIM // groups
    first_pair = group * heads // 2 // PER_STEP
    lanes = 2 * HEAD_DIM * PER_STEP
    key_rows = keys.shape[0]
    return pl.pallas_call(
        audio_kernel,
        grid=(heads // 2 // PER_STEP,),
        in_specs=[
            pl.BlockSpec((rows, lanes), lambda p: (0, p + first_pair)),
            pl.BlockSpec((key_rows, lanes), lambda p: (0, p + first_pair)),
            pl.BlockSpec((key_rows, lanes), lambda p: (0, p + first_pair)),
        ],
        out_specs=[
            pl.BlockSpec((rows, lanes), lambda p: (0, p)),
            pl.BlockSpec((rows, heads), lambda p: (0, 0)),
            pl.BlockSpec((rows, heads), lambda p: (0, 0)),
        ],
        out_shape=[
            jax.ShapeDtypeStruct((rows, heads * HEAD_DIM), jnp.float32),
            jax.ShapeDtypeStruct((rows, heads), jnp.float32),
            jax.ShapeDtypeStruct((rows, heads), jnp.float32),
        ],
        compiler_params=pltpu.CompilerParams(dimension_semantics=("arbitrary",)),
        cost_estimate=pl.CostEstimate(
            flops=8 * rows * key_rows * width // groups,
            transcendentals=rows * key_rows * heads,
            bytes_accessed=(2 * rows * width + 4 * key_rows * width + 4 * rows * width) // groups,
        ),
    )(queries, keys, values)


def local(video_q, video_k, video_v, audio_q, audio_k, audio_v):
    width = video_q.shape[1]
    heads = width // HEAD_DIM
    groups = 4
    steps = (lax.axis_size("seq") - 1).bit_length()
    all_queries = gather_levels(audio_q)
    audio_calls = [
        (
            lambda q, gs=gs: tuple(audio_partial(q, video_k, video_v, g, groups) for g in gs),
            all_queries,
        )
        for gs in ((0, 1), (2, 3))
    ]
    gathered, results = gather_rows(
        jnp.concatenate([audio_k, audio_v], axis=1), [None] * (steps - 2) + audio_calls
    )
    parts = [part for result in results for part in result]
    all_keys = gathered[:, :width]
    all_values = gathered[:, width:]
    state = jnp.concatenate(
        [part[0] for part in parts] + [part[1] for part in parts] + [part[2] for part in parts],
        axis=1,
    )
    video_calls = [
        lambda earlier, g=g: video_part(video_q, all_keys, all_values, earlier, g, groups)
        for g in range(groups)
    ]
    mine, video_out = scatter_rows(state, heads, video_calls)
    audio_out = (mine[:, :width] / spread(mine[:, width : width + heads])).astype(jnp.bfloat16)
    return video_out, audio_out


def solution(mesh):
    placed = P(("groups", "seq"), None)
    return jax.shard_map(
        local,
        mesh=mesh,
        in_specs=(placed,) * 6,
        out_specs=(placed, placed),
        check_vma=False,
    )
```

```python
import jax
import jax.numpy as jnp
from jax import lax
from jax.experimental import pallas as pl
from jax.experimental.pallas import tpu as pltpu
from jax.sharding import PartitionSpec as P

HEAD_DIM = 64


def spread(scales):
    heads = scales.shape[1]
    shape = (heads, heads * HEAD_DIM)
    columns = lax.broadcasted_iota(jnp.int32, shape, 1) // HEAD_DIM
    expand = (columns == lax.broadcasted_iota(jnp.int32, shape, 0)).astype(jnp.float32)
    return jnp.dot(
        scales, expand, precision=lax.Precision.HIGHEST, preferred_element_type=jnp.float32
    )


def exchange(value, bit, count):
    pairs = [(source, source ^ bit) for source in range(count)]
    return lax.ppermute(value, "seq", pairs)


def gather_rows(block, during=()):
    count = lax.axis_size("seq")
    me = lax.axis_index("seq")
    held = block[None]
    results = []
    bit = count // 2
    step = 0
    while bit >= 1:
        work = during[step] if step < len(during) else None
        if work is not None:
            held, ready = lax.optimization_barrier((held, work[1]))
        arrived = exchange(held, bit, count)
        if work is not None:
            done = work[0](ready)
            arrived, done = lax.optimization_barrier((arrived, done))
            results.append(done)
        upper = (me & bit) != 0
        low = jnp.where(upper, arrived, held)
        high = jnp.where(upper, held, arrived)
        held = jnp.stack([low, high], axis=1).reshape((-1,) + block.shape)
        bit //= 2
        step += 1
    return held.reshape((count * block.shape[0],) + block.shape[1:]), results


def gather_levels(block):
    count = lax.axis_size("seq")
    me = lax.axis_index("seq")
    held = block[None]
    levels = []
    bit = count // 2
    if bit >= 2:
        levels.append((bit, bit // 2))
        bit //= 4
    while bit >= 1:
        levels.append((bit,))
        bit //= 2
    for level in levels:
        mask = sum(level)
        offsets = [0]
        for b in level:
            offsets = offsets + [o + b for o in offsets]
        pieces = {0: held}
        for offset in offsets[1:]:
            pairs = [(source, source ^ offset) for source in range(count)]
            pieces[offset] = lax.ppermute(held, "seq", pairs)
        mine = me & mask
        ordered = []
        for target in sorted(offsets):
            choice = pieces[0]
            for offset in offsets[1:]:
                choice = jnp.where((mine ^ offset) == target, pieces[offset], choice)
            ordered.append(choice)
        held = jnp.stack(ordered, axis=1).reshape((-1,) + block.shape)
    return held.reshape((count * block.shape[0],) + block.shape[1:])


def merge(first, second, heads):
    width = heads * HEAD_DIM
    top = jnp.maximum(first[:, width + heads :], second[:, width + heads :])
    first_scale = jnp.exp(first[:, width + heads :] - top)
    second_scale = jnp.exp(second[:, width + heads :] - top)
    totals = first[:, width : width + heads] * first_scale + second[:, width : width + heads] * second_scale
    summed = first[:, :width] * spread(first_scale) + second[:, :width] * spread(second_scale)
    return jnp.concatenate([summed, totals, top], axis=1)


def pieces(value, count):
    terms = []
    rest = value
    for ignored in range(count):
        rounded = lax.reduce_precision(rest, exponent_bits=8, mantissa_bits=7)
        terms.append(rounded.astype(jnp.bfloat16))
        rest = rest - rounded
    return terms


def encode(state, heads):
    width = heads * HEAD_DIM
    summed = state[..., :width].astype(jnp.bfloat16)
    totals = pieces(state[..., width : width + heads], 2)
    tops = pieces(state[..., width + heads :], 3)
    return jnp.concatenate([summed] + totals + tops, axis=-1)


def decode(sent, heads):
    width = heads * HEAD_DIM
    summed = sent[..., :width].astype(jnp.float32)
    parts = [
        sent[..., width + i * heads : width + (i + 1) * heads].astype(jnp.float32) for i in range(5)
    ]
    totals = parts[0] + parts[1]
    tops = (parts[2] + parts[3]) + parts[4]
    return jnp.concatenate([summed, totals, tops], axis=-1)


def scatter_rows(state, heads, during=()):
    count = lax.axis_size("seq")
    me = lax.axis_index("seq")
    rows = state.shape[0] // count
    held = state.reshape((count, rows, state.shape[1]))
    carried = None
    bit = 1
    step = 0
    while bit < count:
        pairs = held.reshape((-1, 2, rows, state.shape[1]))
        upper = (me & bit) != 0
        keep = jnp.where(upper, pairs[:, 1], pairs[:, 0])
        give = jnp.where(upper, pairs[:, 0], pairs[:, 1])
        work = during[step] if step < len(during) else None
        if work is not None:
            give, carried = lax.optimization_barrier((give, carried))
        arrived = decode(exchange(encode(give, heads), bit, count), heads)
        if work is not None:
            carried = work(carried)
            arrived, carried = lax.optimization_barrier((arrived, carried))
        held = merge(
            keep.reshape((-1, state.shape[1])), arrived.reshape((-1, state.shape[1])), heads
        ).reshape((-1, rows, state.shape[1]))
        bit *= 2
        step += 1
    for work in during[step:]:
        carried = work(carried)
    return held.reshape((rows, state.shape[1])), carried


def head_masks(rows):
    lane = lax.broadcasted_iota(jnp.int32, (rows, 2 * HEAD_DIM), 1)
    return lane < HEAD_DIM


def split_pair(block):
    first = head_masks(block.shape[0])
    zeros = jnp.zeros_like(block)
    return jnp.concatenate([jnp.where(first, block, zeros), jnp.where(first, zeros, block)], axis=0)


def pair_attention(queries, keys, values):
    key_rows = keys.shape[0]
    scaled = queries * jnp.asarray(0.125, queries.dtype)
    scores = lax.dot_general(
        scaled, split_pair(keys), (((1,), (1,)), ((), ())), preferred_element_type=jnp.float32
    )
    weights = []
    tops = []
    counts = []
    for half in range(2):
        part = scores[:, half * key_rows : (half + 1) * key_rows]
        highest = jnp.max(part, axis=1, keepdims=True)
        exps = jnp.exp(part - highest)
        tops.append(highest)
        counts.append(jnp.sum(exps, axis=1, keepdims=True))
        weights.append(exps.astype(jnp.bfloat16))
    summed = jnp.dot(
        jnp.concatenate(weights, axis=1), split_pair(values), preferred_element_type=jnp.float32
    )
    return summed, tops, counts


PER_STEP = 2


def video_kernel(query_ref, key_ref, value_ref, *refs):
    out_ref = refs[-1]
    key_rows = key_ref.shape[0]
    for sub in range(PER_STEP):
        lanes = slice(sub * 2 * HEAD_DIM, (sub + 1) * 2 * HEAD_DIM)
        queries = query_ref[:, lanes] * jnp.asarray(0.125, query_ref.dtype)
        scores = lax.dot_general(
            split_pair(key_ref[:, lanes]), queries, (((1,), (1,)), ((), ())),
            preferred_element_type=jnp.float32,
        )
        weights = []
        counts = []
        for half in range(2):
            part = scores[half * key_rows : (half + 1) * key_rows]
            highest = jnp.max(part, axis=0, keepdims=True)
            exps = jnp.exp(part - highest)
            counts.append(jnp.sum(exps, axis=0, keepdims=True))
            weights.append(exps.astype(jnp.bfloat16))
        summed = lax.dot_general(
            split_pair(value_ref[:, lanes]), jnp.concatenate(weights, axis=0),
            (((0,), (0,)), ((), ())), preferred_element_type=jnp.float32,
        )
        lane = lax.broadcasted_iota(jnp.int32, summed.shape, 0)
        inverse = jnp.where(lane < HEAD_DIM, 1.0 / counts[0], 1.0 / counts[1])
        out_ref[:, lanes] = (summed * inverse).T.astype(out_ref.dtype)


def video_part(queries, keys, values, earlier, group, groups):
    rows, width = queries.shape
    pairs = width // (2 * HEAD_DIM) // groups
    first_pair = group * pairs // PER_STEP
    key_rows = keys.shape[0]
    lanes = 2 * HEAD_DIM * PER_STEP
    specs = [
        pl.BlockSpec((rows, lanes), lambda p: (0, p + first_pair)),
        pl.BlockSpec((key_rows, lanes), lambda p: (0, p + first_pair)),
        pl.BlockSpec((key_rows, lanes), lambda p: (0, p + first_pair)),
    ]
    operands = [queries, keys, values]
    aliases = {}
    if earlier is not None:
        specs.append(pl.BlockSpec(memory_space=pl.ANY))
        operands.append(earlier)
        aliases = {3: 0}
    return pl.pallas_call(
        video_kernel,
        grid=(pairs // PER_STEP,),
        in_specs=specs,
        out_specs=pl.BlockSpec((rows, lanes), lambda p: (0, p + first_pair)),
        out_shape=jax.ShapeDtypeStruct((rows, width), jnp.bfloat16),
        input_output_aliases=aliases,
        cost_estimate=pl.CostEstimate(
            flops=8 * rows * key_rows * width // groups,
            transcendentals=rows * key_rows * width // HEAD_DIM // groups,
            bytes_accessed=2 * (2 * rows * width + 2 * key_rows * width) // groups,
        ),
    )(*operands)


def audio_kernel(query_ref, key_ref, value_ref, sum_ref, total_ref, top_ref):
    step = pl.program_id(0)

    @pl.when(step == 0)
    def _():
        total_ref[...] = jnp.zeros_like(total_ref)
        top_ref[...] = jnp.zeros_like(top_ref)

    column = lax.broadcasted_iota(jnp.int32, total_ref.shape, 1)
    totals_now = total_ref[...]
    tops_now = top_ref[...]
    for sub in range(PER_STEP):
        lanes = slice(sub * 2 * HEAD_DIM, (sub + 1) * 2 * HEAD_DIM)
        summed, tops, counts = pair_attention(
            query_ref[:, lanes], key_ref[:, lanes], value_ref[:, lanes]
        )
        for half in range(2):
            here = column == 2 * (step * PER_STEP + sub) + half
            totals_now = jnp.where(here, counts[half], totals_now)
            tops_now = jnp.where(here, tops[half], tops_now)
        sum_ref[:, lanes] = summed
    total_ref[...] = totals_now
    top_ref[...] = tops_now


def audio_partial(queries, keys, values, group, groups):
    rows, width = queries.shape
    heads = width // HEAD_DIM // groups
    first_pair = group * heads // 2 // PER_STEP
    lanes = 2 * HEAD_DIM * PER_STEP
    key_rows = keys.shape[0]
    return pl.pallas_call(
        audio_kernel,
        grid=(heads // 2 // PER_STEP,),
        in_specs=[
            pl.BlockSpec((rows, lanes), lambda p: (0, p + first_pair)),
            pl.BlockSpec((key_rows, lanes), lambda p: (0, p + first_pair)),
            pl.BlockSpec((key_rows, lanes), lambda p: (0, p + first_pair)),
        ],
        out_specs=[
            pl.BlockSpec((rows, lanes), lambda p: (0, p)),
            pl.BlockSpec((rows, heads), lambda p: (0, 0)),
            pl.BlockSpec((rows, heads), lambda p: (0, 0)),
        ],
        out_shape=[
            jax.ShapeDtypeStruct((rows, heads * HEAD_DIM), jnp.float32),
            jax.ShapeDtypeStruct((rows, heads), jnp.float32),
            jax.ShapeDtypeStruct((rows, heads), jnp.float32),
        ],
        compiler_params=pltpu.CompilerParams(dimension_semantics=("arbitrary",)),
        cost_estimate=pl.CostEstimate(
            flops=8 * rows * key_rows * width // groups,
            transcendentals=rows * key_rows * heads,
            bytes_accessed=(2 * rows * width + 4 * key_rows * width + 4 * rows * width) // groups,
        ),
    )(queries, keys, values)


def local(video_q, video_k, video_v, audio_q, audio_k, audio_v):
    width = video_q.shape[1]
    heads = width // HEAD_DIM
    groups = 4
    steps = (lax.axis_size("seq") - 1).bit_length()
    all_queries = gather_levels(audio_q)
    audio_calls = [
        (
            lambda q, gs=gs: tuple(audio_partial(q, video_k, video_v, g, groups) for g in gs),
            all_queries,
        )
        for gs in ((0, 1), (2, 3))
    ]
    gathered, results = gather_rows(
        jnp.concatenate([audio_k, audio_v], axis=1), [None] * (steps - 2) + audio_calls
    )
    parts = [part for result in results for part in result]
    all_keys = gathered[:, :width]
    all_values = gathered[:, width:]
    state = jnp.concatenate(
        [part[0] for part in parts] + [part[1] for part in parts] + [part[2] for part in parts],
        axis=1,
    )
    video_calls = [
        lambda earlier, g=g: video_part(video_q, all_keys, all_values, earlier, g, groups)
        for g in range(groups)
    ]
    mine, video_out = scatter_rows(state, heads, video_calls)
    audio_out = (mine[:, :width] / spread(mine[:, width : width + heads])).astype(jnp.bfloat16)
    return video_out, audio_out


def solution(mesh):
    placed = P(("groups", "seq"), None)
    return jax.shard_map(
        local,
        mesh=mesh,
        in_specs=(placed,) * 6,
        out_specs=(placed, placed),
        check_vma=False,
    )
```

```python
import jax
import jax.numpy as jnp
from jax import lax
from jax.experimental import pallas as pl
from jax.experimental.pallas import tpu as pltpu
from jax.sharding import PartitionSpec as P

HEAD_DIM = 64


def spread(scales):
    heads = scales.shape[1]
    shape = (heads, heads * HEAD_DIM)
    columns = lax.broadcasted_iota(jnp.int32, shape, 1) // HEAD_DIM
    expand = (columns == lax.broadcasted_iota(jnp.int32, shape, 0)).astype(jnp.float32)
    return jnp.dot(
        scales, expand, precision=lax.Precision.HIGHEST, preferred_element_type=jnp.float32
    )


def exchange(value, bit, count):
    pairs = [(source, source ^ bit) for source in range(count)]
    return lax.ppermute(value, "seq", pairs)


def gather_rows(block, during=()):
    count = lax.axis_size("seq")
    me = lax.axis_index("seq")
    held = block[None]
    results = []
    bit = count // 2
    step = 0
    while bit >= 1:
        work = during[step] if step < len(during) else None
        if work is not None:
            held, ready = lax.optimization_barrier((held, work[1]))
        arrived = exchange(held, bit, count)
        if work is not None:
            done = work[0](ready)
            arrived, done = lax.optimization_barrier((arrived, done))
            results.append(done)
        upper = (me & bit) != 0
        low = jnp.where(upper, arrived, held)
        high = jnp.where(upper, held, arrived)
        held = jnp.stack([low, high], axis=1).reshape((-1,) + block.shape)
        bit //= 2
        step += 1
    return held.reshape((count * block.shape[0],) + block.shape[1:]), results


def gather_levels(block):
    count = lax.axis_size("seq")
    me = lax.axis_index("seq")
    held = block[None]
    levels = []
    bit = count // 2
    if bit >= 2:
        levels.append((bit, bit // 2))
        bit //= 4
    while bit >= 1:
        levels.append((bit,))
        bit //= 2
    for level in levels:
        mask = sum(level)
        offsets = [0]
        for b in level:
            offsets = offsets + [o + b for o in offsets]
        pieces = {0: held}
        for offset in offsets[1:]:
            pairs = [(source, source ^ offset) for source in range(count)]
            pieces[offset] = lax.ppermute(held, "seq", pairs)
        mine = me & mask
        ordered = []
        for target in sorted(offsets):
            choice = pieces[0]
            for offset in offsets[1:]:
                choice = jnp.where((mine ^ offset) == target, pieces[offset], choice)
            ordered.append(choice)
        held = jnp.stack(ordered, axis=1).reshape((-1,) + block.shape)
    return held.reshape((count * block.shape[0],) + block.shape[1:])


def merge(first, second, heads):
    width = heads * HEAD_DIM
    top = jnp.maximum(first[:, width + heads :], second[:, width + heads :])
    first_scale = jnp.exp(first[:, width + heads :] - top)
    second_scale = jnp.exp(second[:, width + heads :] - top)
    totals = first[:, width : width + heads] * first_scale + second[:, width : width + heads] * second_scale
    summed = first[:, :width] * spread(first_scale) + second[:, :width] * spread(second_scale)
    return jnp.concatenate([summed, totals, top], axis=1)


def pieces(value, count):
    terms = []
    rest = value
    for ignored in range(count):
        rounded = lax.reduce_precision(rest, exponent_bits=8, mantissa_bits=7)
        terms.append(rounded.astype(jnp.bfloat16))
        rest = rest - rounded
    return terms


def encode(state, heads):
    width = heads * HEAD_DIM
    summed = state[..., :width].astype(jnp.bfloat16)
    totals = pieces(state[..., width : width + heads], 2)
    tops = pieces(state[..., width + heads :], 3)
    return jnp.concatenate([summed] + totals + tops, axis=-1)


def decode(sent, heads):
    width = heads * HEAD_DIM
    summed = sent[..., :width].astype(jnp.float32)
    parts = [
        sent[..., width + i * heads : width + (i + 1) * heads].astype(jnp.float32) for i in range(5)
    ]
    totals = parts[0] + parts[1]
    tops = (parts[2] + parts[3]) + parts[4]
    return jnp.concatenate([summed, totals, tops], axis=-1)


def scatter_rows(state, heads, during=()):
    count = lax.axis_size("seq")
    me = lax.axis_index("seq")
    pieces = state
    rows = pieces[0].shape[0] // count
    columns = sum(piece.shape[1] for piece in pieces)
    held = [piece.reshape((count, rows, piece.shape[1])) for piece in pieces]
    carried = None
    bit = 1
    step = 0
    while bit < count:
        upper = (me & bit) != 0
        pairs = [piece.reshape((-1, 2, rows, piece.shape[-1])) for piece in held]
        keep = jnp.concatenate([jnp.where(upper, p[:, 1], p[:, 0]) for p in pairs], axis=-1)
        give = jnp.concatenate([jnp.where(upper, p[:, 0], p[:, 1]) for p in pairs], axis=-1)
        work = during[step] if step < len(during) else None
        if work is not None:
            give, carried = lax.optimization_barrier((give, carried))
        arrived = decode(exchange(encode(give, heads), bit, count), heads)
        if work is not None:
            carried = work(carried)
            arrived, carried = lax.optimization_barrier((arrived, carried))
        held = [
            merge(keep.reshape((-1, columns)), arrived.reshape((-1, columns)), heads).reshape(
                (-1, rows, columns)
            )
        ]
        bit *= 2
        step += 1
    for work in during[step:]:
        carried = work(carried)
    return held[0].reshape((rows, columns)), carried


def head_masks(rows):
    lane = lax.broadcasted_iota(jnp.int32, (rows, 2 * HEAD_DIM), 1)
    return lane < HEAD_DIM


def split_pair(block):
    first = head_masks(block.shape[0])
    zeros = jnp.zeros_like(block)
    return jnp.concatenate([jnp.where(first, block, zeros), jnp.where(first, zeros, block)], axis=0)


def pair_attention(queries, keys, values):
    key_rows = keys.shape[0]
    scaled = queries * jnp.asarray(0.125, queries.dtype)
    scores = lax.dot_general(
        scaled, split_pair(keys), (((1,), (1,)), ((), ())), preferred_element_type=jnp.float32
    )
    weights = []
    tops = []
    counts = []
    for half in range(2):
        part = scores[:, half * key_rows : (half + 1) * key_rows]
        highest = jnp.max(part, axis=1, keepdims=True)
        exps = jnp.exp(part - highest)
        tops.append(highest)
        counts.append(jnp.sum(exps, axis=1, keepdims=True))
        weights.append(exps.astype(jnp.bfloat16))
    summed = jnp.dot(
        jnp.concatenate(weights, axis=1), split_pair(values), preferred_element_type=jnp.float32
    )
    return summed, tops, counts


PER_STEP = 2


def video_kernel(query_ref, key_ref, value_ref, *refs):
    out_ref = refs[-1]
    key_rows = key_ref.shape[0]
    for sub in range(PER_STEP):
        lanes = slice(sub * 2 * HEAD_DIM, (sub + 1) * 2 * HEAD_DIM)
        queries = query_ref[:, lanes] * jnp.asarray(0.125, query_ref.dtype)
        scores = lax.dot_general(
            split_pair(key_ref[:, lanes]), queries, (((1,), (1,)), ((), ())),
            preferred_element_type=jnp.float32,
        )
        weights = []
        counts = []
        for half in range(2):
            part = scores[half * key_rows : (half + 1) * key_rows]
            highest = jnp.max(part, axis=0, keepdims=True)
            exps = jnp.exp(part - highest)
            counts.append(jnp.sum(exps, axis=0, keepdims=True))
            weights.append(exps.astype(jnp.bfloat16))
        summed = lax.dot_general(
            split_pair(value_ref[:, lanes]), jnp.concatenate(weights, axis=0),
            (((0,), (0,)), ((), ())), preferred_element_type=jnp.float32,
        )
        lane = lax.broadcasted_iota(jnp.int32, summed.shape, 0)
        inverse = jnp.where(lane < HEAD_DIM, 1.0 / counts[0], 1.0 / counts[1])
        out_ref[:, lanes] = (summed * inverse).T.astype(out_ref.dtype)


def video_part(queries, keys, values, earlier, group, groups):
    rows, width = queries.shape
    pairs = width // (2 * HEAD_DIM) // groups
    first_pair = group * pairs // PER_STEP
    key_rows = keys.shape[0]
    lanes = 2 * HEAD_DIM * PER_STEP
    specs = [
        pl.BlockSpec((rows, lanes), lambda p: (0, p + first_pair)),
        pl.BlockSpec((key_rows, lanes), lambda p: (0, p + first_pair)),
        pl.BlockSpec((key_rows, lanes), lambda p: (0, p + first_pair)),
    ]
    operands = [queries, keys, values]
    aliases = {}
    if earlier is not None:
        specs.append(pl.BlockSpec(memory_space=pl.ANY))
        operands.append(earlier)
        aliases = {3: 0}
    return pl.pallas_call(
        video_kernel,
        grid=(pairs // PER_STEP,),
        in_specs=specs,
        out_specs=pl.BlockSpec((rows, lanes), lambda p: (0, p + first_pair)),
        out_shape=jax.ShapeDtypeStruct((rows, width), jnp.bfloat16),
        input_output_aliases=aliases,
        cost_estimate=pl.CostEstimate(
            flops=8 * rows * key_rows * width // groups,
            transcendentals=rows * key_rows * width // HEAD_DIM // groups,
            bytes_accessed=2 * (2 * rows * width + 2 * key_rows * width) // groups,
        ),
    )(*operands)


def audio_kernel(query_ref, key_ref, value_ref, sum_ref, total_ref, top_ref):
    step = pl.program_id(0)

    @pl.when(step == 0)
    def _():
        total_ref[...] = jnp.zeros_like(total_ref)
        top_ref[...] = jnp.zeros_like(top_ref)

    column = lax.broadcasted_iota(jnp.int32, total_ref.shape, 1)
    totals_now = total_ref[...]
    tops_now = top_ref[...]
    for sub in range(PER_STEP):
        lanes = slice(sub * 2 * HEAD_DIM, (sub + 1) * 2 * HEAD_DIM)
        summed, tops, counts = pair_attention(
            query_ref[:, lanes], key_ref[:, lanes], value_ref[:, lanes]
        )
        for half in range(2):
            here = column == 2 * (step * PER_STEP + sub) + half
            totals_now = jnp.where(here, counts[half], totals_now)
            tops_now = jnp.where(here, tops[half], tops_now)
        sum_ref[:, lanes] = summed
    total_ref[...] = totals_now
    top_ref[...] = tops_now


def audio_partial(queries, keys, values, group, groups):
    rows, width = queries.shape
    heads = width // HEAD_DIM // groups
    first_pair = group * heads // 2 // PER_STEP
    lanes = 2 * HEAD_DIM * PER_STEP
    key_rows = keys.shape[0]
    return pl.pallas_call(
        audio_kernel,
        grid=(heads // 2 // PER_STEP,),
        in_specs=[
            pl.BlockSpec((rows, lanes), lambda p: (0, p + first_pair)),
            pl.BlockSpec((key_rows, lanes), lambda p: (0, p + first_pair)),
            pl.BlockSpec((key_rows, lanes), lambda p: (0, p + first_pair)),
        ],
        out_specs=[
            pl.BlockSpec((rows, lanes), lambda p: (0, p)),
            pl.BlockSpec((rows, heads), lambda p: (0, 0)),
            pl.BlockSpec((rows, heads), lambda p: (0, 0)),
        ],
        out_shape=[
            jax.ShapeDtypeStruct((rows, heads * HEAD_DIM), jnp.float32),
            jax.ShapeDtypeStruct((rows, heads), jnp.float32),
            jax.ShapeDtypeStruct((rows, heads), jnp.float32),
        ],
        compiler_params=pltpu.CompilerParams(dimension_semantics=("arbitrary",)),
        cost_estimate=pl.CostEstimate(
            flops=8 * rows * key_rows * width // groups,
            transcendentals=rows * key_rows * heads,
            bytes_accessed=(2 * rows * width + 4 * key_rows * width + 4 * rows * width) // groups,
        ),
    )(queries, keys, values)


def local(video_q, video_k, video_v, audio_q, audio_k, audio_v):
    width = video_q.shape[1]
    heads = width // HEAD_DIM
    groups = 4
    steps = (lax.axis_size("seq") - 1).bit_length()
    all_queries = gather_levels(audio_q)
    audio_calls = [
        (
            lambda q, gs=gs: tuple(audio_partial(q, video_k, video_v, g, groups) for g in gs),
            all_queries,
        )
        for gs in ((0, 1), (2, 3))
    ]
    gathered, results = gather_rows(
        jnp.concatenate([audio_k, audio_v], axis=1), [None] * (steps - 2) + audio_calls
    )
    parts = [part for result in results for part in result]
    all_keys = gathered[:, :width]
    all_values = gathered[:, width:]
    state = [part[0] for part in parts] + [part[1] for part in parts] + [part[2] for part in parts]
    video_calls = [
        lambda earlier, g=g: video_part(video_q, all_keys, all_values, earlier, g, groups)
        for g in range(groups)
    ]
    mine, video_out = scatter_rows(state, heads, video_calls)
    audio_out = (mine[:, :width] / spread(mine[:, width : width + heads])).astype(jnp.bfloat16)
    return video_out, audio_out


def solution(mesh):
    placed = P(("groups", "seq"), None)
    return jax.shard_map(
        local,
        mesh=mesh,
        in_specs=(placed,) * 6,
        out_specs=(placed, placed),
        check_vma=False,
    )
```

```python
import jax
import jax.numpy as jnp
from jax import lax
from jax.experimental import pallas as pl
from jax.experimental.pallas import tpu as pltpu
from jax.sharding import PartitionSpec as P

HEAD_DIM = 64


def spread(scales):
    heads = scales.shape[1]
    shape = (heads, heads * HEAD_DIM)
    columns = lax.broadcasted_iota(jnp.int32, shape, 1) // HEAD_DIM
    expand = (columns == lax.broadcasted_iota(jnp.int32, shape, 0)).astype(jnp.float32)
    return jnp.dot(
        scales, expand, precision=lax.Precision.HIGHEST, preferred_element_type=jnp.float32
    )


def exchange(value, bit, count):
    pairs = [(source, source ^ bit) for source in range(count)]
    return lax.ppermute(value, "seq", pairs)


def gather_rows(block, during=()):
    count = lax.axis_size("seq")
    me = lax.axis_index("seq")
    held = block[None]
    results = []
    bit = count // 2
    step = 0
    while bit >= 1:
        work = during[step] if step < len(during) else None
        if work is not None:
            held, ready = lax.optimization_barrier((held, work[1]))
        arrived = exchange(held, bit, count)
        if work is not None:
            done = work[0](ready)
            arrived, done = lax.optimization_barrier((arrived, done))
            results.append(done)
        upper = (me & bit) != 0
        low = jnp.where(upper, arrived, held)
        high = jnp.where(upper, held, arrived)
        held = jnp.stack([low, high], axis=1).reshape((-1,) + block.shape)
        bit //= 2
        step += 1
    return held.reshape((count * block.shape[0],) + block.shape[1:]), results


def gather_levels(block):
    count = lax.axis_size("seq")
    me = lax.axis_index("seq")
    held = block[None]
    levels = []
    bit = count // 2
    if bit >= 2:
        levels.append((bit, bit // 2))
        bit //= 4
    while bit >= 1:
        levels.append((bit,))
        bit //= 2
    for level in levels:
        mask = sum(level)
        offsets = [0]
        for b in level:
            offsets = offsets + [o + b for o in offsets]
        pieces = {0: held}
        for offset in offsets[1:]:
            pairs = [(source, source ^ offset) for source in range(count)]
            pieces[offset] = lax.ppermute(held, "seq", pairs)
        mine = me & mask
        ordered = []
        for target in sorted(offsets):
            choice = pieces[0]
            for offset in offsets[1:]:
                choice = jnp.where((mine ^ offset) == target, pieces[offset], choice)
            ordered.append(choice)
        held = jnp.stack(ordered, axis=1).reshape((-1,) + block.shape)
    return held.reshape((count * block.shape[0],) + block.shape[1:])


def merge(first, second, heads):
    width = heads * HEAD_DIM
    top = jnp.maximum(first[:, width + heads :], second[:, width + heads :])
    first_scale = jnp.exp(first[:, width + heads :] - top)
    second_scale = jnp.exp(second[:, width + heads :] - top)
    totals = first[:, width : width + heads] * first_scale + second[:, width : width + heads] * second_scale
    summed = first[:, :width] * spread(first_scale) + second[:, :width] * spread(second_scale)
    return jnp.concatenate([summed, totals, top], axis=1)


def pieces(value, count):
    terms = []
    rest = value
    for ignored in range(count):
        rounded = lax.reduce_precision(rest, exponent_bits=8, mantissa_bits=7)
        terms.append(rounded.astype(jnp.bfloat16))
        rest = rest - rounded
    return terms


def encode(state, heads):
    width = heads * HEAD_DIM
    summed = state[..., :width].astype(jnp.bfloat16)
    totals = pieces(state[..., width : width + heads], 2)
    tops = pieces(state[..., width + heads :], 3)
    return jnp.concatenate([summed] + totals + tops, axis=-1)


def decode(sent, heads):
    width = heads * HEAD_DIM
    summed = sent[..., :width].astype(jnp.float32)
    parts = [
        sent[..., width + i * heads : width + (i + 1) * heads].astype(jnp.float32) for i in range(5)
    ]
    totals = parts[0] + parts[1]
    tops = (parts[2] + parts[3]) + parts[4]
    return jnp.concatenate([summed, totals, tops], axis=-1)


def scatter_rows(state, heads, during=()):
    count = lax.axis_size("seq")
    me = lax.axis_index("seq")
    rows = state.shape[0] // count
    held = state.reshape((count, rows, state.shape[1]))
    carried = None
    bit = 1
    step = 0
    while bit < count:
        pairs = held.reshape((-1, 2, rows, state.shape[1]))
        upper = (me & bit) != 0
        keep = jnp.where(upper, pairs[:, 1], pairs[:, 0])
        give = jnp.where(upper, pairs[:, 0], pairs[:, 1])
        work = during[step] if step < len(during) else None
        if work is not None:
            give, carried = lax.optimization_barrier((give, carried))
        arrived = decode(exchange(encode(give, heads), bit, count), heads)
        if work is not None:
            carried = work(carried)
            arrived, carried = lax.optimization_barrier((arrived, carried))
        held = merge(
            keep.reshape((-1, state.shape[1])), arrived.reshape((-1, state.shape[1])), heads
        ).reshape((-1, rows, state.shape[1]))
        bit *= 2
        step += 1
    for work in during[step:]:
        carried = work(carried)
    return held.reshape((rows, state.shape[1])), carried


def head_masks(rows):
    lane = lax.broadcasted_iota(jnp.int32, (rows, 2 * HEAD_DIM), 1)
    return lane < HEAD_DIM


def split_pair(block):
    first = head_masks(block.shape[0])
    zeros = jnp.zeros_like(block)
    return jnp.concatenate([jnp.where(first, block, zeros), jnp.where(first, zeros, block)], axis=0)


def pair_attention(queries, keys, values):
    key_rows = keys.shape[0]
    scores = (
        lax.dot_general(
            queries, split_pair(keys), (((1,), (1,)), ((), ())), preferred_element_type=jnp.float32
        )
        * 0.125
    )
    weights = []
    tops = []
    counts = []
    for half in range(2):
        part = scores[:, half * key_rows : (half + 1) * key_rows]
        highest = jnp.max(part, axis=1, keepdims=True)
        exps = jnp.exp(part - highest)
        tops.append(highest)
        counts.append(jnp.sum(exps, axis=1, keepdims=True))
        weights.append(exps.astype(jnp.bfloat16))
    summed = jnp.dot(
        jnp.concatenate(weights, axis=1), split_pair(values), preferred_element_type=jnp.float32
    )
    return summed, tops, counts


PER_STEP = 2


def video_kernel(query_ref, key_ref, value_ref, *refs):
    out_ref = refs[-1]
    key_rows = key_ref.shape[0]
    for sub in range(PER_STEP):
        lanes = slice(sub * 2 * HEAD_DIM, (sub + 1) * 2 * HEAD_DIM)
        queries = query_ref[:, lanes]
        scores = (
            lax.dot_general(
                split_pair(key_ref[:, lanes]), queries, (((1,), (1,)), ((), ())),
                preferred_element_type=jnp.float32,
            )
            * 0.125
        )
        weights = []
        counts = []
        for half in range(2):
            part = scores[half * key_rows : (half + 1) * key_rows]
            highest = jnp.max(part, axis=0, keepdims=True)
            exps = jnp.exp(part - highest)
            counts.append(jnp.sum(exps, axis=0, keepdims=True))
            weights.append(exps.astype(jnp.bfloat16))
        summed = lax.dot_general(
            split_pair(value_ref[:, lanes]), jnp.concatenate(weights, axis=0),
            (((0,), (0,)), ((), ())), preferred_element_type=jnp.float32,
        )
        lane = lax.broadcasted_iota(jnp.int32, summed.shape, 0)
        totals = jnp.where(lane < HEAD_DIM, counts[0], counts[1])
        out_ref[:, lanes] = (summed / totals).T.astype(out_ref.dtype)


def video_part(queries, keys, values, earlier, group, groups):
    rows, width = queries.shape
    pairs = width // (2 * HEAD_DIM) // groups
    first_pair = group * pairs // PER_STEP
    key_rows = keys.shape[0]
    lanes = 2 * HEAD_DIM * PER_STEP
    specs = [
        pl.BlockSpec((rows, lanes), lambda p: (0, p + first_pair)),
        pl.BlockSpec((key_rows, lanes), lambda p: (0, p + first_pair)),
        pl.BlockSpec((key_rows, lanes), lambda p: (0, p + first_pair)),
    ]
    operands = [queries, keys, values]
    aliases = {}
    if earlier is not None:
        specs.append(pl.BlockSpec(memory_space=pl.ANY))
        operands.append(earlier)
        aliases = {3: 0}
    return pl.pallas_call(
        video_kernel,
        grid=(pairs // PER_STEP,),
        in_specs=specs,
        out_specs=pl.BlockSpec((rows, lanes), lambda p: (0, p + first_pair)),
        out_shape=jax.ShapeDtypeStruct((rows, width), jnp.bfloat16),
        input_output_aliases=aliases,
        cost_estimate=pl.CostEstimate(
            flops=8 * rows * key_rows * width // groups,
            transcendentals=rows * key_rows * width // HEAD_DIM // groups,
            bytes_accessed=2 * (2 * rows * width + 2 * key_rows * width) // groups,
        ),
    )(*operands)


def audio_kernel(query_ref, key_ref, value_ref, sum_ref, total_ref, top_ref):
    step = pl.program_id(0)

    @pl.when(step == 0)
    def _():
        total_ref[...] = jnp.zeros_like(total_ref)
        top_ref[...] = jnp.zeros_like(top_ref)

    column = lax.broadcasted_iota(jnp.int32, total_ref.shape, 1)
    totals_now = total_ref[...]
    tops_now = top_ref[...]
    for sub in range(PER_STEP):
        lanes = slice(sub * 2 * HEAD_DIM, (sub + 1) * 2 * HEAD_DIM)
        summed, tops, counts = pair_attention(
            query_ref[:, lanes], key_ref[:, lanes], value_ref[:, lanes]
        )
        for half in range(2):
            here = column == 2 * (step * PER_STEP + sub) + half
            totals_now = jnp.where(here, counts[half], totals_now)
            tops_now = jnp.where(here, tops[half], tops_now)
        sum_ref[:, lanes] = summed
    total_ref[...] = totals_now
    top_ref[...] = tops_now


def audio_partial(queries, keys, values, group, groups):
    rows, width = queries.shape
    heads = width // HEAD_DIM // groups
    first_pair = group * heads // 2 // PER_STEP
    lanes = 2 * HEAD_DIM * PER_STEP
    key_rows = keys.shape[0]
    return pl.pallas_call(
        audio_kernel,
        grid=(heads // 2 // PER_STEP,),
        in_specs=[
            pl.BlockSpec((rows, lanes), lambda p: (0, p + first_pair)),
            pl.BlockSpec((key_rows, lanes), lambda p: (0, p + first_pair)),
            pl.BlockSpec((key_rows, lanes), lambda p: (0, p + first_pair)),
        ],
        out_specs=[
            pl.BlockSpec((rows, lanes), lambda p: (0, p)),
            pl.BlockSpec((rows, heads), lambda p: (0, 0)),
            pl.BlockSpec((rows, heads), lambda p: (0, 0)),
        ],
        out_shape=[
            jax.ShapeDtypeStruct((rows, heads * HEAD_DIM), jnp.float32),
            jax.ShapeDtypeStruct((rows, heads), jnp.float32),
            jax.ShapeDtypeStruct((rows, heads), jnp.float32),
        ],
        compiler_params=pltpu.CompilerParams(dimension_semantics=("arbitrary",)),
        cost_estimate=pl.CostEstimate(
            flops=8 * rows * key_rows * width // groups,
            transcendentals=rows * key_rows * heads,
            bytes_accessed=(2 * rows * width + 4 * key_rows * width + 4 * rows * width) // groups,
        ),
    )(queries, keys, values)


def local(video_q, video_k, video_v, audio_q, audio_k, audio_v):
    width = video_q.shape[1]
    heads = width // HEAD_DIM
    groups = 4
    steps = (lax.axis_size("seq") - 1).bit_length()
    all_queries = gather_levels(audio_q)
    audio_calls = [
        (
            lambda q, gs=gs: tuple(audio_partial(q, video_k, video_v, g, groups) for g in gs),
            all_queries,
        )
        for gs in ((0, 1), (2, 3))
    ]
    gathered, ignored = gather_rows(jnp.concatenate([audio_k, audio_v], axis=1))
    ready, gathered = lax.optimization_barrier((all_queries, gathered))
    parts = [part for call in audio_calls for part in call[0](ready)]
    all_keys = gathered[:, :width]
    all_values = gathered[:, width:]
    state = jnp.concatenate(
        [part[0] for part in parts] + [part[1] for part in parts] + [part[2] for part in parts],
        axis=1,
    )
    video_calls = [
        lambda earlier, g=g: video_part(video_q, all_keys, all_values, earlier, g, groups)
        for g in range(groups)
    ]
    mine, video_out = scatter_rows(state, heads, video_calls)
    audio_out = (mine[:, :width] / spread(mine[:, width : width + heads])).astype(jnp.bfloat16)
    return video_out, audio_out


def solution(mesh):
    placed = P(("groups", "seq"), None)
    return jax.shard_map(
        local,
        mesh=mesh,
        in_specs=(placed,) * 6,
        out_specs=(placed, placed),
        check_vma=False,
    )
```

```python
import jax
import jax.numpy as jnp
from jax import lax
from jax.experimental import pallas as pl
from jax.experimental.pallas import tpu as pltpu
from jax.sharding import PartitionSpec as P

HEAD_DIM = 64


def spread(scales):
    heads = scales.shape[1]
    shape = (heads, heads * HEAD_DIM)
    columns = lax.broadcasted_iota(jnp.int32, shape, 1) // HEAD_DIM
    expand = (columns == lax.broadcasted_iota(jnp.int32, shape, 0)).astype(jnp.float32)
    return jnp.dot(
        scales, expand, precision=lax.Precision.HIGHEST, preferred_element_type=jnp.float32
    )


def exchange(value, bit, count):
    pairs = [(source, source ^ bit) for source in range(count)]
    return lax.ppermute(value, "seq", pairs)


def gather_rows(block, during=()):
    count = lax.axis_size("seq")
    me = lax.axis_index("seq")
    held = block[None]
    results = []
    bit = count // 2
    step = 0
    while bit >= 1:
        work = during[step] if step < len(during) else None
        if work is not None:
            held, ready = lax.optimization_barrier((held, work[1]))
        arrived = exchange(held, bit, count)
        if work is not None:
            done = work[0](ready)
            arrived, done = lax.optimization_barrier((arrived, done))
            results.append(done)
        upper = (me & bit) != 0
        low = jnp.where(upper, arrived, held)
        high = jnp.where(upper, held, arrived)
        held = jnp.stack([low, high], axis=1).reshape((-1,) + block.shape)
        bit //= 2
        step += 1
    return held.reshape((count * block.shape[0],) + block.shape[1:]), results


def merge(first, second, heads):
    width = heads * HEAD_DIM
    top = jnp.maximum(first[:, width + heads :], second[:, width + heads :])
    first_scale = jnp.exp(first[:, width + heads :] - top)
    second_scale = jnp.exp(second[:, width + heads :] - top)
    totals = first[:, width : width + heads] * first_scale + second[:, width : width + heads] * second_scale
    summed = first[:, :width] * spread(first_scale) + second[:, :width] * spread(second_scale)
    return jnp.concatenate([summed, totals, top], axis=1)


def pieces(value, count):
    terms = []
    rest = value
    for ignored in range(count):
        rounded = lax.reduce_precision(rest, exponent_bits=8, mantissa_bits=7)
        terms.append(rounded.astype(jnp.bfloat16))
        rest = rest - rounded
    return terms


def encode(state, heads):
    width = heads * HEAD_DIM
    summed = state[..., :width].astype(jnp.bfloat16)
    totals = pieces(state[..., width : width + heads], 2)
    tops = pieces(state[..., width + heads :], 3)
    return jnp.concatenate([summed] + totals + tops, axis=-1)


def decode(sent, heads):
    width = heads * HEAD_DIM
    summed = sent[..., :width].astype(jnp.float32)
    parts = [
        sent[..., width + i * heads : width + (i + 1) * heads].astype(jnp.float32) for i in range(5)
    ]
    totals = parts[0] + parts[1]
    tops = (parts[2] + parts[3]) + parts[4]
    return jnp.concatenate([summed, totals, tops], axis=-1)


def scatter_rows(state, heads, during=()):
    count = lax.axis_size("seq")
    me = lax.axis_index("seq")
    rows = state.shape[0] // count
    held = state.reshape((count, rows, state.shape[1]))
    carried = None
    bit = 1
    step = 0
    while bit < count:
        pairs = held.reshape((-1, 2, rows, state.shape[1]))
        upper = (me & bit) != 0
        keep = jnp.where(upper, pairs[:, 1], pairs[:, 0])
        give = jnp.where(upper, pairs[:, 0], pairs[:, 1])
        work = during[step] if step < len(during) else None
        if work is not None:
            give, carried = lax.optimization_barrier((give, carried))
        arrived = decode(exchange(encode(give, heads), bit, count), heads)
        if work is not None:
            carried = work(carried)
            arrived, carried = lax.optimization_barrier((arrived, carried))
        held = merge(
            keep.reshape((-1, state.shape[1])), arrived.reshape((-1, state.shape[1])), heads
        ).reshape((-1, rows, state.shape[1]))
        bit *= 2
        step += 1
    for work in during[step:]:
        carried = work(carried)
    return held.reshape((rows, state.shape[1])), carried


def head_masks(rows):
    lane = lax.broadcasted_iota(jnp.int32, (rows, 2 * HEAD_DIM), 1)
    return lane < HEAD_DIM


def split_pair(block):
    first = head_masks(block.shape[0])
    zeros = jnp.zeros_like(block)
    return jnp.concatenate([jnp.where(first, block, zeros), jnp.where(first, zeros, block)], axis=0)


def pair_attention(queries, keys, values):
    key_rows = keys.shape[0]
    scores = (
        lax.dot_general(
            queries, split_pair(keys), (((1,), (1,)), ((), ())), preferred_element_type=jnp.float32
        )
        * 0.125
    )
    weights = []
    tops = []
    counts = []
    for half in range(2):
        part = scores[:, half * key_rows : (half + 1) * key_rows]
        highest = jnp.max(part, axis=1, keepdims=True)
        exps = jnp.exp(part - highest)
        tops.append(highest)
        counts.append(jnp.sum(exps, axis=1, keepdims=True))
        weights.append(exps.astype(jnp.bfloat16))
    summed = jnp.dot(
        jnp.concatenate(weights, axis=1), split_pair(values), preferred_element_type=jnp.float32
    )
    return summed, tops, counts


PER_STEP = 2


def video_kernel(query_ref, key_ref, value_ref, *refs):
    out_ref = refs[-1]
    key_rows = key_ref.shape[0]
    for sub in range(PER_STEP):
        lanes = slice(sub * 2 * HEAD_DIM, (sub + 1) * 2 * HEAD_DIM)
        queries = query_ref[:, lanes]
        scores = (
            lax.dot_general(
                split_pair(key_ref[:, lanes]), queries, (((1,), (1,)), ((), ())),
                preferred_element_type=jnp.float32,
            )
            * 0.125
        )
        weights = []
        counts = []
        for half in range(2):
            part = scores[half * key_rows : (half + 1) * key_rows]
            highest = jnp.max(part, axis=0, keepdims=True)
            exps = jnp.exp(part - highest)
            counts.append(jnp.sum(exps, axis=0, keepdims=True))
            weights.append(exps.astype(jnp.bfloat16))
        summed = lax.dot_general(
            split_pair(value_ref[:, lanes]), jnp.concatenate(weights, axis=0),
            (((0,), (0,)), ((), ())), preferred_element_type=jnp.float32,
        )
        lane = lax.broadcasted_iota(jnp.int32, summed.shape, 0)
        totals = jnp.where(lane < HEAD_DIM, counts[0], counts[1])
        out_ref[:, lanes] = (summed / totals).T.astype(out_ref.dtype)


def video_part(queries, keys, values, earlier, group, groups):
    rows, width = queries.shape
    pairs = width // (2 * HEAD_DIM) // groups
    first_pair = group * pairs // PER_STEP
    key_rows = keys.shape[0]
    lanes = 2 * HEAD_DIM * PER_STEP
    specs = [
        pl.BlockSpec((rows, lanes), lambda p: (0, p + first_pair)),
        pl.BlockSpec((key_rows, lanes), lambda p: (0, p + first_pair)),
        pl.BlockSpec((key_rows, lanes), lambda p: (0, p + first_pair)),
    ]
    operands = [queries, keys, values]
    aliases = {}
    if earlier is not None:
        specs.append(pl.BlockSpec(memory_space=pl.ANY))
        operands.append(earlier)
        aliases = {3: 0}
    return pl.pallas_call(
        video_kernel,
        grid=(pairs // PER_STEP,),
        in_specs=specs,
        out_specs=pl.BlockSpec((rows, lanes), lambda p: (0, p + first_pair)),
        out_shape=jax.ShapeDtypeStruct((rows, width), jnp.bfloat16),
        input_output_aliases=aliases,
        cost_estimate=pl.CostEstimate(
            flops=8 * rows * key_rows * width // groups,
            transcendentals=rows * key_rows * width // HEAD_DIM // groups,
            bytes_accessed=2 * (2 * rows * width + 2 * key_rows * width) // groups,
        ),
    )(*operands)


def audio_kernel(query_ref, key_ref, value_ref, sum_ref, total_ref, top_ref):
    step = pl.program_id(0)

    @pl.when(step == 0)
    def _():
        total_ref[...] = jnp.zeros_like(total_ref)
        top_ref[...] = jnp.zeros_like(top_ref)

    column = lax.broadcasted_iota(jnp.int32, total_ref.shape, 1)
    totals_now = total_ref[...]
    tops_now = top_ref[...]
    for sub in range(PER_STEP):
        lanes = slice(sub * 2 * HEAD_DIM, (sub + 1) * 2 * HEAD_DIM)
        summed, tops, counts = pair_attention(
            query_ref[:, lanes], key_ref[:, lanes], value_ref[:, lanes]
        )
        for half in range(2):
            here = column == 2 * (step * PER_STEP + sub) + half
            totals_now = jnp.where(here, counts[half], totals_now)
            tops_now = jnp.where(here, tops[half], tops_now)
        sum_ref[:, lanes] = summed
    total_ref[...] = totals_now
    top_ref[...] = tops_now


def audio_partial(queries, keys, values, group, groups):
    rows, width = queries.shape
    heads = width // HEAD_DIM // groups
    first_pair = group * heads // 2 // PER_STEP
    lanes = 2 * HEAD_DIM * PER_STEP
    key_rows = keys.shape[0]
    return pl.pallas_call(
        audio_kernel,
        grid=(heads // 2 // PER_STEP,),
        in_specs=[
            pl.BlockSpec((rows, lanes), lambda p: (0, p + first_pair)),
            pl.BlockSpec((key_rows, lanes), lambda p: (0, p + first_pair)),
            pl.BlockSpec((key_rows, lanes), lambda p: (0, p + first_pair)),
        ],
        out_specs=[
            pl.BlockSpec((rows, lanes), lambda p: (0, p)),
            pl.BlockSpec((rows, heads), lambda p: (0, 0)),
            pl.BlockSpec((rows, heads), lambda p: (0, 0)),
        ],
        out_shape=[
            jax.ShapeDtypeStruct((rows, heads * HEAD_DIM), jnp.float32),
            jax.ShapeDtypeStruct((rows, heads), jnp.float32),
            jax.ShapeDtypeStruct((rows, heads), jnp.float32),
        ],
        compiler_params=pltpu.CompilerParams(dimension_semantics=("arbitrary",)),
        cost_estimate=pl.CostEstimate(
            flops=8 * rows * key_rows * width // groups,
            transcendentals=rows * key_rows * heads,
            bytes_accessed=(2 * rows * width + 4 * key_rows * width + 4 * rows * width) // groups,
        ),
    )(queries, keys, values)


def local(video_q, video_k, video_v, audio_q, audio_k, audio_v):
    width = video_q.shape[1]
    heads = width // HEAD_DIM
    groups = 4
    steps = (lax.axis_size("seq") - 1).bit_length()
    all_queries, ignored = gather_rows(audio_q)
    audio_calls = [
        (
            lambda q, gs=gs: tuple(audio_partial(q, video_k, video_v, g, groups) for g in gs),
            all_queries,
        )
        for gs in ((0, 1), (2, 3))
    ]
    gathered, results = gather_rows(
        jnp.concatenate([audio_k, audio_v], axis=1), [None] * (steps - 2) + audio_calls
    )
    parts = [part for result in results for part in result]
    all_keys = gathered[:, :width]
    all_values = gathered[:, width:]
    state = jnp.concatenate(
        [part[0] for part in parts] + [part[1] for part in parts] + [part[2] for part in parts],
        axis=1,
    )
    video_calls = [
        lambda earlier, g=g: video_part(video_q, all_keys, all_values, earlier, g, groups)
        for g in range(groups)
    ]
    mine, video_out = scatter_rows(state, heads, video_calls)
    audio_out = (mine[:, :width] / spread(mine[:, width : width + heads])).astype(jnp.bfloat16)
    return video_out, audio_out


def solution(mesh):
    placed = P(("groups", "seq"), None)
    return jax.shard_map(
        local,
        mesh=mesh,
        in_specs=(placed,) * 6,
        out_specs=(placed, placed),
        check_vma=False,
    )
```

```python
import jax
import jax.numpy as jnp
from jax import lax
from jax.experimental import pallas as pl
from jax.experimental.pallas import tpu as pltpu
from jax.sharding import PartitionSpec as P

HEAD_DIM = 64


def spread(scales):
    heads = scales.shape[1]
    shape = (heads, heads * HEAD_DIM)
    columns = lax.broadcasted_iota(jnp.int32, shape, 1) // HEAD_DIM
    expand = (columns == lax.broadcasted_iota(jnp.int32, shape, 0)).astype(jnp.float32)
    return jnp.dot(
        scales, expand, precision=lax.Precision.HIGHEST, preferred_element_type=jnp.float32
    )


def exchange(value, bit, count):
    pairs = [(source, source ^ bit) for source in range(count)]
    return lax.ppermute(value, "seq", pairs)


def gather_rows(block, during=()):
    count = lax.axis_size("seq")
    me = lax.axis_index("seq")
    held = block[None]
    results = []
    bit = count // 2
    step = 0
    while bit >= 1:
        work = during[step] if step < len(during) else None
        if work is not None:
            held, ready = lax.optimization_barrier((held, work[1]))
        arrived = exchange(held, bit, count)
        if work is not None:
            done = work[0](ready)
            arrived, done = lax.optimization_barrier((arrived, done))
            results.append(done)
        upper = (me & bit) != 0
        low = jnp.where(upper, arrived, held)
        high = jnp.where(upper, held, arrived)
        held = jnp.stack([low, high], axis=1).reshape((-1,) + block.shape)
        bit //= 2
        step += 1
    return held.reshape((count * block.shape[0],) + block.shape[1:]), results


def gather_levels(block):
    count = lax.axis_size("seq")
    me = lax.axis_index("seq")
    held = block[None]
    levels = []
    bit = count // 2
    if bit >= 2:
        levels.append((bit, bit // 2))
        bit //= 4
    while bit >= 1:
        levels.append((bit,))
        bit //= 2
    for level in levels:
        mask = sum(level)
        offsets = [0]
        for b in level:
            offsets = offsets + [o + b for o in offsets]
        pieces = {0: held}
        for offset in offsets[1:]:
            pairs = [(source, source ^ offset) for source in range(count)]
            pieces[offset] = lax.ppermute(held, "seq", pairs)
        mine = me & mask
        ordered = []
        for target in sorted(offsets):
            choice = pieces[0]
            for offset in offsets[1:]:
                choice = jnp.where((mine ^ offset) == target, pieces[offset], choice)
            ordered.append(choice)
        held = jnp.stack(ordered, axis=1).reshape((-1,) + block.shape)
    return held.reshape((count * block.shape[0],) + block.shape[1:])


def merge(first, second, heads):
    width = heads * HEAD_DIM
    top = jnp.maximum(first[:, width + heads :], second[:, width + heads :])
    first_scale = jnp.exp(first[:, width + heads :] - top)
    second_scale = jnp.exp(second[:, width + heads :] - top)
    totals = first[:, width : width + heads] * first_scale + second[:, width : width + heads] * second_scale
    summed = first[:, :width] * spread(first_scale) + second[:, :width] * spread(second_scale)
    return jnp.concatenate([summed, totals, top], axis=1)


def pieces(value, count):
    terms = []
    rest = value
    for ignored in range(count):
        rounded = lax.reduce_precision(rest, exponent_bits=8, mantissa_bits=7)
        terms.append(rounded.astype(jnp.bfloat16))
        rest = rest - rounded
    return terms


def encode(state, heads):
    width = heads * HEAD_DIM
    summed = state[..., :width].astype(jnp.bfloat16)
    totals = pieces(state[..., width : width + heads], 2)
    tops = pieces(state[..., width + heads :], 3)
    return jnp.concatenate([summed] + totals + tops, axis=-1)


def decode(sent, heads):
    width = heads * HEAD_DIM
    summed = sent[..., :width].astype(jnp.float32)
    parts = [
        sent[..., width + i * heads : width + (i + 1) * heads].astype(jnp.float32) for i in range(5)
    ]
    totals = parts[0] + parts[1]
    tops = (parts[2] + parts[3]) + parts[4]
    return jnp.concatenate([summed, totals, tops], axis=-1)


def scatter_rows(state, heads, during=()):
    count = lax.axis_size("seq")
    me = lax.axis_index("seq")
    rows = state.shape[0] // count
    held = state.reshape((count, rows, state.shape[1]))
    carried = None
    bit = 1
    step = 0
    while bit < count:
        pairs = held.reshape((-1, 2, rows, state.shape[1]))
        upper = (me & bit) != 0
        keep = jnp.where(upper, pairs[:, 1], pairs[:, 0])
        give = jnp.where(upper, pairs[:, 0], pairs[:, 1])
        work = during[step] if step < len(during) else None
        if work is not None:
            give, carried = lax.optimization_barrier((give, carried))
        arrived = decode(exchange(encode(give, heads), bit, count), heads)
        if work is not None:
            carried = work(carried)
            arrived, carried = lax.optimization_barrier((arrived, carried))
        held = merge(
            keep.reshape((-1, state.shape[1])), arrived.reshape((-1, state.shape[1])), heads
        ).reshape((-1, rows, state.shape[1]))
        bit *= 2
        step += 1
    for work in during[step:]:
        carried = work(carried)
    return held.reshape((rows, state.shape[1])), carried


def head_masks(rows):
    lane = lax.broadcasted_iota(jnp.int32, (rows, 2 * HEAD_DIM), 1)
    return lane < HEAD_DIM


def split_pair(block):
    first = head_masks(block.shape[0])
    zeros = jnp.zeros_like(block)
    return jnp.concatenate([jnp.where(first, block, zeros), jnp.where(first, zeros, block)], axis=0)


def pair_attention(queries, keys, values):
    key_rows = keys.shape[0]
    scores = (
        lax.dot_general(
            queries, split_pair(keys), (((1,), (1,)), ((), ())), preferred_element_type=jnp.float32
        )
        * 0.125
    )
    weights = []
    tops = []
    counts = []
    for half in range(2):
        part = scores[:, half * key_rows : (half + 1) * key_rows]
        highest = jnp.max(part, axis=1, keepdims=True)
        exps = jnp.exp(part - highest)
        tops.append(highest)
        counts.append(jnp.sum(exps, axis=1, keepdims=True))
        weights.append(exps.astype(jnp.bfloat16))
    summed = jnp.dot(
        jnp.concatenate(weights, axis=1), split_pair(values), preferred_element_type=jnp.float32
    )
    return summed, tops, counts


PER_STEP = 2


def video_kernel(query_ref, key_ref, value_ref, *refs):
    out_ref = refs[-1]
    key_rows = key_ref.shape[0]
    for sub in range(PER_STEP):
        lanes = slice(sub * 2 * HEAD_DIM, (sub + 1) * 2 * HEAD_DIM)
        queries = query_ref[:, lanes]
        scores = (
            lax.dot_general(
                split_pair(key_ref[:, lanes]), queries, (((1,), (1,)), ((), ())),
                preferred_element_type=jnp.float32,
            )
            * 0.125
        )
        weights = []
        counts = []
        for half in range(2):
            part = scores[half * key_rows : (half + 1) * key_rows]
            highest = jnp.max(part, axis=0, keepdims=True)
            exps = jnp.exp(part - highest)
            counts.append(jnp.sum(exps, axis=0, keepdims=True))
            weights.append(exps.astype(jnp.bfloat16))
        summed = lax.dot_general(
            split_pair(value_ref[:, lanes]), jnp.concatenate(weights, axis=0),
            (((0,), (0,)), ((), ())), preferred_element_type=jnp.float32,
        )
        lane = lax.broadcasted_iota(jnp.int32, summed.shape, 0)
        totals = jnp.where(lane < HEAD_DIM, counts[0], counts[1])
        out_ref[:, lanes] = (summed / totals).T.astype(out_ref.dtype)


def video_part(queries, keys, values, earlier, group, groups):
    rows, width = queries.shape
    pairs = width // (2 * HEAD_DIM) // groups
    first_pair = group * pairs // PER_STEP
    key_rows = keys.shape[0]
    lanes = 2 * HEAD_DIM * PER_STEP
    specs = [
        pl.BlockSpec((rows, lanes), lambda p: (0, p + first_pair)),
        pl.BlockSpec((key_rows, lanes), lambda p: (0, p + first_pair)),
        pl.BlockSpec((key_rows, lanes), lambda p: (0, p + first_pair)),
    ]
    operands = [queries, keys, values]
    aliases = {}
    if earlier is not None:
        specs.append(pl.BlockSpec(memory_space=pl.ANY))
        operands.append(earlier)
        aliases = {3: 0}
    return pl.pallas_call(
        video_kernel,
        grid=(pairs // PER_STEP,),
        in_specs=specs,
        out_specs=pl.BlockSpec((rows, lanes), lambda p: (0, p + first_pair)),
        out_shape=jax.ShapeDtypeStruct((rows, width), jnp.bfloat16),
        input_output_aliases=aliases,
        cost_estimate=pl.CostEstimate(
            flops=8 * rows * key_rows * width // groups,
            transcendentals=rows * key_rows * width // HEAD_DIM // groups,
            bytes_accessed=2 * (2 * rows * width + 2 * key_rows * width) // groups,
        ),
    )(*operands)


def audio_kernel(query_ref, key_ref, value_ref, sum_ref, total_ref, top_ref):
    step = pl.program_id(0)

    @pl.when(step == 0)
    def _():
        total_ref[...] = jnp.zeros_like(total_ref)
        top_ref[...] = jnp.zeros_like(top_ref)

    column = lax.broadcasted_iota(jnp.int32, total_ref.shape, 1)
    totals_now = total_ref[...]
    tops_now = top_ref[...]
    for sub in range(PER_STEP):
        lanes = slice(sub * 2 * HEAD_DIM, (sub + 1) * 2 * HEAD_DIM)
        summed, tops, counts = pair_attention(
            query_ref[:, lanes], key_ref[:, lanes], value_ref[:, lanes]
        )
        for half in range(2):
            here = column == 2 * (step * PER_STEP + sub) + half
            totals_now = jnp.where(here, counts[half], totals_now)
            tops_now = jnp.where(here, tops[half], tops_now)
        sum_ref[:, lanes] = summed
    total_ref[...] = totals_now
    top_ref[...] = tops_now


def audio_partial(queries, keys, values, group, groups):
    rows, width = queries.shape
    heads = width // HEAD_DIM // groups
    first_pair = group * heads // 2 // PER_STEP
    lanes = 2 * HEAD_DIM * PER_STEP
    key_rows = keys.shape[0]
    return pl.pallas_call(
        audio_kernel,
        grid=(heads // 2 // PER_STEP,),
        in_specs=[
            pl.BlockSpec((rows, lanes), lambda p: (0, p + first_pair)),
            pl.BlockSpec((key_rows, lanes), lambda p: (0, p + first_pair)),
            pl.BlockSpec((key_rows, lanes), lambda p: (0, p + first_pair)),
        ],
        out_specs=[
            pl.BlockSpec((rows, lanes), lambda p: (0, p)),
            pl.BlockSpec((rows, heads), lambda p: (0, 0)),
            pl.BlockSpec((rows, heads), lambda p: (0, 0)),
        ],
        out_shape=[
            jax.ShapeDtypeStruct((rows, heads * HEAD_DIM), jnp.float32),
            jax.ShapeDtypeStruct((rows, heads), jnp.float32),
            jax.ShapeDtypeStruct((rows, heads), jnp.float32),
        ],
        compiler_params=pltpu.CompilerParams(dimension_semantics=("arbitrary",)),
        cost_estimate=pl.CostEstimate(
            flops=8 * rows * key_rows * width // groups,
            transcendentals=rows * key_rows * heads,
            bytes_accessed=(2 * rows * width + 4 * key_rows * width + 4 * rows * width) // groups,
        ),
    )(queries, keys, values)


def local(video_q, video_k, video_v, audio_q, audio_k, audio_v):
    width = video_q.shape[1]
    heads = width // HEAD_DIM
    groups = 4
    steps = (lax.axis_size("seq") - 1).bit_length()
    all_queries = gather_levels(audio_q)
    audio_calls = [
        (
            lambda q, g=g: (audio_partial(q, video_k, video_v, g, 2),),
            all_queries,
        )
        for g in range(2)
    ]
    gathered, results = gather_rows(
        jnp.concatenate([audio_k, audio_v], axis=1), [None] * (steps - 2) + audio_calls
    )
    parts = [part for result in results for part in result]
    all_keys = gathered[:, :width]
    all_values = gathered[:, width:]
    state = jnp.concatenate(
        [part[0] for part in parts] + [part[1] for part in parts] + [part[2] for part in parts],
        axis=1,
    )
    video_calls = [
        lambda earlier, g=g: video_part(video_q, all_keys, all_values, earlier, g, groups)
        for g in range(groups)
    ]
    mine, video_out = scatter_rows(state, heads, video_calls)
    audio_out = (mine[:, :width] / spread(mine[:, width : width + heads])).astype(jnp.bfloat16)
    return video_out, audio_out


def solution(mesh):
    placed = P(("groups", "seq"), None)
    return jax.shard_map(
        local,
        mesh=mesh,
        in_specs=(placed,) * 6,
        out_specs=(placed, placed),
        check_vma=False,
    )
```

```python
import jax
import jax.numpy as jnp
from jax import lax
from jax.experimental import pallas as pl
from jax.experimental.pallas import tpu as pltpu
from jax.sharding import PartitionSpec as P

HEAD_DIM = 64


def spread(scales):
    heads = scales.shape[1]
    shape = (heads, heads * HEAD_DIM)
    columns = lax.broadcasted_iota(jnp.int32, shape, 1) // HEAD_DIM
    expand = (columns == lax.broadcasted_iota(jnp.int32, shape, 0)).astype(jnp.float32)
    return jnp.dot(
        scales, expand, precision=lax.Precision.HIGHEST, preferred_element_type=jnp.float32
    )


def exchange(value, bit, count):
    pairs = [(source, source ^ bit) for source in range(count)]
    return lax.ppermute(value, "seq", pairs)


def gather_rows(block, during=()):
    count = lax.axis_size("seq")
    me = lax.axis_index("seq")
    held = block[None]
    results = []
    bit = count // 2
    step = 0
    while bit >= 1:
        work = during[step] if step < len(during) else None
        if work is not None:
            held, ready = lax.optimization_barrier((held, work[1]))
        arrived = exchange(held, bit, count)
        if work is not None:
            done = work[0](ready)
            arrived, done = lax.optimization_barrier((arrived, done))
            results.append(done)
        upper = (me & bit) != 0
        low = jnp.where(upper, arrived, held)
        high = jnp.where(upper, held, arrived)
        held = jnp.stack([low, high], axis=1).reshape((-1,) + block.shape)
        bit //= 2
        step += 1
    return held.reshape((count * block.shape[0],) + block.shape[1:]), results


def gather_levels(block):
    count = lax.axis_size("seq")
    me = lax.axis_index("seq")
    held = block[None]
    levels = []
    bit = count // 2
    if bit >= 2:
        levels.append((bit, bit // 2))
        bit //= 4
    while bit >= 1:
        levels.append((bit,))
        bit //= 2
    for level in levels:
        mask = sum(level)
        offsets = [0]
        for b in level:
            offsets = offsets + [o + b for o in offsets]
        pieces = {0: held}
        for offset in offsets[1:]:
            pairs = [(source, source ^ offset) for source in range(count)]
            pieces[offset] = lax.ppermute(held, "seq", pairs)
        mine = me & mask
        ordered = []
        for target in sorted(offsets):
            choice = pieces[0]
            for offset in offsets[1:]:
                choice = jnp.where((mine ^ offset) == target, pieces[offset], choice)
            ordered.append(choice)
        held = jnp.stack(ordered, axis=1).reshape((-1,) + block.shape)
    return held.reshape((count * block.shape[0],) + block.shape[1:])


def merge(first, second, heads):
    width = heads * HEAD_DIM
    top = jnp.maximum(first[:, width + heads :], second[:, width + heads :])
    first_scale = jnp.exp(first[:, width + heads :] - top)
    second_scale = jnp.exp(second[:, width + heads :] - top)
    totals = first[:, width : width + heads] * first_scale + second[:, width : width + heads] * second_scale
    summed = first[:, :width] * spread(first_scale) + second[:, :width] * spread(second_scale)
    return jnp.concatenate([summed, totals, top], axis=1)


def pieces(value, count):
    terms = []
    rest = value
    for ignored in range(count):
        rounded = lax.reduce_precision(rest, exponent_bits=8, mantissa_bits=7)
        terms.append(rounded.astype(jnp.bfloat16))
        rest = rest - rounded
    return terms


def encode(state, heads):
    width = heads * HEAD_DIM
    summed = state[..., :width].astype(jnp.bfloat16)
    totals = pieces(state[..., width : width + heads], 2)
    tops = pieces(state[..., width + heads :], 3)
    return jnp.concatenate([summed] + totals + tops, axis=-1)


def decode(sent, heads):
    width = heads * HEAD_DIM
    summed = sent[..., :width].astype(jnp.float32)
    parts = [
        sent[..., width + i * heads : width + (i + 1) * heads].astype(jnp.float32) for i in range(5)
    ]
    totals = parts[0] + parts[1]
    tops = (parts[2] + parts[3]) + parts[4]
    return jnp.concatenate([summed, totals, tops], axis=-1)


def scatter_rows(state, heads, during=()):
    count = lax.axis_size("seq")
    me = lax.axis_index("seq")
    rows = state.shape[0] // count
    held = state.reshape((count, rows, state.shape[1]))
    carried = None
    bit = 1
    step = 0
    while bit < count:
        pairs = held.reshape((-1, 2, rows, state.shape[1]))
        upper = (me & bit) != 0
        keep = jnp.where(upper, pairs[:, 1], pairs[:, 0])
        give = jnp.where(upper, pairs[:, 0], pairs[:, 1])
        work = during[step] if step < len(during) else None
        if work is not None:
            give, carried = lax.optimization_barrier((give, carried))
        arrived = decode(exchange(encode(give, heads), bit, count), heads)
        if work is not None:
            carried = work(carried)
            arrived, carried = lax.optimization_barrier((arrived, carried))
        held = merge(
            keep.reshape((-1, state.shape[1])), arrived.reshape((-1, state.shape[1])), heads
        ).reshape((-1, rows, state.shape[1]))
        bit *= 2
        step += 1
    for work in during[step:]:
        carried = work(carried)
    return held.reshape((rows, state.shape[1])), carried


def head_masks(rows):
    lane = lax.broadcasted_iota(jnp.int32, (rows, 2 * HEAD_DIM), 1)
    return lane < HEAD_DIM


def split_pair(block):
    first = head_masks(block.shape[0])
    zeros = jnp.zeros_like(block)
    return jnp.concatenate([jnp.where(first, block, zeros), jnp.where(first, zeros, block)], axis=0)


def pair_attention(queries, keys, values):
    key_rows = keys.shape[0]
    scores = (
        lax.dot_general(
            queries, split_pair(keys), (((1,), (1,)), ((), ())), preferred_element_type=jnp.float32
        )
        * 0.125
    )
    weights = []
    tops = []
    counts = []
    for half in range(2):
        part = scores[:, half * key_rows : (half + 1) * key_rows]
        highest = jnp.max(part, axis=1, keepdims=True)
        exps = jnp.exp(part - highest)
        tops.append(highest)
        counts.append(jnp.sum(exps, axis=1, keepdims=True))
        weights.append(exps.astype(jnp.bfloat16))
    summed = jnp.dot(
        jnp.concatenate(weights, axis=1), split_pair(values), preferred_element_type=jnp.float32
    )
    return summed, tops, counts


PER_STEP = 2


def video_kernel(query_ref, key_ref, value_ref, *refs):
    out_ref = refs[-1]
    key_rows = key_ref.shape[0]
    for sub in range(PER_STEP):
        lanes = slice(sub * 2 * HEAD_DIM, (sub + 1) * 2 * HEAD_DIM)
        queries = query_ref[:, lanes]
        scores = (
            lax.dot_general(
                split_pair(key_ref[:, lanes]), queries, (((1,), (1,)), ((), ())),
                preferred_element_type=jnp.float32,
            )
            * 0.125
        )
        weights = []
        counts = []
        for half in range(2):
            part = scores[half * key_rows : (half + 1) * key_rows]
            highest = jnp.max(part, axis=0, keepdims=True)
            exps = jnp.exp(part - highest)
            counts.append(jnp.sum(exps, axis=0, keepdims=True))
            weights.append(exps.astype(jnp.bfloat16))
        summed = lax.dot_general(
            split_pair(value_ref[:, lanes]), jnp.concatenate(weights, axis=0),
            (((0,), (0,)), ((), ())), preferred_element_type=jnp.float32,
        )
        lane = lax.broadcasted_iota(jnp.int32, summed.shape, 0)
        totals = jnp.where(lane < HEAD_DIM, counts[0], counts[1])
        out_ref[:, lanes] = (summed / totals).T.astype(out_ref.dtype)


def video_part(queries, keys, values, earlier, group, groups):
    rows, width = queries.shape
    pairs = width // (2 * HEAD_DIM) // groups
    first_pair = group * pairs // PER_STEP
    key_rows = keys.shape[0]
    lanes = 2 * HEAD_DIM * PER_STEP
    specs = [
        pl.BlockSpec((rows, lanes), lambda p: (0, p + first_pair)),
        pl.BlockSpec((key_rows, lanes), lambda p: (0, p + first_pair)),
        pl.BlockSpec((key_rows, lanes), lambda p: (0, p + first_pair)),
    ]
    operands = [queries, keys, values]
    aliases = {}
    if earlier is not None:
        specs.append(pl.BlockSpec(memory_space=pl.ANY))
        operands.append(earlier)
        aliases = {3: 0}
    return pl.pallas_call(
        video_kernel,
        grid=(pairs // PER_STEP,),
        in_specs=specs,
        out_specs=pl.BlockSpec((rows, lanes), lambda p: (0, p + first_pair)),
        out_shape=jax.ShapeDtypeStruct((rows, width), jnp.bfloat16),
        input_output_aliases=aliases,
        cost_estimate=pl.CostEstimate(
            flops=8 * rows * key_rows * width // groups,
            transcendentals=rows * key_rows * width // HEAD_DIM // groups,
            bytes_accessed=2 * (2 * rows * width + 2 * key_rows * width) // groups,
        ),
    )(*operands)


AUDIO_STEP = 4


def audio_kernel(query_ref, key_ref, value_ref, sum_ref, total_ref, top_ref):
    step = pl.program_id(0)

    @pl.when(step == 0)
    def _():
        total_ref[...] = jnp.zeros_like(total_ref)
        top_ref[...] = jnp.zeros_like(top_ref)

    column = lax.broadcasted_iota(jnp.int32, total_ref.shape, 1)
    totals_now = total_ref[...]
    tops_now = top_ref[...]
    for sub in range(AUDIO_STEP):
        lanes = slice(sub * 2 * HEAD_DIM, (sub + 1) * 2 * HEAD_DIM)
        summed, tops, counts = pair_attention(
            query_ref[:, lanes], key_ref[:, lanes], value_ref[:, lanes]
        )
        for half in range(2):
            here = column == 2 * (step * AUDIO_STEP + sub) + half
            totals_now = jnp.where(here, counts[half], totals_now)
            tops_now = jnp.where(here, tops[half], tops_now)
        sum_ref[:, lanes] = summed
    total_ref[...] = totals_now
    top_ref[...] = tops_now


def audio_partial(queries, keys, values, group, groups):
    rows, width = queries.shape
    heads = width // HEAD_DIM // groups
    first_pair = group * heads // 2 // AUDIO_STEP
    lanes = 2 * HEAD_DIM * AUDIO_STEP
    key_rows = keys.shape[0]
    return pl.pallas_call(
        audio_kernel,
        grid=(heads // 2 // AUDIO_STEP,),
        in_specs=[
            pl.BlockSpec((rows, lanes), lambda p: (0, p + first_pair)),
            pl.BlockSpec((key_rows, lanes), lambda p: (0, p + first_pair)),
            pl.BlockSpec((key_rows, lanes), lambda p: (0, p + first_pair)),
        ],
        out_specs=[
            pl.BlockSpec((rows, lanes), lambda p: (0, p)),
            pl.BlockSpec((rows, heads), lambda p: (0, 0)),
            pl.BlockSpec((rows, heads), lambda p: (0, 0)),
        ],
        out_shape=[
            jax.ShapeDtypeStruct((rows, heads * HEAD_DIM), jnp.float32),
            jax.ShapeDtypeStruct((rows, heads), jnp.float32),
            jax.ShapeDtypeStruct((rows, heads), jnp.float32),
        ],
        compiler_params=pltpu.CompilerParams(dimension_semantics=("arbitrary",)),
        cost_estimate=pl.CostEstimate(
            flops=8 * rows * key_rows * width // groups,
            transcendentals=rows * key_rows * heads,
            bytes_accessed=(2 * rows * width + 4 * key_rows * width + 4 * rows * width) // groups,
        ),
    )(queries, keys, values)


def local(video_q, video_k, video_v, audio_q, audio_k, audio_v):
    width = video_q.shape[1]
    heads = width // HEAD_DIM
    groups = 4
    steps = (lax.axis_size("seq") - 1).bit_length()
    all_queries = gather_levels(audio_q)
    audio_calls = [
        (
            lambda q, g=g: (audio_partial(q, video_k, video_v, g, 2),),
            all_queries,
        )
        for g in range(2)
    ]
    gathered, results = gather_rows(
        jnp.concatenate([audio_k, audio_v], axis=1), [None] * (steps - 2) + audio_calls
    )
    parts = [part for result in results for part in result]
    all_keys = gathered[:, :width]
    all_values = gathered[:, width:]
    state = jnp.concatenate(
        [part[0] for part in parts] + [part[1] for part in parts] + [part[2] for part in parts],
        axis=1,
    )
    video_calls = [
        lambda earlier, g=g: video_part(video_q, all_keys, all_values, earlier, g, groups)
        for g in range(groups)
    ]
    mine, video_out = scatter_rows(state, heads, video_calls)
    audio_out = (mine[:, :width] / spread(mine[:, width : width + heads])).astype(jnp.bfloat16)
    return video_out, audio_out


def solution(mesh):
    placed = P(("groups", "seq"), None)
    return jax.shard_map(
        local,
        mesh=mesh,
        in_specs=(placed,) * 6,
        out_specs=(placed, placed),
        check_vma=False,
    )
```

```python
import jax
import jax.numpy as jnp
from jax import lax
from jax.experimental import pallas as pl
from jax.experimental.pallas import tpu as pltpu
from jax.sharding import PartitionSpec as P

HEAD_DIM = 64


def spread(scales):
    heads = scales.shape[1]
    shape = (heads, heads * HEAD_DIM)
    columns = lax.broadcasted_iota(jnp.int32, shape, 1) // HEAD_DIM
    expand = (columns == lax.broadcasted_iota(jnp.int32, shape, 0)).astype(jnp.float32)
    return jnp.dot(
        scales, expand, precision=lax.Precision.HIGHEST, preferred_element_type=jnp.float32
    )


def exchange(value, bit, count):
    pairs = [(source, source ^ bit) for source in range(count)]
    return lax.ppermute(value, "seq", pairs)


def gather_rows(block, during=()):
    count = lax.axis_size("seq")
    me = lax.axis_index("seq")
    held = block[None]
    results = []
    bit = count // 2
    step = 0
    while bit >= 1:
        work = during[step] if step < len(during) else None
        if work is not None:
            held, ready = lax.optimization_barrier((held, work[1]))
        arrived = exchange(held, bit, count)
        if work is not None:
            done = work[0](ready)
            arrived, done = lax.optimization_barrier((arrived, done))
            results.append(done)
        upper = (me & bit) != 0
        low = jnp.where(upper, arrived, held)
        high = jnp.where(upper, held, arrived)
        held = jnp.stack([low, high], axis=1).reshape((-1,) + block.shape)
        bit //= 2
        step += 1
    return held.reshape((count * block.shape[0],) + block.shape[1:]), results


def gather_levels(block):
    count = lax.axis_size("seq")
    me = lax.axis_index("seq")
    held = block[None]
    levels = []
    bit = count // 2
    if bit >= 2:
        levels.append((bit, bit // 2))
        bit //= 4
    while bit >= 1:
        levels.append((bit,))
        bit //= 2
    for level in levels:
        mask = sum(level)
        offsets = [0]
        for b in level:
            offsets = offsets + [o + b for o in offsets]
        pieces = {0: held}
        for offset in offsets[1:]:
            pairs = [(source, source ^ offset) for source in range(count)]
            pieces[offset] = lax.ppermute(held, "seq", pairs)
        mine = me & mask
        ordered = []
        for target in sorted(offsets):
            choice = pieces[0]
            for offset in offsets[1:]:
                choice = jnp.where((mine ^ offset) == target, pieces[offset], choice)
            ordered.append(choice)
        held = jnp.stack(ordered, axis=1).reshape((-1,) + block.shape)
    return held.reshape((count * block.shape[0],) + block.shape[1:])


def merge(first, second, heads):
    width = heads * HEAD_DIM
    top = jnp.maximum(first[:, width + heads :], second[:, width + heads :])
    first_scale = jnp.exp(first[:, width + heads :] - top)
    second_scale = jnp.exp(second[:, width + heads :] - top)
    totals = first[:, width : width + heads] * first_scale + second[:, width : width + heads] * second_scale
    summed = first[:, :width] * spread(first_scale) + second[:, :width] * spread(second_scale)
    return jnp.concatenate([summed, totals, top], axis=1)


def pieces(value, count):
    terms = []
    rest = value
    for ignored in range(count):
        rounded = lax.reduce_precision(rest, exponent_bits=8, mantissa_bits=7)
        terms.append(rounded.astype(jnp.bfloat16))
        rest = rest - rounded
    return terms


def encode(state, heads):
    width = heads * HEAD_DIM
    summed = state[..., :width].astype(jnp.bfloat16)
    totals = pieces(state[..., width : width + heads], 2)
    tops = pieces(state[..., width + heads :], 3)
    return jnp.concatenate([summed] + totals + tops, axis=-1)


def decode(sent, heads):
    width = heads * HEAD_DIM
    summed = sent[..., :width].astype(jnp.float32)
    parts = [
        sent[..., width + i * heads : width + (i + 1) * heads].astype(jnp.float32) for i in range(5)
    ]
    totals = parts[0] + parts[1]
    tops = (parts[2] + parts[3]) + parts[4]
    return jnp.concatenate([summed, totals, tops], axis=-1)


def scatter_rows(state, heads, during=()):
    count = lax.axis_size("seq")
    me = lax.axis_index("seq")
    rows = state.shape[0] // count
    held = state.reshape((count, rows, state.shape[1]))
    carried = None
    bit = 1
    step = 0
    while bit < count:
        pairs = held.reshape((-1, 2, rows, state.shape[1]))
        upper = (me & bit) != 0
        keep = jnp.where(upper, pairs[:, 1], pairs[:, 0])
        give = jnp.where(upper, pairs[:, 0], pairs[:, 1])
        work = during[step] if step < len(during) else None
        if work is not None:
            give, carried = lax.optimization_barrier((give, carried))
        arrived = decode(exchange(encode(give, heads), bit, count), heads)
        if work is not None:
            carried = work(carried)
            arrived, carried = lax.optimization_barrier((arrived, carried))
        held = merge(
            keep.reshape((-1, state.shape[1])), arrived.reshape((-1, state.shape[1])), heads
        ).reshape((-1, rows, state.shape[1]))
        bit *= 2
        step += 1
    for work in during[step:]:
        carried = work(carried)
    return held.reshape((rows, state.shape[1])), carried


def head_masks(rows):
    lane = lax.broadcasted_iota(jnp.int32, (rows, 2 * HEAD_DIM), 1)
    return lane < HEAD_DIM


def split_pair(block):
    first = head_masks(block.shape[0])
    zeros = jnp.zeros_like(block)
    return jnp.concatenate([jnp.where(first, block, zeros), jnp.where(first, zeros, block)], axis=0)


def pair_attention(queries, keys, values):
    key_rows = keys.shape[0]
    scores = (
        lax.dot_general(
            queries, split_pair(keys), (((1,), (1,)), ((), ())), preferred_element_type=jnp.float32
        )
        * 0.125
    )
    weights = []
    tops = []
    counts = []
    for half in range(2):
        part = scores[:, half * key_rows : (half + 1) * key_rows]
        highest = jnp.max(part, axis=1, keepdims=True)
        exps = jnp.exp(part - highest)
        tops.append(highest)
        counts.append(jnp.sum(exps, axis=1, keepdims=True))
        weights.append(exps.astype(jnp.bfloat16))
    summed = jnp.dot(
        jnp.concatenate(weights, axis=1), split_pair(values), preferred_element_type=jnp.float32
    )
    return summed, tops, counts


PER_STEP = 2


def video_kernel(query_ref, key_ref, value_ref, *refs):
    out_ref = refs[-1]
    key_rows = key_ref.shape[0]
    for sub in range(PER_STEP):
        lanes = slice(sub * 2 * HEAD_DIM, (sub + 1) * 2 * HEAD_DIM)
        queries = query_ref[:, lanes]
        scores = (
            lax.dot_general(
                split_pair(key_ref[:, lanes]), queries, (((1,), (1,)), ((), ())),
                preferred_element_type=jnp.float32,
            )
            * 0.125
        )
        weights = []
        counts = []
        for half in range(2):
            part = scores[half * key_rows : (half + 1) * key_rows]
            highest = jnp.max(part, axis=0, keepdims=True)
            exps = jnp.exp(part - highest)
            counts.append(jnp.sum(exps, axis=0, keepdims=True))
            weights.append(exps.astype(jnp.bfloat16))
        summed = lax.dot_general(
            split_pair(value_ref[:, lanes]), jnp.concatenate(weights, axis=0),
            (((0,), (0,)), ((), ())), preferred_element_type=jnp.float32,
        )
        lane = lax.broadcasted_iota(jnp.int32, summed.shape, 0)
        totals = jnp.where(lane < HEAD_DIM, counts[0], counts[1])
        out_ref[:, lanes] = (summed / totals).T.astype(out_ref.dtype)


def video_part(queries, keys, values, earlier, group, groups):
    rows, width = queries.shape
    pairs = width // (2 * HEAD_DIM) // groups
    first_pair = group * pairs // PER_STEP
    key_rows = keys.shape[0]
    lanes = 2 * HEAD_DIM * PER_STEP
    specs = [
        pl.BlockSpec((rows, lanes), lambda p: (0, p + first_pair)),
        pl.BlockSpec((key_rows, lanes), lambda p: (0, p + first_pair)),
        pl.BlockSpec((key_rows, lanes), lambda p: (0, p + first_pair)),
    ]
    operands = [queries, keys, values]
    aliases = {}
    if earlier is not None:
        specs.append(pl.BlockSpec(memory_space=pl.ANY))
        operands.append(earlier)
        aliases = {3: 0}
    return pl.pallas_call(
        video_kernel,
        grid=(pairs // PER_STEP,),
        in_specs=specs,
        out_specs=pl.BlockSpec((rows, lanes), lambda p: (0, p + first_pair)),
        out_shape=jax.ShapeDtypeStruct((rows, width), jnp.bfloat16),
        input_output_aliases=aliases,
        cost_estimate=pl.CostEstimate(
            flops=8 * rows * key_rows * width // groups,
            transcendentals=rows * key_rows * width // HEAD_DIM // groups,
            bytes_accessed=2 * (2 * rows * width + 2 * key_rows * width) // groups,
        ),
    )(*operands)


AUDIO_STEP = 4


def audio_kernel(query_ref, key_ref, value_ref, sum_ref, total_ref, top_ref):
    step = pl.program_id(0)

    @pl.when(step == 0)
    def _():
        total_ref[...] = jnp.zeros_like(total_ref)
        top_ref[...] = jnp.zeros_like(top_ref)

    column = lax.broadcasted_iota(jnp.int32, total_ref.shape, 1)
    totals_now = total_ref[...]
    tops_now = top_ref[...]
    for sub in range(AUDIO_STEP):
        lanes = slice(sub * 2 * HEAD_DIM, (sub + 1) * 2 * HEAD_DIM)
        summed, tops, counts = pair_attention(
            query_ref[:, lanes], key_ref[:, lanes], value_ref[:, lanes]
        )
        for half in range(2):
            here = column == 2 * (step * AUDIO_STEP + sub) + half
            totals_now = jnp.where(here, counts[half], totals_now)
            tops_now = jnp.where(here, tops[half], tops_now)
        sum_ref[:, lanes] = summed
    total_ref[...] = totals_now
    top_ref[...] = tops_now


def audio_partial(queries, keys, values, group, groups):
    rows, width = queries.shape
    heads = width // HEAD_DIM // groups
    first_pair = group * heads // 2 // AUDIO_STEP
    lanes = 2 * HEAD_DIM * AUDIO_STEP
    key_rows = keys.shape[0]
    return pl.pallas_call(
        audio_kernel,
        grid=(heads // 2 // AUDIO_STEP,),
        in_specs=[
            pl.BlockSpec((rows, lanes), lambda p: (0, p + first_pair)),
            pl.BlockSpec((key_rows, lanes), lambda p: (0, p + first_pair)),
            pl.BlockSpec((key_rows, lanes), lambda p: (0, p + first_pair)),
        ],
        out_specs=[
            pl.BlockSpec((rows, lanes), lambda p: (0, p)),
            pl.BlockSpec((rows, heads), lambda p: (0, 0)),
            pl.BlockSpec((rows, heads), lambda p: (0, 0)),
        ],
        out_shape=[
            jax.ShapeDtypeStruct((rows, heads * HEAD_DIM), jnp.float32),
            jax.ShapeDtypeStruct((rows, heads), jnp.float32),
            jax.ShapeDtypeStruct((rows, heads), jnp.float32),
        ],
        compiler_params=pltpu.CompilerParams(dimension_semantics=("arbitrary",)),
        cost_estimate=pl.CostEstimate(
            flops=8 * rows * key_rows * width // groups,
            transcendentals=rows * key_rows * heads,
            bytes_accessed=(2 * rows * width + 4 * key_rows * width + 4 * rows * width) // groups,
        ),
    )(queries, keys, values)


def local(video_q, video_k, video_v, audio_q, audio_k, audio_v):
    width = video_q.shape[1]
    heads = width // HEAD_DIM
    groups = 4
    steps = (lax.axis_size("seq") - 1).bit_length()
    all_queries = gather_levels(audio_q)
    audio_calls = [
        (
            lambda q: (audio_partial(q, video_k, video_v, 0, 1),),
            all_queries,
        )
        for ignored in range(1)
    ]
    gathered, results = gather_rows(
        jnp.concatenate([audio_k, audio_v], axis=1), [None] * (steps - 2) + audio_calls + [None]
    )
    parts = [part for result in results for part in result]
    all_keys = gathered[:, :width]
    all_values = gathered[:, width:]
    state = jnp.concatenate(
        [part[0] for part in parts] + [part[1] for part in parts] + [part[2] for part in parts],
        axis=1,
    )
    video_calls = [
        lambda earlier, g=g: video_part(video_q, all_keys, all_values, earlier, g, groups)
        for g in range(groups)
    ]
    mine, video_out = scatter_rows(state, heads, video_calls)
    audio_out = (mine[:, :width] / spread(mine[:, width : width + heads])).astype(jnp.bfloat16)
    return video_out, audio_out


def solution(mesh):
    placed = P(("groups", "seq"), None)
    return jax.shard_map(
        local,
        mesh=mesh,
        in_specs=(placed,) * 6,
        out_specs=(placed, placed),
        check_vma=False,
    )
```

```python
import jax
import jax.numpy as jnp
from jax import lax
from jax.experimental import pallas as pl
from jax.experimental.pallas import tpu as pltpu
from jax.sharding import PartitionSpec as P

HEAD_DIM = 64


def spread(scales):
    heads = scales.shape[1]
    shape = (heads, heads * HEAD_DIM)
    columns = lax.broadcasted_iota(jnp.int32, shape, 1) // HEAD_DIM
    expand = (columns == lax.broadcasted_iota(jnp.int32, shape, 0)).astype(jnp.float32)
    return jnp.dot(
        scales, expand, precision=lax.Precision.HIGHEST, preferred_element_type=jnp.float32
    )


def exchange(value, bit, count):
    pairs = [(source, source ^ bit) for source in range(count)]
    return lax.ppermute(value, "seq", pairs)


def gather_rows(block, during=()):
    count = lax.axis_size("seq")
    me = lax.axis_index("seq")
    held = block[None]
    results = []
    bit = count // 2
    step = 0
    while bit >= 1:
        work = during[step] if step < len(during) else None
        if work is not None:
            held, ready = lax.optimization_barrier((held, work[1]))
        arrived = exchange(held, bit, count)
        if work is not None:
            done = work[0](ready)
            arrived, done = lax.optimization_barrier((arrived, done))
            results.append(done)
        upper = (me & bit) != 0
        low = jnp.where(upper, arrived, held)
        high = jnp.where(upper, held, arrived)
        held = jnp.stack([low, high], axis=1).reshape((-1,) + block.shape)
        bit //= 2
        step += 1
    return held.reshape((count * block.shape[0],) + block.shape[1:]), results


def gather_levels(block):
    count = lax.axis_size("seq")
    me = lax.axis_index("seq")
    held = block[None]
    levels = []
    bit = count // 2
    if bit >= 2:
        levels.append((bit, bit // 2))
        bit //= 4
    while bit >= 1:
        levels.append((bit,))
        bit //= 2
    for level in levels:
        mask = sum(level)
        offsets = [0]
        for b in level:
            offsets = offsets + [o + b for o in offsets]
        pieces = {0: held}
        for offset in offsets[1:]:
            pairs = [(source, source ^ offset) for source in range(count)]
            pieces[offset] = lax.ppermute(held, "seq", pairs)
        mine = me & mask
        ordered = []
        for target in sorted(offsets):
            choice = pieces[0]
            for offset in offsets[1:]:
                choice = jnp.where((mine ^ offset) == target, pieces[offset], choice)
            ordered.append(choice)
        held = jnp.stack(ordered, axis=1).reshape((-1,) + block.shape)
    return held.reshape((count * block.shape[0],) + block.shape[1:])


def merge(first, second, heads):
    width = heads * HEAD_DIM
    top = jnp.maximum(first[:, width + heads :], second[:, width + heads :])
    first_scale = jnp.exp(first[:, width + heads :] - top)
    second_scale = jnp.exp(second[:, width + heads :] - top)
    totals = first[:, width : width + heads] * first_scale + second[:, width : width + heads] * second_scale
    summed = first[:, :width] * spread(first_scale) + second[:, :width] * spread(second_scale)
    return jnp.concatenate([summed, totals, top], axis=1)


def pieces(value, count):
    terms = []
    rest = value
    for ignored in range(count):
        rounded = lax.reduce_precision(rest, exponent_bits=8, mantissa_bits=7)
        terms.append(rounded.astype(jnp.bfloat16))
        rest = rest - rounded
    return terms


def encode(state, heads):
    width = heads * HEAD_DIM
    summed = state[..., :width].astype(jnp.bfloat16)
    totals = pieces(state[..., width : width + heads], 2)
    tops = pieces(state[..., width + heads :], 3)
    return jnp.concatenate([summed] + totals + tops, axis=-1)


def decode(sent, heads):
    width = heads * HEAD_DIM
    summed = sent[..., :width].astype(jnp.float32)
    parts = [
        sent[..., width + i * heads : width + (i + 1) * heads].astype(jnp.float32) for i in range(5)
    ]
    totals = parts[0] + parts[1]
    tops = (parts[2] + parts[3]) + parts[4]
    return jnp.concatenate([summed, totals, tops], axis=-1)


def scatter_rows(state, heads, during=()):
    count = lax.axis_size("seq")
    me = lax.axis_index("seq")
    rows = state.shape[0] // count
    held = state.reshape((count, rows, state.shape[1]))
    carried = None
    bit = 1
    step = 0
    while bit < count:
        pairs = held.reshape((-1, 2, rows, state.shape[1]))
        upper = (me & bit) != 0
        keep = jnp.where(upper, pairs[:, 1], pairs[:, 0])
        give = jnp.where(upper, pairs[:, 0], pairs[:, 1])
        work = during[step] if step < len(during) else None
        if work is not None:
            give, carried = lax.optimization_barrier((give, carried))
        arrived = decode(exchange(encode(give, heads), bit, count), heads)
        if work is not None:
            carried = work(carried)
            arrived, carried = lax.optimization_barrier((arrived, carried))
        held = merge(
            keep.reshape((-1, state.shape[1])), arrived.reshape((-1, state.shape[1])), heads
        ).reshape((-1, rows, state.shape[1]))
        bit *= 2
        step += 1
    for work in during[step:]:
        carried = work(carried)
    return held.reshape((rows, state.shape[1])), carried


def head_masks(rows):
    lane = lax.broadcasted_iota(jnp.int32, (rows, 2 * HEAD_DIM), 1)
    return lane < HEAD_DIM


def split_pair(block):
    first = head_masks(block.shape[0])
    zeros = jnp.zeros_like(block)
    return jnp.concatenate([jnp.where(first, block, zeros), jnp.where(first, zeros, block)], axis=0)


def pair_attention(queries, keys, values):
    key_rows = keys.shape[0]
    scores = (
        lax.dot_general(
            queries, split_pair(keys), (((1,), (1,)), ((), ())), preferred_element_type=jnp.float32
        )
        * 0.125
    )
    weights = []
    tops = []
    counts = []
    for half in range(2):
        part = scores[:, half * key_rows : (half + 1) * key_rows]
        highest = jnp.max(part, axis=1, keepdims=True)
        exps = jnp.exp(part - highest)
        tops.append(highest)
        counts.append(jnp.sum(exps, axis=1, keepdims=True))
        weights.append(exps.astype(jnp.bfloat16))
    summed = jnp.dot(
        jnp.concatenate(weights, axis=1), split_pair(values), preferred_element_type=jnp.float32
    )
    return summed, tops, counts


PER_STEP = 2


def video_kernel(query_ref, key_ref, value_ref, *refs):
    out_ref = refs[-1]
    key_rows = key_ref.shape[0]
    for sub in range(PER_STEP):
        lanes = slice(sub * 2 * HEAD_DIM, (sub + 1) * 2 * HEAD_DIM)
        queries = query_ref[:, lanes]
        scores = (
            lax.dot_general(
                split_pair(key_ref[:, lanes]), queries, (((1,), (1,)), ((), ())),
                preferred_element_type=jnp.float32,
            )
            * 0.125
        )
        weights = []
        counts = []
        for half in range(2):
            part = scores[half * key_rows : (half + 1) * key_rows]
            highest = jnp.max(part, axis=0, keepdims=True)
            exps = jnp.exp(part - highest)
            counts.append(jnp.sum(exps, axis=0, keepdims=True))
            weights.append(exps.astype(jnp.bfloat16))
        summed = lax.dot_general(
            split_pair(value_ref[:, lanes]), jnp.concatenate(weights, axis=0),
            (((0,), (0,)), ((), ())), preferred_element_type=jnp.float32,
        )
        lane = lax.broadcasted_iota(jnp.int32, summed.shape, 0)
        totals = jnp.where(lane < HEAD_DIM, counts[0], counts[1])
        out_ref[:, lanes] = (summed / totals).T.astype(out_ref.dtype)


def video_part(queries, keys, values, earlier, group, groups):
    rows, width = queries.shape
    pairs = width // (2 * HEAD_DIM) // groups
    first_pair = group * pairs // PER_STEP
    key_rows = keys.shape[0]
    lanes = 2 * HEAD_DIM * PER_STEP
    specs = [
        pl.BlockSpec((rows, lanes), lambda p: (0, p + first_pair)),
        pl.BlockSpec((key_rows, lanes), lambda p: (0, p + first_pair)),
        pl.BlockSpec((key_rows, lanes), lambda p: (0, p + first_pair)),
    ]
    operands = [queries, keys, values]
    aliases = {}
    if earlier is not None:
        specs.append(pl.BlockSpec(memory_space=pl.ANY))
        operands.append(earlier)
        aliases = {3: 0}
    return pl.pallas_call(
        video_kernel,
        grid=(pairs // PER_STEP,),
        in_specs=specs,
        out_specs=pl.BlockSpec((rows, lanes), lambda p: (0, p + first_pair)),
        out_shape=jax.ShapeDtypeStruct((rows, width), jnp.bfloat16),
        input_output_aliases=aliases,
        cost_estimate=pl.CostEstimate(
            flops=8 * rows * key_rows * width // groups,
            transcendentals=rows * key_rows * width // HEAD_DIM // groups,
            bytes_accessed=2 * (2 * rows * width + 2 * key_rows * width) // groups,
        ),
    )(*operands)


AUDIO_STEP = 4


def audio_kernel(query_ref, key_ref, value_ref, sum_ref, total_ref, top_ref):
    step = pl.program_id(0)

    @pl.when(step == 0)
    def _():
        total_ref[...] = jnp.zeros_like(total_ref)
        top_ref[...] = jnp.zeros_like(top_ref)

    column = lax.broadcasted_iota(jnp.int32, total_ref.shape, 1)
    totals_now = total_ref[...]
    tops_now = top_ref[...]
    for sub in range(AUDIO_STEP):
        lanes = slice(sub * 2 * HEAD_DIM, (sub + 1) * 2 * HEAD_DIM)
        summed, tops, counts = pair_attention(
            query_ref[:, lanes], key_ref[:, lanes], value_ref[:, lanes]
        )
        for half in range(2):
            here = column == 2 * (step * AUDIO_STEP + sub) + half
            totals_now = jnp.where(here, counts[half], totals_now)
            tops_now = jnp.where(here, tops[half], tops_now)
        sum_ref[:, lanes] = summed
    total_ref[...] = totals_now
    top_ref[...] = tops_now


def audio_partial(queries, keys, values, group, groups):
    rows, width = queries.shape
    heads = width // HEAD_DIM // groups
    first_pair = group * heads // 2 // AUDIO_STEP
    lanes = 2 * HEAD_DIM * AUDIO_STEP
    key_rows = keys.shape[0]
    return pl.pallas_call(
        audio_kernel,
        grid=(heads // 2 // AUDIO_STEP,),
        in_specs=[
            pl.BlockSpec((rows, lanes), lambda p: (0, p + first_pair)),
            pl.BlockSpec((key_rows, lanes), lambda p: (0, p + first_pair)),
            pl.BlockSpec((key_rows, lanes), lambda p: (0, p + first_pair)),
        ],
        out_specs=[
            pl.BlockSpec((rows, lanes), lambda p: (0, p)),
            pl.BlockSpec((rows, heads), lambda p: (0, 0)),
            pl.BlockSpec((rows, heads), lambda p: (0, 0)),
        ],
        out_shape=[
            jax.ShapeDtypeStruct((rows, heads * HEAD_DIM), jnp.float32),
            jax.ShapeDtypeStruct((rows, heads), jnp.float32),
            jax.ShapeDtypeStruct((rows, heads), jnp.float32),
        ],
        compiler_params=pltpu.CompilerParams(dimension_semantics=("arbitrary",)),
        cost_estimate=pl.CostEstimate(
            flops=8 * rows * key_rows * width // groups,
            transcendentals=rows * key_rows * heads,
            bytes_accessed=(2 * rows * width + 4 * key_rows * width + 4 * rows * width) // groups,
        ),
    )(queries, keys, values)


def local(video_q, video_k, video_v, audio_q, audio_k, audio_v):
    width = video_q.shape[1]
    heads = width // HEAD_DIM
    groups = 4
    steps = (lax.axis_size("seq") - 1).bit_length()
    all_queries = gather_levels(audio_q)
    audio_calls = [
        (
            lambda q: (audio_partial(q, video_k, video_v, 0, 1),),
            all_queries,
        )
        for ignored in range(1)
    ]
    gathered, results = gather_rows(
        jnp.concatenate([audio_k, audio_v], axis=1), [None] * (steps - 2) + audio_calls + [None]
    )
    parts = [part for result in results for part in result]
    all_keys = gathered[:, :width]
    all_values = gathered[:, width:]
    state = jnp.concatenate(
        [part[0] for part in parts] + [part[1] for part in parts] + [part[2] for part in parts],
        axis=1,
    )
    video_calls = [
        lambda earlier, g=g: video_part(video_q, all_keys, all_values, earlier, g, 2)
        for g in range(2)
    ]
    video_calls = [None] * (steps - 3) + [video_calls[0], None, video_calls[1]]
    mine, video_out = scatter_rows(state, heads, video_calls)
    audio_out = (mine[:, :width] / spread(mine[:, width : width + heads])).astype(jnp.bfloat16)
    return video_out, audio_out


def solution(mesh):
    placed = P(("groups", "seq"), None)
    return jax.shard_map(
        local,
        mesh=mesh,
        in_specs=(placed,) * 6,
        out_specs=(placed, placed),
        check_vma=False,
    )
```

```python
import jax
import jax.numpy as jnp
from jax import lax
from jax.experimental import pallas as pl
from jax.experimental.pallas import tpu as pltpu
from jax.sharding import PartitionSpec as P

HEAD_DIM = 64


def spread(scales):
    heads = scales.shape[1]
    shape = (heads, heads * HEAD_DIM)
    columns = lax.broadcasted_iota(jnp.int32, shape, 1) // HEAD_DIM
    expand = (columns == lax.broadcasted_iota(jnp.int32, shape, 0)).astype(jnp.float32)
    return jnp.dot(
        scales, expand, precision=lax.Precision.HIGHEST, preferred_element_type=jnp.float32
    )


def exchange(value, bit, count):
    pairs = [(source, source ^ bit) for source in range(count)]
    return lax.ppermute(value, "seq", pairs)


def gather_rows(block, during=()):
    count = lax.axis_size("seq")
    me = lax.axis_index("seq")
    held = block[None]
    results = []
    bit = count // 2
    step = 0
    while bit >= 1:
        work = during[step] if step < len(during) else None
        if work is not None:
            held, ready = lax.optimization_barrier((held, work[1]))
        arrived = exchange(held, bit, count)
        if work is not None:
            done = work[0](ready)
            arrived, done = lax.optimization_barrier((arrived, done))
            results.append(done)
        upper = (me & bit) != 0
        low = jnp.where(upper, arrived, held)
        high = jnp.where(upper, held, arrived)
        held = jnp.stack([low, high], axis=1).reshape((-1,) + block.shape)
        bit //= 2
        step += 1
    return held.reshape((count * block.shape[0],) + block.shape[1:]), results


def gather_levels(block):
    count = lax.axis_size("seq")
    me = lax.axis_index("seq")
    held = block[None]
    levels = []
    bit = count // 2
    if bit >= 2:
        levels.append((bit, bit // 2))
        bit //= 4
    while bit >= 1:
        levels.append((bit,))
        bit //= 2
    for level in levels:
        mask = sum(level)
        offsets = [0]
        for b in level:
            offsets = offsets + [o + b for o in offsets]
        pieces = {0: held}
        for offset in offsets[1:]:
            pairs = [(source, source ^ offset) for source in range(count)]
            pieces[offset] = lax.ppermute(held, "seq", pairs)
        mine = me & mask
        ordered = []
        for target in sorted(offsets):
            choice = pieces[0]
            for offset in offsets[1:]:
                choice = jnp.where((mine ^ offset) == target, pieces[offset], choice)
            ordered.append(choice)
        held = jnp.stack(ordered, axis=1).reshape((-1,) + block.shape)
    return held.reshape((count * block.shape[0],) + block.shape[1:])


def merge(first, second, heads):
    width = heads * HEAD_DIM
    top = jnp.maximum(first[:, width + heads :], second[:, width + heads :])
    first_scale = jnp.exp(first[:, width + heads :] - top)
    second_scale = jnp.exp(second[:, width + heads :] - top)
    totals = first[:, width : width + heads] * first_scale + second[:, width : width + heads] * second_scale
    summed = first[:, :width] * spread(first_scale) + second[:, :width] * spread(second_scale)
    return jnp.concatenate([summed, totals, top], axis=1)


def pieces(value, count):
    terms = []
    rest = value
    for ignored in range(count):
        rounded = lax.reduce_precision(rest, exponent_bits=8, mantissa_bits=7)
        terms.append(rounded.astype(jnp.bfloat16))
        rest = rest - rounded
    return terms


def encode(state, heads):
    width = heads * HEAD_DIM
    summed = state[..., :width].astype(jnp.bfloat16)
    totals = pieces(state[..., width : width + heads], 2)
    tops = pieces(state[..., width + heads :], 3)
    return jnp.concatenate([summed] + totals + tops, axis=-1)


def decode(sent, heads):
    width = heads * HEAD_DIM
    summed = sent[..., :width].astype(jnp.float32)
    parts = [
        sent[..., width + i * heads : width + (i + 1) * heads].astype(jnp.float32) for i in range(5)
    ]
    totals = parts[0] + parts[1]
    tops = (parts[2] + parts[3]) + parts[4]
    return jnp.concatenate([summed, totals, tops], axis=-1)


def scatter_rows(state, heads, during=()):
    count = lax.axis_size("seq")
    me = lax.axis_index("seq")
    rows = state.shape[0] // count
    held = state.reshape((count, rows, state.shape[1]))
    carried = None
    bit = 1
    step = 0
    while bit < count:
        pairs = held.reshape((-1, 2, rows, state.shape[1]))
        upper = (me & bit) != 0
        keep = jnp.where(upper, pairs[:, 1], pairs[:, 0])
        give = jnp.where(upper, pairs[:, 0], pairs[:, 1])
        work = during[step] if step < len(during) else None
        if work is not None:
            give, carried = lax.optimization_barrier((give, carried))
        arrived = decode(exchange(encode(give, heads), bit, count), heads)
        if work is not None:
            carried = work(carried)
            arrived, carried = lax.optimization_barrier((arrived, carried))
        held = merge(
            keep.reshape((-1, state.shape[1])), arrived.reshape((-1, state.shape[1])), heads
        ).reshape((-1, rows, state.shape[1]))
        bit *= 2
        step += 1
    for work in during[step:]:
        carried = work(carried)
    return held.reshape((rows, state.shape[1])), carried


def head_masks(rows):
    lane = lax.broadcasted_iota(jnp.int32, (rows, 2 * HEAD_DIM), 1)
    return lane < HEAD_DIM


def split_pair(block):
    first = head_masks(block.shape[0])
    zeros = jnp.zeros_like(block)
    return jnp.concatenate([jnp.where(first, block, zeros), jnp.where(first, zeros, block)], axis=0)


def pair_attention(queries, keys, values):
    key_rows = keys.shape[0]
    scores = (
        lax.dot_general(
            queries, split_pair(keys), (((1,), (1,)), ((), ())), preferred_element_type=jnp.float32
        )
        * 0.125
    )
    weights = []
    tops = []
    counts = []
    for half in range(2):
        part = scores[:, half * key_rows : (half + 1) * key_rows]
        highest = jnp.max(part, axis=1, keepdims=True)
        exps = jnp.exp(part - highest)
        tops.append(highest)
        counts.append(jnp.sum(exps, axis=1, keepdims=True))
        weights.append(exps.astype(jnp.bfloat16))
    summed = jnp.dot(
        jnp.concatenate(weights, axis=1), split_pair(values), preferred_element_type=jnp.float32
    )
    return summed, tops, counts


PER_STEP = 2


def video_kernel(query_ref, key_ref, value_ref, *refs):
    out_ref = refs[-1]
    key_rows = key_ref.shape[0]
    for sub in range(PER_STEP):
        lanes = slice(sub * 2 * HEAD_DIM, (sub + 1) * 2 * HEAD_DIM)
        queries = query_ref[:, lanes]
        scores = (
            lax.dot_general(
                split_pair(key_ref[:, lanes]), queries, (((1,), (1,)), ((), ())),
                preferred_element_type=jnp.float32,
            )
            * 0.125
        )
        weights = []
        counts = []
        for half in range(2):
            part = scores[half * key_rows : (half + 1) * key_rows]
            highest = jnp.max(part, axis=0, keepdims=True)
            exps = jnp.exp(part - highest)
            counts.append(jnp.sum(exps, axis=0, keepdims=True))
            weights.append(exps.astype(jnp.bfloat16))
        summed = lax.dot_general(
            split_pair(value_ref[:, lanes]), jnp.concatenate(weights, axis=0),
            (((0,), (0,)), ((), ())), preferred_element_type=jnp.float32,
        )
        lane = lax.broadcasted_iota(jnp.int32, summed.shape, 0)
        totals = jnp.where(lane < HEAD_DIM, counts[0], counts[1])
        out_ref[:, lanes] = (summed / totals).T.astype(out_ref.dtype)


def video_part(queries, keys, values, earlier, group, groups):
    rows, width = queries.shape
    pairs = width // (2 * HEAD_DIM) // groups
    first_pair = group * pairs // PER_STEP
    key_rows = keys.shape[0]
    lanes = 2 * HEAD_DIM * PER_STEP
    specs = [
        pl.BlockSpec((rows, lanes), lambda p: (0, p + first_pair)),
        pl.BlockSpec((key_rows, lanes), lambda p: (0, p + first_pair)),
        pl.BlockSpec((key_rows, lanes), lambda p: (0, p + first_pair)),
    ]
    operands = [queries, keys, values]
    aliases = {}
    if earlier is not None:
        specs.append(pl.BlockSpec(memory_space=pl.ANY))
        operands.append(earlier)
        aliases = {3: 0}
    return pl.pallas_call(
        video_kernel,
        grid=(pairs // PER_STEP,),
        in_specs=specs,
        out_specs=pl.BlockSpec((rows, lanes), lambda p: (0, p + first_pair)),
        out_shape=jax.ShapeDtypeStruct((rows, width), jnp.bfloat16),
        input_output_aliases=aliases,
        cost_estimate=pl.CostEstimate(
            flops=8 * rows * key_rows * width // groups,
            transcendentals=rows * key_rows * width // HEAD_DIM // groups,
            bytes_accessed=2 * (2 * rows * width + 2 * key_rows * width) // groups,
        ),
    )(*operands)


AUDIO_STEP = 8


def audio_kernel(query_ref, key_ref, value_ref, sum_ref, total_ref, top_ref):
    step = pl.program_id(0)

    @pl.when(step == 0)
    def _():
        total_ref[...] = jnp.zeros_like(total_ref)
        top_ref[...] = jnp.zeros_like(top_ref)

    column = lax.broadcasted_iota(jnp.int32, total_ref.shape, 1)
    totals_now = total_ref[...]
    tops_now = top_ref[...]
    for sub in range(AUDIO_STEP):
        lanes = slice(sub * 2 * HEAD_DIM, (sub + 1) * 2 * HEAD_DIM)
        summed, tops, counts = pair_attention(
            query_ref[:, lanes], key_ref[:, lanes], value_ref[:, lanes]
        )
        for half in range(2):
            here = column == 2 * (step * AUDIO_STEP + sub) + half
            totals_now = jnp.where(here, counts[half], totals_now)
            tops_now = jnp.where(here, tops[half], tops_now)
        sum_ref[:, lanes] = summed
    total_ref[...] = totals_now
    top_ref[...] = tops_now


def audio_partial(queries, keys, values, group, groups):
    rows, width = queries.shape
    heads = width // HEAD_DIM // groups
    first_pair = group * heads // 2 // AUDIO_STEP
    lanes = 2 * HEAD_DIM * AUDIO_STEP
    key_rows = keys.shape[0]
    return pl.pallas_call(
        audio_kernel,
        grid=(heads // 2 // AUDIO_STEP,),
        in_specs=[
            pl.BlockSpec((rows, lanes), lambda p: (0, p + first_pair)),
            pl.BlockSpec((key_rows, lanes), lambda p: (0, p + first_pair)),
            pl.BlockSpec((key_rows, lanes), lambda p: (0, p + first_pair)),
        ],
        out_specs=[
            pl.BlockSpec((rows, lanes), lambda p: (0, p)),
            pl.BlockSpec((rows, heads), lambda p: (0, 0)),
            pl.BlockSpec((rows, heads), lambda p: (0, 0)),
        ],
        out_shape=[
            jax.ShapeDtypeStruct((rows, heads * HEAD_DIM), jnp.float32),
            jax.ShapeDtypeStruct((rows, heads), jnp.float32),
            jax.ShapeDtypeStruct((rows, heads), jnp.float32),
        ],
        compiler_params=pltpu.CompilerParams(dimension_semantics=("arbitrary",)),
        cost_estimate=pl.CostEstimate(
            flops=8 * rows * key_rows * width // groups,
            transcendentals=rows * key_rows * heads,
            bytes_accessed=(2 * rows * width + 4 * key_rows * width + 4 * rows * width) // groups,
        ),
    )(queries, keys, values)


def local(video_q, video_k, video_v, audio_q, audio_k, audio_v):
    width = video_q.shape[1]
    heads = width // HEAD_DIM
    groups = 4
    steps = (lax.axis_size("seq") - 1).bit_length()
    all_queries = gather_levels(audio_q)
    audio_calls = [
        (
            lambda q: (audio_partial(q, video_k, video_v, 0, 1),),
            all_queries,
        )
        for ignored in range(1)
    ]
    gathered, results = gather_rows(
        jnp.concatenate([audio_k, audio_v], axis=1), [None] * (steps - 2) + audio_calls + [None]
    )
    parts = [part for result in results for part in result]
    all_keys = gathered[:, :width]
    all_values = gathered[:, width:]
    state = jnp.concatenate(
        [part[0] for part in parts] + [part[1] for part in parts] + [part[2] for part in parts],
        axis=1,
    )
    video_calls = [
        lambda earlier, g=g: video_part(video_q, all_keys, all_values, earlier, g, groups)
        for g in range(groups)
    ]
    mine, video_out = scatter_rows(state, heads, video_calls)
    audio_out = (mine[:, :width] / spread(mine[:, width : width + heads])).astype(jnp.bfloat16)
    return video_out, audio_out


def solution(mesh):
    placed = P(("groups", "seq"), None)
    return jax.shard_map(
        local,
        mesh=mesh,
        in_specs=(placed,) * 6,
        out_specs=(placed, placed),
        check_vma=False,
    )
```
